32 devices in a mesh: groups: 2 (over y), seq: 4 (over z), chan: 2 (over x), rep: 2 (over core).
Axes of the slice: x: 2, y: 2, z: 4, core: 2. Of those that a mesh axis runs over, the one named last changes fastest.
Arguments:
- query_proj: bfloat16 [2048, 8192], P(('groups', 'seq'), ('chan', 'rep')), parts along dimension 0, may hold values from -6 to 6
- key_proj: bfloat16 [2048, 8192], P(('groups', 'seq'), ('chan', 'rep')), parts along dimension 0, may hold values from -6 to 6
- value_proj: bfloat16 [2048, 8192], P(('groups', 'seq'), ('chan', 'rep')), parts along dimension 0, may hold values from -6 to 6
- short_taps: bfloat16 [7, 8192], P(None, ('chan', 'rep')), may hold values from -2 to 2
- medium_taps: bfloat16 [128, 512], P(None, ('chan', 'rep')), may hold values from -0.5 to 0.5
- modal_poles: float32 [4, 512, 16], P(None, ('chan', 'rep')), may hold values from -3.1416 to 3.1416, as said below
- skip_gain: float32 [8192], P(('chan', 'rep')), may hold values from 0.5 to 1.5
- norm_gain: float32 [8192], P(('chan', 'rep')), may hold values from 0.5 to 1.5
- unembed: bfloat16 [8192, 512], P(('chan', 'rep')), may hold values from -0.1875 to 0.1875
- token_ids: int32 [2048], P(('groups', 'seq')), parts along dimension 0, may hold values from 0 to 511
- genome_lengths: int32 [16], P('groups'), parts along dimension 0, may hold values from 1 to 512, 1024 in all
Outputs:
- token_logprob: float32 [2048], P(('groups', 'seq')), parts along dimension 0
- genome_score: float32 [16], P('groups'), parts along dimension 0
The draws below stay inside these ranges and needn't reach their ends.
There are 2 independent parts, one for each index of `groups`. The reference program is written for one: setup_inputs(seed, part) draws one part's arguments, and reference() takes and returns one part's arrays. A program takes and returns all parts, laid end to end along the dimension named above; an argument that names none is the same for every part. Nothing has to cross between parts.
Inputs may be any that keep to these rules, and one draw needn't show every extreme that they name: `genome_lengths`: the 8 genomes are packed end to end from position 0; their lengths sum to 1024. `modal_poles`: row 0 holds positive decay rates, row 1 angles, rows 2 and 3 residues.
All inputs are finite; a program needn't handle non-finite values.
Results may differ from the reference program's by a relative error of at most 0.0033.
Values may be sent and summed in bfloat16 or wider, within the bound.
No kernel may reach another device: no remote copies, remote signals or barrier semaphores. Data moves between devices by JAX's collectives and lax.ppermute only.
A program may use at most 128 MiB of HBM per device.

```python
import math
import jax
import jax.numpy as jnp
import numpy as np
from jax import lax

D = 8192
VOCAB = 512
GROUP = 16
SHORT = 7
MEDIUM = 128
MODES = 16
NGEN = 8
SLAB = 1024
GROUPS = 512


def draw_modal_poles(key, part):
    key_list = jax.random.split(key, 5)
    array_shape = (GROUPS, MODES)
    slow_share = 0.5
    slow_mask = jax.random.uniform(key_list[0], array_shape) < slow_share
    spread = jax.random.uniform(key_list[1], array_shape)
    slow_rate = 0.1 / SLAB * jnp.power(10.0, spread)
    fast_rate = 0.02 * jnp.power(4.0, spread)
    decay_rate = jnp.where(slow_mask, slow_rate, fast_rate)
    angles = jax.random.uniform(key_list[2], array_shape, minval=-math.pi, maxval=math.pi)
    res_scale = jnp.sqrt(2.0 * jnp.maximum(decay_rate, 8.0 / SLAB) / MODES)
    residue_re = jax.random.normal(key_list[3], array_shape) * res_scale
    residue_im = jax.random.normal(key_list[4], array_shape) * res_scale
    return jnp.stack([decay_rate, angles, residue_re, residue_im]).astype(jnp.float32)


def with_ends(drawn, key, least, high):
    place = [jax.random.randint(jax.random.fold_in(key, axis), (), 0, length) for axis, length in enumerate(drawn.shape)]
    longest = drawn.shape.index(max(drawn.shape))
    beside = place[:longest] + [(place[longest] + 1) % drawn.shape[longest]] + place[longest + 1:]
    return drawn.at[tuple(place)].set(least).at[tuple(beside)].set(high)


def block_levels(own_key, extent, pieces, least, top_value):
    gain = 1.0
    for axis_at, shards_of in pieces:
        heights = jax.random.uniform(jax.random.fold_in(jax.random.fold_in(own_key, 6), axis_at), (shards_of,), jnp.float32, least / len(pieces), top_value / len(pieces))
        gain = gain * jnp.repeat(jnp.exp(heights), extent[axis_at] // shards_of).reshape((-1,) + (1,) * (len(extent) - 1 - axis_at))
    return gain


def length_profile(number_of, total, bound, skew):
    portions = [(1 << 20) // math.isqrt(rank ** skew) + 1 for rank in range(2, number_of + 1)]
    surplus, given = total - bound - (number_of - 1), [1] * (number_of - 1)
    while surplus > 0:
        movable = [i for i in range(number_of - 1) if given[i] < bound]
        whole, budget = sum([portions[i] for i in movable]), surplus
        for i in movable:
            extra = min(bound - given[i], max(1, budget * portions[i] // whole), surplus)
            given[i] = given[i] + extra
            surplus = surplus - extra
    return np.array([bound] + given)


def ragged(own_key, count, total, reach, lean):
    if count == 2:
        one = jax.random.randint(own_key, (), max(1, total - reach), min(reach, total - 1) + 1)
        return jnp.stack([one, total - one])
    sizes = jnp.asarray(length_profile(count, total, reach, lean), jnp.int32)
    couples = (count - 1) // 2
    donor, taker = sizes[1:1 + 2 * couples:2], sizes[2:2 + 2 * couples:2]
    margin = jnp.minimum(donor - 1, reach - taker)
    moved = jax.random.randint(jax.random.fold_in(own_key, 1), (couples,), 0, 1 << 20) % (margin + 1)
    sizes = sizes.at[1:1 + 2 * couples:2].set(donor - moved).at[2:2 + 2 * couples:2].set(taker + moved)
    return sizes[jax.random.permutation(jax.random.fold_in(own_key, 2), count)]


def gaussian(key, shape, deviation, limit, shards=(), kind=jnp.bfloat16):
    array = jax.random.normal(key, shape, jnp.float32) * deviation
    if len(shards) > 0:
        array = block_levels(key, shape, shards, -0.22, 0.18) * array
    return jnp.clip(array, min=-limit, max=limit).astype(kind)


def setup_inputs(seed: int = 0, part: int = 0) -> dict:
    splits = jax.random.split(jax.random.key(seed), 12)
    part_splits = jax.random.split(jax.random.fold_in(splits[11], part), 12)
    return {
        "query_proj": gaussian(part_splits[0], (SLAB, D), 1.0, 6.0, ((0, 4), (1, 4))),
        "key_proj": gaussian(part_splits[1], (SLAB, D), 1.0, 6.0, ((0, 4), (1, 4))),
        "value_proj": gaussian(part_splits[2], (SLAB, D), 1.0, 6.0, ((0, 4), (1, 4))),
        "short_taps": gaussian(splits[3], (SHORT, D), SHORT ** -0.5, 2.0, ((1, 4),)),
        "medium_taps": gaussian(splits[4], (MEDIUM, GROUPS), MEDIUM ** -0.5, 0.5, ((1, 4),)),
        "modal_poles": draw_modal_poles(jax.random.fold_in(splits[11], 71), part),
        "skip_gain": jnp.clip(0.5 + 1.0 * jax.random.uniform(splits[6], (D,), jnp.float32) ** block_levels(splits[6], (D,), ((0, 4),), -0.2, 0.2), 0.5, 1.5),
        "norm_gain": jnp.clip(1.0 + 0.1 * jax.random.normal(splits[7], (D,), jnp.float32), 0.5, 1.5),
        "unembed": gaussian(splits[8], (D, VOCAB), (D // 9) ** -0.5, 0.1875, ((0, 4),)),
        "token_ids": with_ends(jax.random.randint(part_splits[9], (SLAB,), 0, VOCAB), jax.random.fold_in(part_splits[9], 1), 0, VOCAB - 1).astype(jnp.int32),
        "genome_lengths": ragged(part_splits[10], NGEN, SLAB, SLAB // 2, 2).astype(jnp.int32),
    }


tile_rows = 128
short_margin = 8
norm_eps = 1e-05

def segment_ids(positions, genome_lengths):
    starts = (jnp.cumsum(genome_lengths) - genome_lengths).astype(jnp.int32)
    at_or_past = (positions[:, None] >= starts[None, :]).astype(jnp.int32)
    return lax.optimization_barrier(jnp.sum(at_or_past, axis=1)).astype(jnp.int32) - 1

def short_filter(keys_in, values_in, seg_list, out_rows, short_taps):
    gated = keys_in.astype(jnp.float32) * values_in.astype(jnp.float32)
    total_rows = keys_in.shape[0]
    lead_rows = total_rows - out_rows
    own_segs = seg_list[lead_rows:]
    result = jnp.zeros((out_rows, keys_in.shape[1]), jnp.float32)
    for lag_index in range(short_taps.shape[0]):
        shifted = gated[lead_rows - lag_index:total_rows - lag_index]
        same_genome = (seg_list[lead_rows - lag_index:total_rows - lag_index] == own_segs).astype(jnp.float32)
        result = result + short_taps[lag_index].astype(jnp.float32)[None, :] * shifted * same_genome[:, None]
    return result.astype(jnp.bfloat16)

def medium_toeplitz(medium_taps):
    out_pos = jnp.arange(tile_rows, dtype=jnp.int32)[:, None]
    in_pos = jnp.arange(2 * tile_rows, dtype=jnp.int32)[None, :]
    lag_grid = out_pos + tile_rows - in_pos
    tap_count = medium_taps.shape[0]
    valid = (lag_grid >= 0) & (lag_grid < tap_count)
    gathered = jnp.take(medium_taps, jnp.clip(lag_grid, 0, tap_count - 1), axis=0)
    masked = jnp.where(valid[:, :, None], gathered, jnp.zeros_like(gathered))
    return jnp.transpose(masked, (2, 0, 1))

def modal_tables(modal_poles):
    decay_rate = modal_poles[0]
    angles = modal_poles[1]
    residue_re = modal_poles[2]
    residue_im = modal_poles[3]
    powers = jnp.arange(tile_rows + 1).astype(jnp.float32)[:, None, None]
    magnitude = jnp.exp(-powers * decay_rate[None])
    power_re = magnitude * jnp.cos(powers * angles[None])
    power_im = magnitude * jnp.sin(powers * angles[None])
    kernel_re = residue_re[None] * power_re - residue_im[None] * power_im
    kernel_im = residue_re[None] * power_im + residue_im[None] * power_re
    kernel = lax.optimization_barrier(jnp.sum(kernel_re[:tile_rows], axis=2))
    lag_grid = jnp.arange(tile_rows, dtype=jnp.int32)[:, None] - jnp.arange(tile_rows, dtype=jnp.int32)[None, :]
    taken = jnp.take(kernel, jnp.clip(lag_grid, 0, tile_rows - 1), axis=0)
    toeplitz = jnp.transpose(jnp.where((lag_grid >= 0)[:, :, None], taken, jnp.zeros_like(taken)), (2, 0, 1))
    outward = jnp.transpose(jnp.concatenate((kernel_re[1:], -kernel_im[1:]), axis=2), (1, 0, 2))
    inward = jnp.transpose(jnp.concatenate((power_re[tile_rows - 1::-1], power_im[tile_rows - 1::-1]), axis=2), (1, 0, 2))
    return (toeplitz, outward, inward, power_re[tile_rows], power_im[tile_rows])

def log_probs(logits, targets):
    vocab_ids = jnp.arange(logits.shape[1], dtype=jnp.int32)
    picked = lax.optimization_barrier(jnp.sum(jnp.where(targets[:, None] == vocab_ids[None, :], logits, jnp.zeros_like(logits)), axis=1))
    return picked - jnp.log(lax.optimization_barrier(jnp.sum(jnp.exp(logits), axis=1)))

def reference(query_proj, key_proj, value_proj, short_taps, medium_taps, modal_poles, skip_gain, norm_gain, unembed, token_ids, genome_lengths):
    highest = lax.Precision.HIGHEST
    segments = segment_ids(jnp.arange(SLAB, dtype=jnp.int32), genome_lengths)
    pad_rows = jnp.zeros((short_margin, D), jnp.bfloat16)
    short_segs = segment_ids(jnp.arange(SLAB + short_margin, dtype=jnp.int32) - short_margin, genome_lengths)
    filtered = short_filter(jnp.concatenate((pad_rows, key_proj)), jnp.concatenate((pad_rows, value_proj)), short_segs, SLAB, short_taps)
    ext_short = jnp.concatenate((jnp.zeros((tile_rows, D), jnp.bfloat16), filtered))
    medium_segs = segment_ids(jnp.arange(SLAB + tile_rows, dtype=jnp.int32) - tile_rows, genome_lengths)
    toeplitz = medium_toeplitz(medium_taps).astype(jnp.float32)
    tile_count = SLAB // tile_rows

    def medium_block(tile_index):
        start = tile_index * tile_rows
        window = lax.dynamic_slice_in_dim(ext_short, start, 2 * tile_rows, 0)
        window_segs = lax.dynamic_slice_in_dim(medium_segs, start, 2 * tile_rows, 0)
        own_segs = lax.dynamic_slice_in_dim(segments, start, tile_rows, 0)
        same_genome = own_segs[:, None] == window_segs[None, :]
        matrix = jnp.where(same_genome[None], toeplitz, jnp.zeros_like(toeplitz))
        grouped = window.astype(jnp.float32).reshape(2 * tile_rows, GROUPS, GROUP)
        return jnp.einsum('gts,sgi->tgi', matrix, grouped, precision=highest)
    medium = lax.map(medium_block, jnp.arange(tile_count, dtype=jnp.int32)).reshape(SLAB, D).astype(jnp.bfloat16)
    long_toeplitz, outward, inward, decay_re, decay_im = modal_tables(modal_poles)
    signal = medium.astype(jnp.float32).reshape(tile_count, tile_rows, GROUPS, GROUP)
    tile_segs = segments.reshape(tile_count, tile_rows)
    before = segment_ids(jnp.arange(tile_count, dtype=jnp.int32) * tile_rows - 1, genome_lengths)
    skip_grouped = skip_gain.reshape(GROUPS, GROUP)

    def chain_step(carry_in, inputs):
        state_re, state_im = carry_in
        block_in, own_segs, seg_before = inputs
        same_genome = own_segs[:, None] == own_segs[None, :]
        matrix = jnp.where(same_genome[None], long_toeplitz, jnp.zeros_like(long_toeplitz))
        local_part = jnp.einsum('gts,sgi->tgi', matrix, block_in, precision=highest)
        keep_mask = (own_segs == seg_before).astype(jnp.float32)
        carried_part = jnp.einsum('gtm,gim->tgi', outward, jnp.concatenate((state_re, state_im), axis=2), precision=highest) * keep_mask[:, None, None]
        end_mask = (own_segs == own_segs[-1]).astype(jnp.float32)
        block_states = jnp.einsum('gsm,sgi->gim', inward, block_in * end_mask[:, None, None], precision=highest)
        kept_flag = (own_segs[-1] == seg_before).astype(jnp.float32)
        step_re = (decay_re * kept_flag)[:, None, :]
        step_im = (decay_im * kept_flag)[:, None, :]
        new_re = step_re * state_re - step_im * state_im + block_states[..., :MODES]
        new_im = step_re * state_im + step_im * state_re + block_states[..., MODES:]
        output = local_part + carried_part + skip_grouped[None] * block_in
        return ((new_re, new_im), output)
    start_state = (jnp.zeros((GROUPS, GROUP, MODES), jnp.float32), jnp.zeros((GROUPS, GROUP, MODES), jnp.float32))
    unused_state, longconv = lax.scan(chain_step, start_state, (signal, tile_segs, before))
    mixed = (query_proj.astype(jnp.float32) * longconv.reshape(SLAB, D)).astype(jnp.bfloat16)
    mixed_wide = mixed.astype(jnp.float32)
    mean_square = lax.optimization_barrier(jnp.mean(mixed_wide * mixed_wide, axis=1))
    normed = (mixed_wide * lax.rsqrt(mean_square + norm_eps)[:, None] * norm_gain[None, :]).astype(jnp.bfloat16)
    logits = jnp.dot(normed, unembed, preferred_element_type=jnp.float32)
    token_logprob = log_probs(logits, token_ids)
    genome_index = jnp.arange(NGEN, dtype=jnp.int32)
    totals = lax.optimization_barrier(jnp.sum(jnp.where(segments[:, None] == genome_index[None, :], token_logprob[:, None], jnp.zeros((SLAB, NGEN), jnp.float32)), axis=0))
    genome_score = totals / genome_lengths.astype(jnp.float32)
    return (token_logprob, genome_score)
```

```python
import jax
import jax.numpy as jnp
from jax import lax
from jax.sharding import PartitionSpec as P

D = 8192
GROUP = 16


tile_rows = 128
short_margin = 8
norm_eps = 1e-05


def from_behind(shard, axis, by):
    count = lax.axis_size(axis)
    pairs = [(i, i + by) for i in range(count) if 0 <= i + by < count]
    return lax.ppermute(shard, axis, pairs)


def entering_2(part, axis, combine, identity):
    place = lax.axis_index(axis)
    lead = part[0].shape[0]
    flat = jnp.concatenate([a.reshape(lead, -1) for a in part], axis=1)
    gathered_flat = lax.all_gather(flat, axis)
    gathered = []
    offset = 0
    for a in part:
        width = a.size // lead
        gathered.append(gathered_flat[:, :, offset : offset + width].reshape((-1,) + a.shape))
        offset += width
    gathered = tuple(gathered)
    state = jax.tree.map(lambda a, e: jnp.zeros_like(a) + jnp.asarray(e, a.dtype), part, identity)

    def one(step, state):
        return combine(
            state, jax.tree.map(lambda a: lax.dynamic_index_in_dim(a, step, 0, False), gathered)
        )

    return lax.fori_loop(0, place, one, state)


def segment_ids(positions, genome_lengths):
    starts = jnp.cumsum(genome_lengths) - genome_lengths
    at_or_past = (positions[:, None] >= starts[None, :]).astype(jnp.int32)
    return jnp.sum(at_or_past, axis=1) - 1


def short_filter(keys_in, values_in, seg_list, out_rows, short_taps):
    gated = keys_in.astype(jnp.float32) * values_in.astype(jnp.float32)
    total_rows = keys_in.shape[0]
    lead_rows = total_rows - out_rows
    own_segs = seg_list[lead_rows:]
    result = jnp.zeros((out_rows, keys_in.shape[1]), jnp.float32)
    for lag_index in range(short_taps.shape[0]):
        shifted = gated[lead_rows - lag_index : total_rows - lag_index]
        same_genome = (seg_list[lead_rows - lag_index : total_rows - lag_index] == own_segs).astype(
            jnp.float32
        )
        result = (
            result
            + short_taps[lag_index].astype(jnp.float32)[None, :] * shifted * same_genome[:, None]
        )
    return result.astype(jnp.bfloat16)


def banded(q, width):
    rows = q.shape[1] - width + 1
    return jnp.stack([q[:, rows - 1 - t : rows - 1 - t + width] for t in range(rows)], axis=1)


def medium_toeplitz(medium_taps):
    tap_count = medium_taps.shape[0]
    flipped = medium_taps.T[:, ::-1]
    q = jnp.concatenate(
        (
            jnp.zeros((flipped.shape[0], tile_rows), flipped.dtype),
            flipped,
            jnp.zeros((flipped.shape[0], 2 * tile_rows - tap_count - 1), flipped.dtype),
        ),
        axis=1,
    )
    return banded(q, 2 * tile_rows)


def modal_tables(modal_poles):
    decay_rate = modal_poles[0]
    angles = modal_poles[1]
    residue_re = modal_poles[2]
    residue_im = modal_poles[3]
    powers = jnp.arange(tile_rows + 1).astype(jnp.float32)[:, None, None]
    magnitude = jnp.exp(-powers * decay_rate[None])
    power_re = magnitude * jnp.cos(powers * angles[None])
    power_im = magnitude * jnp.sin(powers * angles[None])
    kernel_re = residue_re[None] * power_re - residue_im[None] * power_im
    kernel_im = residue_re[None] * power_im + residue_im[None] * power_re
    kernel = jnp.sum(kernel_re[:tile_rows], axis=2)
    flipped = kernel.T[:, ::-1]
    q = jnp.concatenate((flipped, jnp.zeros((flipped.shape[0], tile_rows - 1), flipped.dtype)), axis=1)
    toeplitz = banded(q, tile_rows)
    outward = jnp.transpose(jnp.concatenate((kernel_re[1:], -kernel_im[1:]), axis=2), (1, 0, 2))
    inward = jnp.transpose(
        jnp.concatenate((power_re[tile_rows - 1 :: -1], power_im[tile_rows - 1 :: -1]), axis=2),
        (1, 0, 2),
    )
    return (toeplitz, outward, inward, power_re[tile_rows], power_im[tile_rows])


def split_table(table):
    upper = table.astype(jnp.bfloat16)
    lower = (table - upper.astype(jnp.float32)).astype(jnp.bfloat16)
    return (upper, lower)


def complex_link(earlier, later):
    early_are, early_aim, early_sre, early_sim = earlier
    late_are, late_aim, late_sre, late_sim = later
    lead_re = late_are[..., None, :]
    lead_im = late_aim[..., None, :]
    return (
        late_are * early_are - late_aim * early_aim,
        late_are * early_aim + late_aim * early_are,
        lead_re * early_sre - lead_im * early_sim + late_sre,
        lead_re * early_sim + lead_im * early_sre + late_sim,
    )


def log_probs(logits, targets):
    vocab_ids = jnp.arange(logits.shape[1], dtype=jnp.int32)
    picked = jnp.sum(
        jnp.where(targets[:, None] == vocab_ids[None, :], logits, jnp.zeros_like(logits)), axis=1
    )
    return picked - jnp.log(jnp.sum(jnp.exp(logits), axis=1))


def channel_logits(normed_cols, unembed):
    return lax.dot_general(
        normed_cols, unembed, (((0,), (0,)), ((), ())), preferred_element_type=jnp.float32
    )


def per_device(
    query_proj,
    key_proj,
    value_proj,
    short_taps,
    medium_taps,
    modal_poles,
    skip_gain,
    norm_gain,
    unembed,
    token_ids,
    genome_lengths,
):
    highest = lax.Precision.HIGHEST
    row_count, chan_count = query_proj.shape
    group_count = chan_count // GROUP
    mode_count = modal_poles.shape[2]
    tile_count = row_count // tile_rows
    first_row = lax.axis_index("seq") * row_count
    segments = segment_ids(first_row + jnp.arange(row_count, dtype=jnp.int32), genome_lengths)
    edge_pair = from_behind(
        jnp.stack((key_proj[row_count - short_margin :], value_proj[row_count - short_margin :])),
        "seq",
        1,
    )
    ext_segs = segment_ids(
        first_row - short_margin + jnp.arange(row_count + short_margin, dtype=jnp.int32),
        genome_lengths,
    )
    filtered = short_filter(
        jnp.concatenate((edge_pair[0], key_proj)),
        jnp.concatenate((edge_pair[1], value_proj)),
        ext_segs,
        row_count,
        short_taps,
    )
    previous = from_behind(filtered[row_count - tile_rows :], "seq", 1)
    ext_short = jnp.concatenate((previous, filtered)).T.reshape(
        group_count, GROUP, row_count + tile_rows
    )
    medium_segs = segment_ids(
        first_row - tile_rows + jnp.arange(row_count + tile_rows, dtype=jnp.int32), genome_lengths
    )
    toeplitz = medium_toeplitz(medium_taps)

    def medium_block(tile_index):
        start = tile_index * tile_rows
        window = lax.dynamic_slice_in_dim(ext_short, start, 2 * tile_rows, 2)
        window_segs = lax.dynamic_slice_in_dim(medium_segs, start, 2 * tile_rows, 0)
        own_segs = lax.dynamic_slice_in_dim(segments, start, tile_rows, 0)
        same_genome = own_segs[:, None] == window_segs[None, :]
        matrix = jnp.where(same_genome[None], toeplitz, jnp.zeros_like(toeplitz))
        return jnp.einsum(
            "gts,gis->git", matrix, window, preferred_element_type=jnp.float32
        ).astype(jnp.bfloat16)

    signal = lax.map(medium_block, jnp.arange(tile_count, dtype=jnp.int32))
    long_toeplitz, outward, inward, decay_re, decay_im = modal_tables(modal_poles)
    toeplitz_upper, toeplitz_lower = split_table(long_toeplitz)
    inward_upper, inward_lower = split_table(inward)
    tile_segs = segments.reshape(tile_count, tile_rows)
    before = segment_ids(
        first_row + jnp.arange(tile_count, dtype=jnp.int32) * tile_rows - 1, genome_lengths
    )

    def intra_block(inputs):
        block_in, own_segs = inputs
        same_genome = (own_segs[:, None] == own_segs[None, :])[None]
        upper = jnp.where(same_genome, toeplitz_upper, jnp.zeros_like(toeplitz_upper))
        lower = jnp.where(same_genome, toeplitz_lower, jnp.zeros_like(toeplitz_lower))
        return jnp.einsum(
            "gts,gis->git", upper, block_in, preferred_element_type=jnp.float32
        ) + jnp.einsum("gts,gis->git", lower, block_in, preferred_element_type=jnp.float32)

    local_part = lax.map(intra_block, (signal, tile_segs))
    end_keep = (tile_segs == tile_segs[:, -1:])[:, None, None, :]
    masked_signal = jnp.where(end_keep, signal, jnp.zeros_like(signal))
    states = jnp.einsum(
        "gsm,jgis->jgim", inward_upper, masked_signal, preferred_element_type=jnp.float32
    ) + jnp.einsum(
        "gsm,jgis->jgim", inward_lower, masked_signal, preferred_element_type=jnp.float32
    )
    carried = (tile_segs[:, -1] == before).astype(jnp.float32)

    def chain_link(carry_in, inputs):
        block_states, kept_flag = inputs
        step = (
            decay_re * kept_flag,
            decay_im * kept_flag,
            block_states[..., :mode_count],
            block_states[..., mode_count:],
        )
        return (complex_link(carry_in, step), carry_in)

    state_zero = jnp.zeros((group_count, GROUP, mode_count), jnp.float32)
    start_carry = (
        jnp.ones((group_count, mode_count), jnp.float32),
        jnp.zeros((group_count, mode_count), jnp.float32),
        state_zero,
        state_zero,
    )
    summary, entering = lax.scan(chain_link, start_carry, (states, carried))
    incoming = entering_2(
        (summary[0], summary[1], summary[2], summary[3]),
        "seq",
        complex_link,
        (start_carry[0], start_carry[1], start_carry[2], start_carry[3]),
    )
    incoming_re = incoming[2]
    incoming_im = incoming[3]
    reach_re = entering[0][:, :, None, :]
    reach_im = entering[1][:, :, None, :]
    full_re = entering[2] + reach_re * incoming_re - reach_im * incoming_im
    full_im = entering[3] + reach_re * incoming_im + reach_im * incoming_re
    keep_mask = (tile_segs == before[:, None]).astype(jnp.float32)
    carried_part = (
        jnp.einsum(
            "gtm,jgim->jgit",
            outward,
            jnp.concatenate((full_re, full_im), axis=3),
            precision=highest,
        )
        * keep_mask[:, None, None, :]
    )
    longconv = (
        local_part
        + carried_part
        + skip_gain.reshape(group_count, GROUP)[None, :, :, None] * signal.astype(jnp.float32)
    )
    long_cols = jnp.transpose(longconv, (1, 2, 0, 3)).reshape(chan_count, row_count)
    mixed = (query_proj.T.astype(jnp.float32) * long_cols).astype(jnp.bfloat16)
    mixed_wide = mixed.astype(jnp.float32)
    squares = lax.psum(jnp.sum(mixed_wide * mixed_wide, axis=0), ("chan", "rep"))
    normed = (mixed_wide * lax.rsqrt(squares / D + norm_eps)[None, :] * norm_gain[:, None]).astype(
        jnp.bfloat16
    )
    partial_value = channel_logits(normed, unembed)
    logits = lax.psum(partial_value, ("chan", "rep"))
    logprob = log_probs(logits, token_ids)
    genome_index = jnp.arange(genome_lengths.shape[0], dtype=jnp.int32)
    genome_part = jnp.sum(
        jnp.where(
            segments[:, None] == genome_index[None, :],
            logprob[:, None],
            jnp.zeros((row_count, genome_lengths.shape[0]), jnp.float32),
        ),
        axis=0,
    )
    totals = lax.psum(genome_part, "seq")
    return (logprob, totals / genome_lengths.astype(jnp.float32))


def solution(mesh):
    return jax.shard_map(
        per_device,
        mesh=mesh,
        in_specs=(
            P(("groups", "seq"), ("chan", "rep")),
            P(("groups", "seq"), ("chan", "rep")),
            P(("groups", "seq"), ("chan", "rep")),
            P(None, ("chan", "rep")),
            P(None, ("chan", "rep")),
            P(None, ("chan", "rep"), None),
            P(("chan", "rep")),
            P(("chan", "rep")),
            P(("chan", "rep"), None),
            P(("groups", "seq")),
            P("groups"),
        ),
        out_specs=(P(("groups", "seq")), P("groups")),
        check_vma=False,
    )
```

```python
import jax
import jax.numpy as jnp
from jax import lax
from jax.sharding import PartitionSpec as P

D = 8192
GROUP = 16


tile_rows = 128
short_margin = 8
norm_eps = 1e-05


def from_behind(shard, axis, by):
    count = lax.axis_size(axis)
    pairs = [(i, i + by) for i in range(count) if 0 <= i + by < count]
    return lax.ppermute(shard, axis, pairs)


def entering_2(part, axis, combine, identity):
    place = lax.axis_index(axis)
    lead = part[0].shape[0]
    flat = jnp.concatenate([a.reshape(lead, -1) for a in part], axis=1)
    gathered_flat = lax.all_gather(flat, axis)
    gathered = []
    offset = 0
    for a in part:
        width = a.size // lead
        gathered.append(gathered_flat[:, :, offset : offset + width].reshape((-1,) + a.shape))
        offset += width
    gathered = tuple(gathered)
    state = jax.tree.map(lambda a, e: jnp.zeros_like(a) + jnp.asarray(e, a.dtype), part, identity)

    def one(step, state):
        return combine(
            state, jax.tree.map(lambda a: lax.dynamic_index_in_dim(a, step, 0, False), gathered)
        )

    return lax.fori_loop(0, place, one, state)


def segment_ids(positions, genome_lengths):
    starts = jnp.cumsum(genome_lengths) - genome_lengths
    at_or_past = (positions[:, None] >= starts[None, :]).astype(jnp.int32)
    return jnp.sum(at_or_past, axis=1) - 1


def short_filter(keys_in, values_in, seg_list, out_rows, short_taps):
    gated = keys_in.astype(jnp.float32) * values_in.astype(jnp.float32)
    total_rows = keys_in.shape[0]
    lead_rows = total_rows - out_rows
    own_segs = seg_list[lead_rows:]
    result = jnp.zeros((out_rows, keys_in.shape[1]), jnp.float32)
    for lag_index in range(short_taps.shape[0]):
        shifted = gated[lead_rows - lag_index : total_rows - lag_index]
        same_genome = (seg_list[lead_rows - lag_index : total_rows - lag_index] == own_segs).astype(
            jnp.float32
        )
        result = (
            result
            + short_taps[lag_index].astype(jnp.float32)[None, :] * shifted * same_genome[:, None]
        )
    return result.astype(jnp.bfloat16)


def lag_select(table, rows, cols, shift):
    lag_count = table.shape[0]
    lag_ids = lax.optimization_barrier(jnp.arange(lag_count, dtype=jnp.int32))
    out_pos = jnp.arange(rows, dtype=jnp.int32)[:, None]
    in_pos = jnp.arange(cols, dtype=jnp.int32)[None, :]
    lag_grid = out_pos + shift - in_pos
    one_hot = (lag_grid[None] == lag_ids[:, None, None]).astype(table.dtype)
    picked = lax.dot_general(
        table, one_hot, (((0,), (0,)), ((), ())), preferred_element_type=jnp.float32
    )
    return picked.astype(table.dtype)


def medium_toeplitz(medium_taps):
    return lag_select(medium_taps, tile_rows, 2 * tile_rows, tile_rows)


def modal_tables(modal_poles):
    decay_rate = modal_poles[0]
    angles = modal_poles[1]
    residue_re = modal_poles[2]
    residue_im = modal_poles[3]
    powers = jnp.arange(tile_rows + 1).astype(jnp.float32)[:, None, None]
    magnitude = jnp.exp(-powers * decay_rate[None])
    power_re = magnitude * jnp.cos(powers * angles[None])
    power_im = magnitude * jnp.sin(powers * angles[None])
    kernel_re = residue_re[None] * power_re - residue_im[None] * power_im
    kernel_im = residue_re[None] * power_im + residue_im[None] * power_re
    kernel = jnp.sum(kernel_re[:tile_rows], axis=2)
    upper, lower = split_table(kernel)
    group_count = kernel.shape[1]
    both = lag_select(jnp.concatenate((upper, lower), axis=1), tile_rows, tile_rows, 0)
    toeplitz = (both[:group_count], both[group_count:])
    outward = jnp.transpose(jnp.concatenate((kernel_re[1:], -kernel_im[1:]), axis=2), (1, 0, 2))
    inward = jnp.transpose(
        jnp.concatenate((power_re[tile_rows - 1 :: -1], power_im[tile_rows - 1 :: -1]), axis=2),
        (1, 0, 2),
    )
    return (toeplitz, outward, inward, power_re[tile_rows], power_im[tile_rows])


def split_table(table):
    upper = table.astype(jnp.bfloat16)
    lower = (table - upper.astype(jnp.float32)).astype(jnp.bfloat16)
    return (upper, lower)


def complex_link(earlier, later):
    early_are, early_aim, early_sre, early_sim = earlier
    late_are, late_aim, late_sre, late_sim = later
    lead_re = late_are[..., None, :]
    lead_im = late_aim[..., None, :]
    return (
        late_are * early_are - late_aim * early_aim,
        late_are * early_aim + late_aim * early_are,
        lead_re * early_sre - lead_im * early_sim + late_sre,
        lead_re * early_sim + lead_im * early_sre + late_sim,
    )


def log_probs(logits, targets):
    vocab_ids = jnp.arange(logits.shape[1], dtype=jnp.int32)
    picked = jnp.sum(
        jnp.where(targets[:, None] == vocab_ids[None, :], logits, jnp.zeros_like(logits)), axis=1
    )
    return picked - jnp.log(jnp.sum(jnp.exp(logits), axis=1))


def channel_logits(normed_cols, unembed):
    return lax.dot_general(
        normed_cols, unembed, (((0,), (0,)), ((), ())), preferred_element_type=jnp.float32
    )


def per_device(
    query_proj,
    key_proj,
    value_proj,
    short_taps,
    medium_taps,
    modal_poles,
    skip_gain,
    norm_gain,
    unembed,
    token_ids,
    genome_lengths,
):
    highest = lax.Precision.HIGHEST
    row_count, chan_count = query_proj.shape
    group_count = chan_count // GROUP
    mode_count = modal_poles.shape[2]
    tile_count = row_count // tile_rows
    first_row = lax.axis_index("seq") * row_count
    segments = segment_ids(first_row + jnp.arange(row_count, dtype=jnp.int32), genome_lengths)
    edge_pair = from_behind(
        jnp.stack((key_proj[row_count - short_margin :], value_proj[row_count - short_margin :])),
        "seq",
        1,
    )
    ext_segs = segment_ids(
        first_row - short_margin + jnp.arange(row_count + short_margin, dtype=jnp.int32),
        genome_lengths,
    )
    filtered = short_filter(
        jnp.concatenate((edge_pair[0], key_proj)),
        jnp.concatenate((edge_pair[1], value_proj)),
        ext_segs,
        row_count,
        short_taps,
    )
    previous = from_behind(filtered[row_count - tile_rows :], "seq", 1)
    ext_short = jnp.concatenate((previous, filtered)).T.reshape(
        group_count, GROUP, row_count + tile_rows
    )
    medium_segs = segment_ids(
        first_row - tile_rows + jnp.arange(row_count + tile_rows, dtype=jnp.int32), genome_lengths
    )
    toeplitz = medium_toeplitz(medium_taps)

    def medium_block(tile_index):
        start = tile_index * tile_rows
        window = lax.dynamic_slice_in_dim(ext_short, start, 2 * tile_rows, 2)
        window_segs = lax.dynamic_slice_in_dim(medium_segs, start, 2 * tile_rows, 0)
        own_segs = lax.dynamic_slice_in_dim(segments, start, tile_rows, 0)
        same_genome = own_segs[:, None] == window_segs[None, :]
        matrix = jnp.where(same_genome[None], toeplitz, jnp.zeros_like(toeplitz))
        return jnp.einsum(
            "gts,gis->git", matrix, window, preferred_element_type=jnp.float32
        ).astype(jnp.bfloat16)

    signal = lax.map(medium_block, jnp.arange(tile_count, dtype=jnp.int32))
    long_toeplitz, outward, inward, decay_re, decay_im = modal_tables(modal_poles)
    toeplitz_upper, toeplitz_lower = long_toeplitz
    inward_upper, inward_lower = split_table(inward)
    tile_segs = segments.reshape(tile_count, tile_rows)
    before = segment_ids(
        first_row + jnp.arange(tile_count, dtype=jnp.int32) * tile_rows - 1, genome_lengths
    )

    def intra_block(inputs):
        block_in, own_segs = inputs
        same_genome = (own_segs[:, None] == own_segs[None, :])[None]
        upper = jnp.where(same_genome, toeplitz_upper, jnp.zeros_like(toeplitz_upper))
        lower = jnp.where(same_genome, toeplitz_lower, jnp.zeros_like(toeplitz_lower))
        return jnp.einsum(
            "gts,gis->git", upper, block_in, preferred_element_type=jnp.float32
        ) + jnp.einsum("gts,gis->git", lower, block_in, preferred_element_type=jnp.float32)

    local_part = lax.map(intra_block, (signal, tile_segs))
    end_keep = (tile_segs == tile_segs[:, -1:])[:, None, None, :]
    masked_signal = jnp.where(end_keep, signal, jnp.zeros_like(signal))
    states = jnp.einsum(
        "gsm,jgis->jgim", inward_upper, masked_signal, preferred_element_type=jnp.float32
    ) + jnp.einsum(
        "gsm,jgis->jgim", inward_lower, masked_signal, preferred_element_type=jnp.float32
    )
    carried = (tile_segs[:, -1] == before).astype(jnp.float32)

    def chain_link(carry_in, inputs):
        block_states, kept_flag = inputs
        step = (
            decay_re * kept_flag,
            decay_im * kept_flag,
            block_states[..., :mode_count],
            block_states[..., mode_count:],
        )
        return (complex_link(carry_in, step), carry_in)

    state_zero = jnp.zeros((group_count, GROUP, mode_count), jnp.float32)
    start_carry = (
        jnp.ones((group_count, mode_count), jnp.float32),
        jnp.zeros((group_count, mode_count), jnp.float32),
        state_zero,
        state_zero,
    )
    summary, entering = lax.scan(chain_link, start_carry, (states, carried))
    incoming = entering_2(
        (summary[0], summary[1], summary[2], summary[3]),
        "seq",
        complex_link,
        (start_carry[0], start_carry[1], start_carry[2], start_carry[3]),
    )
    incoming_re = incoming[2]
    incoming_im = incoming[3]
    reach_re = entering[0][:, :, None, :]
    reach_im = entering[1][:, :, None, :]
    full_re = entering[2] + reach_re * incoming_re - reach_im * incoming_im
    full_im = entering[3] + reach_re * incoming_im + reach_im * incoming_re
    keep_mask = (tile_segs == before[:, None]).astype(jnp.float32)
    carried_part = (
        jnp.einsum(
            "gtm,jgim->jgit",
            outward,
            jnp.concatenate((full_re, full_im), axis=3),
            precision=highest,
        )
        * keep_mask[:, None, None, :]
    )
    longconv = (
        local_part
        + carried_part
        + skip_gain.reshape(group_count, GROUP)[None, :, :, None] * signal.astype(jnp.float32)
    )
    long_cols = jnp.transpose(longconv, (1, 2, 0, 3)).reshape(chan_count, row_count)
    mixed = (query_proj.T.astype(jnp.float32) * long_cols).astype(jnp.bfloat16)
    mixed_wide = mixed.astype(jnp.float32)
    squares = lax.psum(jnp.sum(mixed_wide * mixed_wide, axis=0), ("chan", "rep"))
    normed = (mixed_wide * lax.rsqrt(squares / D + norm_eps)[None, :] * norm_gain[:, None]).astype(
        jnp.bfloat16
    )
    partial_value = channel_logits(normed, unembed)
    logits = lax.psum(partial_value, ("chan", "rep"))
    logprob = log_probs(logits, token_ids)
    genome_index = jnp.arange(genome_lengths.shape[0], dtype=jnp.int32)
    genome_part = jnp.sum(
        jnp.where(
            segments[:, None] == genome_index[None, :],
            logprob[:, None],
            jnp.zeros((row_count, genome_lengths.shape[0]), jnp.float32),
        ),
        axis=0,
    )
    totals = lax.psum(genome_part, "seq")
    return (logprob, totals / genome_lengths.astype(jnp.float32))


def solution(mesh):
    return jax.shard_map(
        per_device,
        mesh=mesh,
        in_specs=(
            P(("groups", "seq"), ("chan", "rep")),
            P(("groups", "seq"), ("chan", "rep")),
            P(("groups", "seq"), ("chan", "rep")),
            P(None, ("chan", "rep")),
            P(None, ("chan", "rep")),
            P(None, ("chan", "rep"), None),
            P(("chan", "rep")),
            P(("chan", "rep")),
            P(("chan", "rep"), None),
            P(("groups", "seq")),
            P("groups"),
        ),
        out_specs=(P(("groups", "seq")), P("groups")),
        check_vma=False,
    )
```

```python
import jax
import jax.numpy as jnp
from jax import lax
from jax.sharding import PartitionSpec as P

D = 8192
GROUP = 16


tile_rows = 128
short_margin = 8
norm_eps = 1e-05


def from_behind(shard, axis, by):
    count = lax.axis_size(axis)
    pairs = [(i, i + by) for i in range(count) if 0 <= i + by < count]
    return lax.ppermute(shard, axis, pairs)


def entering_2(part, axis, combine, identity):
    place = lax.axis_index(axis)
    lead = part[0].shape[0]
    flat = jnp.concatenate([a.reshape(lead, -1) for a in part], axis=1)
    gathered_flat = lax.all_gather(flat, axis)
    gathered = []
    offset = 0
    for a in part:
        width = a.size // lead
        gathered.append(gathered_flat[:, :, offset : offset + width].reshape((-1,) + a.shape))
        offset += width
    gathered = tuple(gathered)
    state = jax.tree.map(lambda a, e: jnp.zeros_like(a) + jnp.asarray(e, a.dtype), part, identity)

    def one(step, state):
        return combine(
            state, jax.tree.map(lambda a: lax.dynamic_index_in_dim(a, step, 0, False), gathered)
        )

    return lax.fori_loop(0, place, one, state)


def segment_ids(positions, genome_lengths):
    starts = jnp.cumsum(genome_lengths) - genome_lengths
    at_or_past = (positions[:, None] >= starts[None, :]).astype(jnp.int32)
    return jnp.sum(at_or_past, axis=1) - 1


def short_filter(keys_in, values_in, seg_list, out_rows, short_taps):
    gated = keys_in.astype(jnp.float32) * values_in.astype(jnp.float32)
    total_rows = keys_in.shape[0]
    lead_rows = total_rows - out_rows
    own_segs = seg_list[lead_rows:]
    result = jnp.zeros((out_rows, keys_in.shape[1]), jnp.float32)
    for lag_index in range(short_taps.shape[0]):
        shifted = gated[lead_rows - lag_index : total_rows - lag_index]
        same_genome = (seg_list[lead_rows - lag_index : total_rows - lag_index] == own_segs).astype(
            jnp.float32
        )
        result = (
            result
            + short_taps[lag_index].astype(jnp.float32)[None, :] * shifted * same_genome[:, None]
        )
    return result.astype(jnp.bfloat16)


def lag_select(table, rows, cols, shift):
    lag_count = table.shape[0]
    lag_ids = lax.optimization_barrier(jnp.arange(lag_count, dtype=jnp.int32))
    out_pos = jnp.arange(rows, dtype=jnp.int32)[:, None]
    in_pos = jnp.arange(cols, dtype=jnp.int32)[None, :]
    lag_grid = out_pos + shift - in_pos
    one_hot = (lag_grid[None] == lag_ids[:, None, None]).astype(table.dtype)
    picked = lax.dot_general(
        table, one_hot, (((0,), (0,)), ((), ())), preferred_element_type=jnp.float32
    )
    return picked.astype(table.dtype)


def medium_toeplitz(medium_taps):
    return lag_select(medium_taps, tile_rows, 2 * tile_rows, tile_rows)


def modal_tables(modal_poles):
    decay_rate = modal_poles[0]
    angles = modal_poles[1]
    residue_re = modal_poles[2]
    residue_im = modal_poles[3]
    powers = jnp.arange(tile_rows + 1).astype(jnp.float32)[:, None, None]
    magnitude = jnp.exp(-powers * decay_rate[None])
    power_re = magnitude * jnp.cos(powers * angles[None])
    power_im = magnitude * jnp.sin(powers * angles[None])
    kernel_re = residue_re[None] * power_re - residue_im[None] * power_im
    kernel_im = residue_re[None] * power_im + residue_im[None] * power_re
    kernel = jnp.sum(kernel_re[:tile_rows], axis=2)
    upper, lower = split_table(kernel)
    group_count = kernel.shape[1]
    both = lag_select(jnp.concatenate((upper, lower), axis=1), tile_rows, tile_rows, 0)
    toeplitz = (both[:group_count], both[group_count:])
    outward = jnp.transpose(jnp.concatenate((kernel_re[1:], -kernel_im[1:]), axis=2), (1, 0, 2))
    inward = jnp.transpose(
        jnp.concatenate((power_re[tile_rows - 1 :: -1], power_im[tile_rows - 1 :: -1]), axis=2),
        (1, 0, 2),
    )
    return (toeplitz, outward, inward, power_re[tile_rows], power_im[tile_rows])


def split_table(table):
    upper = table.astype(jnp.bfloat16)
    lower = (table - upper.astype(jnp.float32)).astype(jnp.bfloat16)
    return (upper, lower)


def complex_link(earlier, later):
    early_are, early_aim, early_sre, early_sim = earlier
    late_are, late_aim, late_sre, late_sim = later
    lead_re = late_are[..., None, :]
    lead_im = late_aim[..., None, :]
    return (
        late_are * early_are - late_aim * early_aim,
        late_are * early_aim + late_aim * early_are,
        lead_re * early_sre - lead_im * early_sim + late_sre,
        lead_re * early_sim + lead_im * early_sre + late_sim,
    )


def log_probs(logits, targets):
    vocab_ids = jnp.arange(logits.shape[1], dtype=jnp.int32)
    picked = jnp.sum(
        jnp.where(targets[:, None] == vocab_ids[None, :], logits, jnp.zeros_like(logits)), axis=1
    )
    return picked - jnp.log(jnp.sum(jnp.exp(logits), axis=1))


def channel_logits(normed_cols, unembed):
    return lax.dot_general(
        normed_cols, unembed, (((0,), (0,)), ((), ())), preferred_element_type=jnp.float32
    )


def per_device(
    query_proj,
    key_proj,
    value_proj,
    short_taps,
    medium_taps,
    modal_poles,
    skip_gain,
    norm_gain,
    unembed,
    token_ids,
    genome_lengths,
):
    highest = lax.Precision.HIGHEST
    row_count, chan_count = query_proj.shape
    group_count = chan_count // GROUP
    mode_count = modal_poles.shape[2]
    tile_count = row_count // tile_rows
    first_row = lax.axis_index("seq") * row_count
    segments = segment_ids(first_row + jnp.arange(row_count, dtype=jnp.int32), genome_lengths)
    halo = tile_rows + short_margin
    edge_pair = from_behind(
        jnp.stack((key_proj[row_count - halo :], value_proj[row_count - halo :])),
        "seq",
        1,
    )
    ext_segs = segment_ids(
        first_row - halo + jnp.arange(row_count + halo, dtype=jnp.int32),
        genome_lengths,
    )
    filtered = short_filter(
        jnp.concatenate((edge_pair[0], key_proj)),
        jnp.concatenate((edge_pair[1], value_proj)),
        ext_segs,
        row_count + tile_rows,
        short_taps,
    )
    ext_short = filtered.T.reshape(group_count, GROUP, row_count + tile_rows)
    medium_segs = segment_ids(
        first_row - tile_rows + jnp.arange(row_count + tile_rows, dtype=jnp.int32), genome_lengths
    )
    toeplitz = medium_toeplitz(medium_taps)

    def medium_block(tile_index):
        start = tile_index * tile_rows
        window = lax.dynamic_slice_in_dim(ext_short, start, 2 * tile_rows, 2)
        window_segs = lax.dynamic_slice_in_dim(medium_segs, start, 2 * tile_rows, 0)
        own_segs = lax.dynamic_slice_in_dim(segments, start, tile_rows, 0)
        same_genome = own_segs[:, None] == window_segs[None, :]
        matrix = jnp.where(same_genome[None], toeplitz, jnp.zeros_like(toeplitz))
        return jnp.einsum(
            "gts,gis->git", matrix, window, preferred_element_type=jnp.float32
        ).astype(jnp.bfloat16)

    signal = lax.map(medium_block, jnp.arange(tile_count, dtype=jnp.int32))
    long_toeplitz, outward, inward, decay_re, decay_im = modal_tables(modal_poles)
    toeplitz_upper, toeplitz_lower = long_toeplitz
    inward_upper, inward_lower = split_table(inward)
    tile_segs = segments.reshape(tile_count, tile_rows)
    before = segment_ids(
        first_row + jnp.arange(tile_count, dtype=jnp.int32) * tile_rows - 1, genome_lengths
    )

    def intra_block(inputs):
        block_in, own_segs = inputs
        same_genome = (own_segs[:, None] == own_segs[None, :])[None]
        upper = jnp.where(same_genome, toeplitz_upper, jnp.zeros_like(toeplitz_upper))
        lower = jnp.where(same_genome, toeplitz_lower, jnp.zeros_like(toeplitz_lower))
        return jnp.einsum(
            "gts,gis->git", upper, block_in, preferred_element_type=jnp.float32
        ) + jnp.einsum("gts,gis->git", lower, block_in, preferred_element_type=jnp.float32)

    local_part = lax.map(intra_block, (signal, tile_segs))
    end_keep = (tile_segs == tile_segs[:, -1:])[:, None, None, :]
    masked_signal = jnp.where(end_keep, signal, jnp.zeros_like(signal))
    states = jnp.einsum(
        "gsm,jgis->jgim", inward_upper, masked_signal, preferred_element_type=jnp.float32
    ) + jnp.einsum(
        "gsm,jgis->jgim", inward_lower, masked_signal, preferred_element_type=jnp.float32
    )
    carried = (tile_segs[:, -1] == before).astype(jnp.float32)

    def chain_link(carry_in, inputs):
        block_states, kept_flag = inputs
        step = (
            decay_re * kept_flag,
            decay_im * kept_flag,
            block_states[..., :mode_count],
            block_states[..., mode_count:],
        )
        return (complex_link(carry_in, step), carry_in)

    state_zero = jnp.zeros((group_count, GROUP, mode_count), jnp.float32)
    start_carry = (
        jnp.ones((group_count, mode_count), jnp.float32),
        jnp.zeros((group_count, mode_count), jnp.float32),
        state_zero,
        state_zero,
    )
    summary, entering = lax.scan(chain_link, start_carry, (states, carried))
    incoming = entering_2(
        (summary[0], summary[1], summary[2], summary[3]),
        "seq",
        complex_link,
        (start_carry[0], start_carry[1], start_carry[2], start_carry[3]),
    )
    incoming_re = incoming[2]
    incoming_im = incoming[3]
    reach_re = entering[0][:, :, None, :]
    reach_im = entering[1][:, :, None, :]
    full_re = entering[2] + reach_re * incoming_re - reach_im * incoming_im
    full_im = entering[3] + reach_re * incoming_im + reach_im * incoming_re
    keep_mask = (tile_segs == before[:, None]).astype(jnp.float32)
    carried_part = (
        jnp.einsum(
            "gtm,jgim->jgit",
            outward,
            jnp.concatenate((full_re, full_im), axis=3),
            precision=highest,
        )
        * keep_mask[:, None, None, :]
    )
    longconv = (
        local_part
        + carried_part
        + skip_gain.reshape(group_count, GROUP)[None, :, :, None] * signal.astype(jnp.float32)
    )
    long_cols = jnp.transpose(longconv, (1, 2, 0, 3)).reshape(chan_count, row_count)
    mixed = (query_proj.T.astype(jnp.float32) * long_cols).astype(jnp.bfloat16)
    mixed_wide = mixed.astype(jnp.float32)
    squares = lax.psum(jnp.sum(mixed_wide * mixed_wide, axis=0), ("chan", "rep"))
    normed = (mixed_wide * lax.rsqrt(squares / D + norm_eps)[None, :] * norm_gain[:, None]).astype(
        jnp.bfloat16
    )
    partial_value = channel_logits(normed, unembed)
    lanes = ("chan", "rep")
    lane_count = lax.axis_size(lanes)
    piece = row_count // lane_count
    piece_at = lax.axis_index(lanes) * piece
    logits = lax.psum_scatter(partial_value, lanes, scatter_dimension=0, tiled=True)
    logprob = log_probs(logits, lax.dynamic_slice_in_dim(token_ids, piece_at, piece, 0))
    piece_segs = lax.dynamic_slice_in_dim(segments, piece_at, piece, 0)
    genome_index = jnp.arange(genome_lengths.shape[0], dtype=jnp.int32)
    genome_part = jnp.sum(
        jnp.where(
            piece_segs[:, None] == genome_index[None, :],
            logprob[:, None],
            jnp.zeros((piece, genome_lengths.shape[0]), jnp.float32),
        ),
        axis=0,
    )
    packed = lax.all_gather(jnp.concatenate((logprob, genome_part)), ("seq",) + lanes)
    own = lax.dynamic_slice_in_dim(packed, lax.axis_index("seq") * lane_count, lane_count, 0)
    totals = jnp.sum(packed[:, piece:], axis=0)
    return (own[:, :piece].reshape(row_count), totals / genome_lengths.astype(jnp.float32))


def solution(mesh):
    return jax.shard_map(
        per_device,
        mesh=mesh,
        in_specs=(
            P(("groups", "seq"), ("chan", "rep")),
            P(("groups", "seq"), ("chan", "rep")),
            P(("groups", "seq"), ("chan", "rep")),
            P(None, ("chan", "rep")),
            P(None, ("chan", "rep")),
            P(None, ("chan", "rep"), None),
            P(("chan", "rep")),
            P(("chan", "rep")),
            P(("chan", "rep"), None),
            P(("groups", "seq")),
            P("groups"),
        ),
        out_specs=(P(("groups", "seq")), P("groups")),
        check_vma=False,
    )
```

```python
import jax
import jax.numpy as jnp
from jax import lax
from jax.sharding import PartitionSpec as P

D = 8192
GROUP = 16


tile_rows = 128
short_margin = 8
norm_eps = 1e-05


def from_behind(shard, axis, by):
    count = lax.axis_size(axis)
    pairs = [(i, i + by) for i in range(count) if 0 <= i + by < count]
    return lax.ppermute(shard, axis, pairs)


def entering_2(part, axis, combine, identity):
    place = lax.axis_index(axis)
    lead = part[0].shape[0]
    flat = jnp.concatenate([a.reshape(lead, -1) for a in part], axis=1)
    gathered_flat = lax.all_gather(flat, axis)
    gathered = []
    offset = 0
    for a in part:
        width = a.size // lead
        gathered.append(gathered_flat[:, :, offset : offset + width].reshape((-1,) + a.shape))
        offset += width
    gathered = tuple(gathered)
    state = jax.tree.map(lambda a, e: jnp.zeros_like(a) + jnp.asarray(e, a.dtype), part, identity)

    def one(step, state):
        return combine(
            state, jax.tree.map(lambda a: lax.dynamic_index_in_dim(a, step, 0, False), gathered)
        )

    return lax.fori_loop(0, place, one, state)


def segment_ids(positions, genome_lengths):
    starts = jnp.cumsum(genome_lengths) - genome_lengths
    at_or_past = (positions[:, None] >= starts[None, :]).astype(jnp.int32)
    return jnp.sum(at_or_past, axis=1) - 1


def short_filter(keys_in, values_in, seg_list, out_rows, short_taps):
    gated = keys_in.astype(jnp.float32) * values_in.astype(jnp.float32)
    total_rows = keys_in.shape[0]
    lead_rows = total_rows - out_rows
    own_segs = seg_list[lead_rows:]
    result = jnp.zeros((out_rows, keys_in.shape[1]), jnp.float32)
    for lag_index in range(short_taps.shape[0]):
        shifted = gated[lead_rows - lag_index : total_rows - lag_index]
        same_genome = (seg_list[lead_rows - lag_index : total_rows - lag_index] == own_segs).astype(
            jnp.float32
        )
        result = (
            result
            + short_taps[lag_index].astype(jnp.float32)[None, :] * shifted * same_genome[:, None]
        )
    return result.astype(jnp.bfloat16)


def lag_select(table, rows, cols, shift):
    lag_count = table.shape[0]
    lag_ids = lax.optimization_barrier(jnp.arange(lag_count, dtype=jnp.int32))
    out_pos = jnp.arange(rows, dtype=jnp.int32)[:, None]
    in_pos = jnp.arange(cols, dtype=jnp.int32)[None, :]
    lag_grid = out_pos + shift - in_pos
    one_hot = (lag_grid[None] == lag_ids[:, None, None]).astype(table.dtype)
    picked = lax.dot_general(
        table, one_hot, (((0,), (0,)), ((), ())), preferred_element_type=jnp.float32
    )
    return picked.astype(table.dtype)


def medium_toeplitz(medium_taps):
    return lag_select(medium_taps, tile_rows, 2 * tile_rows, tile_rows)


def modal_tables(modal_poles):
    decay_rate = modal_poles[0]
    angles = modal_poles[1]
    residue_re = modal_poles[2]
    residue_im = modal_poles[3]
    powers = jnp.arange(tile_rows + 1).astype(jnp.float32)[:, None, None]
    magnitude = jnp.exp(-powers * decay_rate[None])
    power_re = magnitude * jnp.cos(powers * angles[None])
    power_im = magnitude * jnp.sin(powers * angles[None])
    kernel_re = residue_re[None] * power_re - residue_im[None] * power_im
    kernel_im = residue_re[None] * power_im + residue_im[None] * power_re
    kernel = jnp.sum(kernel_re[:tile_rows], axis=2)
    upper, lower = split_table(kernel)
    group_count = kernel.shape[1]
    both = lag_select(jnp.concatenate((upper, lower), axis=1), tile_rows, tile_rows, 0)
    toeplitz = (both[:group_count], both[group_count:])
    outward = jnp.transpose(jnp.concatenate((kernel_re[1:], -kernel_im[1:]), axis=2), (1, 0, 2))
    inward = jnp.transpose(
        jnp.concatenate((power_re[tile_rows - 1 :: -1], power_im[tile_rows - 1 :: -1]), axis=2),
        (1, 0, 2),
    )
    return (toeplitz, outward, inward, power_re[tile_rows], power_im[tile_rows])


def split_table(table):
    upper = table.astype(jnp.bfloat16)
    lower = (table - upper.astype(jnp.float32)).astype(jnp.bfloat16)
    return (upper, lower)


def complex_link(earlier, later):
    early_are, early_aim, early_sre, early_sim = earlier
    late_are, late_aim, late_sre, late_sim = later
    lead_re = late_are[..., None, :]
    lead_im = late_aim[..., None, :]
    return (
        late_are * early_are - late_aim * early_aim,
        late_are * early_aim + late_aim * early_are,
        lead_re * early_sre - lead_im * early_sim + late_sre,
        lead_re * early_sim + lead_im * early_sre + late_sim,
    )


def log_probs(logits, targets):
    vocab_ids = jnp.arange(logits.shape[1], dtype=jnp.int32)
    picked = jnp.sum(
        jnp.where(targets[:, None] == vocab_ids[None, :], logits, jnp.zeros_like(logits)), axis=1
    )
    return picked - jnp.log(jnp.sum(jnp.exp(logits), axis=1))


def channel_logits(normed_cols, unembed):
    return lax.dot_general(
        normed_cols, unembed, (((0,), (0,)), ((), ())), preferred_element_type=jnp.float32
    )


def per_device(
    query_proj,
    key_proj,
    value_proj,
    short_taps,
    medium_taps,
    modal_poles,
    skip_gain,
    norm_gain,
    unembed,
    token_ids,
    genome_lengths,
):
    highest = lax.Precision.HIGHEST
    row_count, chan_count = query_proj.shape
    group_count = chan_count // GROUP
    mode_count = modal_poles.shape[2]
    tile_count = row_count // tile_rows
    first_row = lax.axis_index("seq") * row_count
    segments = segment_ids(first_row + jnp.arange(row_count, dtype=jnp.int32), genome_lengths)
    halo = tile_rows + short_margin
    edge_pair = from_behind(
        jnp.stack((key_proj[row_count - halo :], value_proj[row_count - halo :])),
        "seq",
        1,
    )
    ext_segs = segment_ids(
        first_row - halo + jnp.arange(row_count + halo, dtype=jnp.int32),
        genome_lengths,
    )
    filtered = short_filter(
        jnp.concatenate((edge_pair[0], key_proj)),
        jnp.concatenate((edge_pair[1], value_proj)),
        ext_segs,
        row_count + tile_rows,
        short_taps,
    )
    ext_short = filtered.T.reshape(group_count, GROUP, row_count + tile_rows)
    medium_segs = segment_ids(
        first_row - tile_rows + jnp.arange(row_count + tile_rows, dtype=jnp.int32), genome_lengths
    )
    toeplitz = medium_toeplitz(medium_taps)

    def medium_block(tile_index):
        start = tile_index * tile_rows
        window = lax.dynamic_slice_in_dim(ext_short, start, 2 * tile_rows, 2)
        window_segs = lax.dynamic_slice_in_dim(medium_segs, start, 2 * tile_rows, 0)
        own_segs = lax.dynamic_slice_in_dim(segments, start, tile_rows, 0)
        same_genome = own_segs[:, None] == window_segs[None, :]
        matrix = jnp.where(same_genome[None], toeplitz, jnp.zeros_like(toeplitz))
        return jnp.einsum(
            "gts,gis->git", matrix, window, preferred_element_type=jnp.float32
        ).astype(jnp.bfloat16)

    signal = lax.map(medium_block, jnp.arange(tile_count, dtype=jnp.int32))
    long_toeplitz, outward, inward, decay_re, decay_im = modal_tables(modal_poles)
    toeplitz_upper, toeplitz_lower = long_toeplitz
    inward_upper, inward_lower = split_table(inward)
    tile_segs = segments.reshape(tile_count, tile_rows)
    before = segment_ids(
        first_row + jnp.arange(tile_count, dtype=jnp.int32) * tile_rows - 1, genome_lengths
    )

    def intra_block(inputs):
        block_in, own_segs = inputs
        same_genome = (own_segs[:, None] == own_segs[None, :])[None]
        upper = jnp.where(same_genome, toeplitz_upper, jnp.zeros_like(toeplitz_upper))
        lower = jnp.where(same_genome, toeplitz_lower, jnp.zeros_like(toeplitz_lower))
        return jnp.einsum(
            "gts,gis->git", upper, block_in, preferred_element_type=jnp.float32
        ) + jnp.einsum("gts,gis->git", lower, block_in, preferred_element_type=jnp.float32)

    local_part = lax.map(intra_block, (signal, tile_segs))
    end_keep = (tile_segs == tile_segs[:, -1:])[:, None, None, :]
    masked_signal = jnp.where(end_keep, signal, jnp.zeros_like(signal))
    states = jnp.einsum(
        "gsm,jgis->jgim", inward_upper, masked_signal, preferred_element_type=jnp.float32
    ) + jnp.einsum(
        "gsm,jgis->jgim", inward_lower, masked_signal, preferred_element_type=jnp.float32
    )
    carried = (tile_segs[:, -1] == before).astype(jnp.float32)

    def chain_link(carry_in, inputs):
        block_states, kept_flag = inputs
        step = (
            decay_re * kept_flag,
            decay_im * kept_flag,
            block_states[..., :mode_count],
            block_states[..., mode_count:],
        )
        return (complex_link(carry_in, step), carry_in)

    state_zero = jnp.zeros((group_count, GROUP, mode_count), jnp.float32)
    start_carry = (
        jnp.ones((group_count, mode_count), jnp.float32),
        jnp.zeros((group_count, mode_count), jnp.float32),
        state_zero,
        state_zero,
    )
    summary, entering = lax.scan(chain_link, start_carry, (states, carried))
    incoming = entering_2(
        (summary[0], summary[1], summary[2], summary[3]),
        "seq",
        complex_link,
        (start_carry[0], start_carry[1], start_carry[2], start_carry[3]),
    )
    incoming_re = incoming[2]
    incoming_im = incoming[3]
    reach_re = entering[0][:, :, None, :]
    reach_im = entering[1][:, :, None, :]
    full_re = entering[2] + reach_re * incoming_re - reach_im * incoming_im
    full_im = entering[3] + reach_re * incoming_im + reach_im * incoming_re
    keep_mask = (tile_segs == before[:, None]).astype(jnp.float32)
    carried_part = (
        jnp.einsum(
            "gtm,jgim->jgit",
            outward,
            jnp.concatenate((full_re, full_im), axis=3),
            precision=highest,
        )
        * keep_mask[:, None, None, :]
    )
    longconv = (
        local_part
        + carried_part
        + skip_gain.reshape(group_count, GROUP)[None, :, :, None] * signal.astype(jnp.float32)
    )
    long_cols = jnp.transpose(longconv, (1, 2, 0, 3)).reshape(chan_count, row_count)
    mixed = (query_proj.T.astype(jnp.float32) * long_cols).astype(jnp.bfloat16)
    mixed_wide = mixed.astype(jnp.float32)
    squares = lax.psum(jnp.sum(mixed_wide * mixed_wide, axis=0), ("chan", "rep"))
    normed = (mixed_wide * lax.rsqrt(squares / D + norm_eps)[None, :] * norm_gain[:, None]).astype(
        jnp.bfloat16
    )
    partial_value = channel_logits(normed, unembed)
    lanes = ("chan", "rep")
    lane_count = lax.axis_size(lanes)
    piece = row_count // lane_count
    piece_at = lax.axis_index(lanes) * piece
    logits = lax.psum_scatter(partial_value, lanes, scatter_dimension=0, tiled=True)
    logprob_piece = log_probs(logits, lax.dynamic_slice_in_dim(token_ids, piece_at, piece, 0))
    logprob = lax.all_gather(logprob_piece, lanes, tiled=True)
    genome_index = jnp.arange(genome_lengths.shape[0], dtype=jnp.int32)
    genome_part = jnp.sum(
        jnp.where(
            segments[:, None] == genome_index[None, :],
            logprob[:, None],
            jnp.zeros((row_count, genome_lengths.shape[0]), jnp.float32),
        ),
        axis=0,
    )
    totals = lax.psum(genome_part, "seq")
    return (logprob, totals / genome_lengths.astype(jnp.float32))


def solution(mesh):
    return jax.shard_map(
        per_device,
        mesh=mesh,
        in_specs=(
            P(("groups", "seq"), ("chan", "rep")),
            P(("groups", "seq"), ("chan", "rep")),
            P(("groups", "seq"), ("chan", "rep")),
            P(None, ("chan", "rep")),
            P(None, ("chan", "rep")),
            P(None, ("chan", "rep"), None),
            P(("chan", "rep")),
            P(("chan", "rep")),
            P(("chan", "rep"), None),
            P(("groups", "seq")),
            P("groups"),
        ),
        out_specs=(P(("groups", "seq")), P("groups")),
        check_vma=False,
    )
```

```python
import jax
import jax.numpy as jnp
from jax import lax
from jax.sharding import PartitionSpec as P

D = 8192
GROUP = 16


tile_rows = 128
short_margin = 8
norm_eps = 1e-05


def from_behind(shard, axis, by):
    count = lax.axis_size(axis)
    pairs = [(i, i + by) for i in range(count) if 0 <= i + by < count]
    return lax.ppermute(shard, axis, pairs)


def entering_2(part, axis, combine, identity):
    place = lax.axis_index(axis)
    count = lax.axis_size(axis)
    lead = part[0].shape[0]
    widths = [a.size // lead for a in part]

    def pack(t):
        return jnp.concatenate([a.reshape(lead, -1) for a in t], axis=1)

    def unpack(flat):
        pieces = []
        offset = 0
        for a, width in zip(part, widths):
            pieces.append(flat[:, offset : offset + width].reshape(a.shape))
            offset += width
        return tuple(pieces)

    ident = tuple(jnp.zeros_like(a) + jnp.asarray(e, a.dtype) for a, e in zip(part, identity))
    before = ident
    upto = tuple(part)
    shift = 1
    while shift < count:
        arrived = unpack(from_behind(pack(upto), axis, shift))
        arrived = tuple(jnp.where(place >= shift, r, i) for r, i in zip(arrived, ident))
        before = combine(arrived, before)
        upto = combine(arrived, upto)
        shift *= 2
    return before


def segment_ids(positions, genome_lengths):
    starts = jnp.cumsum(genome_lengths) - genome_lengths
    at_or_past = (positions[:, None] >= starts[None, :]).astype(jnp.int32)
    return jnp.sum(at_or_past, axis=1) - 1


def short_filter(keys_in, values_in, seg_list, out_rows, short_taps):
    gated = keys_in.astype(jnp.float32) * values_in.astype(jnp.float32)
    total_rows = keys_in.shape[0]
    lead_rows = total_rows - out_rows
    own_segs = seg_list[lead_rows:]
    result = jnp.zeros((out_rows, keys_in.shape[1]), jnp.float32)
    for lag_index in range(short_taps.shape[0]):
        shifted = gated[lead_rows - lag_index : total_rows - lag_index]
        same_genome = (seg_list[lead_rows - lag_index : total_rows - lag_index] == own_segs).astype(
            jnp.float32
        )
        result = (
            result
            + short_taps[lag_index].astype(jnp.float32)[None, :] * shifted * same_genome[:, None]
        )
    return result.astype(jnp.bfloat16)


def lag_select(table, rows, cols, shift):
    lag_count = table.shape[0]
    lag_ids = lax.optimization_barrier(jnp.arange(lag_count, dtype=jnp.int32))
    out_pos = jnp.arange(rows, dtype=jnp.int32)[:, None]
    in_pos = jnp.arange(cols, dtype=jnp.int32)[None, :]
    lag_grid = out_pos + shift - in_pos
    one_hot = (lag_grid[None] == lag_ids[:, None, None]).astype(table.dtype)
    picked = lax.dot_general(
        table, one_hot, (((0,), (0,)), ((), ())), preferred_element_type=jnp.float32
    )
    return picked.astype(table.dtype)


def medium_toeplitz(medium_taps):
    return lag_select(medium_taps, tile_rows, 2 * tile_rows, tile_rows)


def modal_tables(modal_poles):
    decay_rate = modal_poles[0]
    angles = modal_poles[1]
    residue_re = modal_poles[2]
    residue_im = modal_poles[3]
    powers = jnp.arange(tile_rows + 1).astype(jnp.float32)[:, None, None]
    magnitude = jnp.exp(-powers * decay_rate[None])
    power_re = magnitude * jnp.cos(powers * angles[None])
    power_im = magnitude * jnp.sin(powers * angles[None])
    kernel_re = residue_re[None] * power_re - residue_im[None] * power_im
    kernel_im = residue_re[None] * power_im + residue_im[None] * power_re
    kernel = jnp.sum(kernel_re[:tile_rows], axis=2)
    upper, lower = split_table(kernel)
    group_count = kernel.shape[1]
    both = lag_select(jnp.concatenate((upper, lower), axis=1), tile_rows, tile_rows, 0)
    toeplitz = (both[:group_count], both[group_count:])
    outward = jnp.transpose(jnp.concatenate((kernel_re[1:], -kernel_im[1:]), axis=2), (1, 0, 2))
    inward = jnp.transpose(
        jnp.concatenate((power_re[tile_rows - 1 :: -1], power_im[tile_rows - 1 :: -1]), axis=2),
        (1, 0, 2),
    )
    return (toeplitz, outward, inward, power_re[tile_rows], power_im[tile_rows])


def split_table(table):
    upper = table.astype(jnp.bfloat16)
    lower = (table - upper.astype(jnp.float32)).astype(jnp.bfloat16)
    return (upper, lower)


def complex_link(earlier, later):
    early_are, early_aim, early_sre, early_sim = earlier
    late_are, late_aim, late_sre, late_sim = later
    lead_re = late_are[..., None, :]
    lead_im = late_aim[..., None, :]
    return (
        late_are * early_are - late_aim * early_aim,
        late_are * early_aim + late_aim * early_are,
        lead_re * early_sre - lead_im * early_sim + late_sre,
        lead_re * early_sim + lead_im * early_sre + late_sim,
    )


def log_probs(logits, targets):
    vocab_ids = jnp.arange(logits.shape[1], dtype=jnp.int32)
    picked = jnp.sum(
        jnp.where(targets[:, None] == vocab_ids[None, :], logits, jnp.zeros_like(logits)), axis=1
    )
    return picked - jnp.log(jnp.sum(jnp.exp(logits), axis=1))


def channel_logits(normed_cols, unembed):
    return lax.dot_general(
        normed_cols, unembed, (((0,), (0,)), ((), ())), preferred_element_type=jnp.float32
    )


def per_device(
    query_proj,
    key_proj,
    value_proj,
    short_taps,
    medium_taps,
    modal_poles,
    skip_gain,
    norm_gain,
    unembed,
    token_ids,
    genome_lengths,
):
    highest = lax.Precision.HIGHEST
    row_count, chan_count = query_proj.shape
    group_count = chan_count // GROUP
    mode_count = modal_poles.shape[2]
    tile_count = row_count // tile_rows
    first_row = lax.axis_index("seq") * row_count
    segments = segment_ids(first_row + jnp.arange(row_count, dtype=jnp.int32), genome_lengths)
    halo = tile_rows + short_margin
    edge_pair = from_behind(
        jnp.stack((key_proj[row_count - halo :], value_proj[row_count - halo :])),
        "seq",
        1,
    )
    ext_segs = segment_ids(
        first_row - halo + jnp.arange(row_count + halo, dtype=jnp.int32),
        genome_lengths,
    )
    filtered = short_filter(
        jnp.concatenate((edge_pair[0], key_proj)),
        jnp.concatenate((edge_pair[1], value_proj)),
        ext_segs,
        row_count + tile_rows,
        short_taps,
    )
    ext_short = filtered.T.reshape(group_count, GROUP, row_count + tile_rows)
    medium_segs = segment_ids(
        first_row - tile_rows + jnp.arange(row_count + tile_rows, dtype=jnp.int32), genome_lengths
    )
    toeplitz = medium_toeplitz(medium_taps)

    def medium_block(tile_index):
        start = tile_index * tile_rows
        window = lax.dynamic_slice_in_dim(ext_short, start, 2 * tile_rows, 2)
        window_segs = lax.dynamic_slice_in_dim(medium_segs, start, 2 * tile_rows, 0)
        own_segs = lax.dynamic_slice_in_dim(segments, start, tile_rows, 0)
        same_genome = own_segs[:, None] == window_segs[None, :]
        matrix = jnp.where(same_genome[None], toeplitz, jnp.zeros_like(toeplitz))
        return jnp.einsum(
            "gts,gis->git", matrix, window, preferred_element_type=jnp.float32
        ).astype(jnp.bfloat16)

    signal = lax.map(medium_block, jnp.arange(tile_count, dtype=jnp.int32))
    long_toeplitz, outward, inward, decay_re, decay_im = modal_tables(modal_poles)
    toeplitz_upper, toeplitz_lower = long_toeplitz
    inward_upper, inward_lower = split_table(inward)
    tile_segs = segments.reshape(tile_count, tile_rows)
    before = segment_ids(
        first_row + jnp.arange(tile_count, dtype=jnp.int32) * tile_rows - 1, genome_lengths
    )

    def intra_block(inputs):
        block_in, own_segs = inputs
        same_genome = (own_segs[:, None] == own_segs[None, :])[None]
        upper = jnp.where(same_genome, toeplitz_upper, jnp.zeros_like(toeplitz_upper))
        lower = jnp.where(same_genome, toeplitz_lower, jnp.zeros_like(toeplitz_lower))
        return jnp.einsum(
            "gts,gis->git", upper, block_in, preferred_element_type=jnp.float32
        ) + jnp.einsum("gts,gis->git", lower, block_in, preferred_element_type=jnp.float32)

    local_part = lax.map(intra_block, (signal, tile_segs))
    end_keep = (tile_segs == tile_segs[:, -1:])[:, None, None, :]
    masked_signal = jnp.where(end_keep, signal, jnp.zeros_like(signal))
    states = jnp.einsum(
        "gsm,jgis->jgim", inward_upper, masked_signal, preferred_element_type=jnp.float32
    ) + jnp.einsum(
        "gsm,jgis->jgim", inward_lower, masked_signal, preferred_element_type=jnp.float32
    )
    carried = (tile_segs[:, -1] == before).astype(jnp.float32)

    def chain_link(carry_in, inputs):
        block_states, kept_flag = inputs
        step = (
            decay_re * kept_flag,
            decay_im * kept_flag,
            block_states[..., :mode_count],
            block_states[..., mode_count:],
        )
        return (complex_link(carry_in, step), carry_in)

    state_zero = jnp.zeros((group_count, GROUP, mode_count), jnp.float32)
    start_carry = (
        jnp.ones((group_count, mode_count), jnp.float32),
        jnp.zeros((group_count, mode_count), jnp.float32),
        state_zero,
        state_zero,
    )
    summary, entering = lax.scan(chain_link, start_carry, (states, carried))
    incoming = entering_2(
        (summary[0], summary[1], summary[2], summary[3]),
        "seq",
        complex_link,
        (start_carry[0], start_carry[1], start_carry[2], start_carry[3]),
    )
    incoming_re = incoming[2]
    incoming_im = incoming[3]
    reach_re = entering[0][:, :, None, :]
    reach_im = entering[1][:, :, None, :]
    full_re = entering[2] + reach_re * incoming_re - reach_im * incoming_im
    full_im = entering[3] + reach_re * incoming_im + reach_im * incoming_re
    keep_mask = (tile_segs == before[:, None]).astype(jnp.float32)
    carried_part = (
        jnp.einsum(
            "gtm,jgim->jgit",
            outward,
            jnp.concatenate((full_re, full_im), axis=3),
            precision=highest,
        )
        * keep_mask[:, None, None, :]
    )
    longconv = (
        local_part
        + carried_part
        + skip_gain.reshape(group_count, GROUP)[None, :, :, None] * signal.astype(jnp.float32)
    )
    long_cols = jnp.transpose(longconv, (1, 2, 0, 3)).reshape(chan_count, row_count)
    mixed = (query_proj.T.astype(jnp.float32) * long_cols).astype(jnp.bfloat16)
    mixed_wide = mixed.astype(jnp.float32)
    squares = lax.psum(jnp.sum(mixed_wide * mixed_wide, axis=0), ("chan", "rep"))
    normed = (mixed_wide * lax.rsqrt(squares / D + norm_eps)[None, :] * norm_gain[:, None]).astype(
        jnp.bfloat16
    )
    partial_value = channel_logits(normed, unembed)
    lanes = ("chan", "rep")
    lane_count = lax.axis_size(lanes)
    piece = row_count // lane_count
    piece_at = lax.axis_index(lanes) * piece
    logits = lax.psum_scatter(partial_value, lanes, scatter_dimension=0, tiled=True)
    logprob_piece = log_probs(logits, lax.dynamic_slice_in_dim(token_ids, piece_at, piece, 0))
    logprob = lax.all_gather(logprob_piece, lanes, tiled=True)
    genome_index = jnp.arange(genome_lengths.shape[0], dtype=jnp.int32)
    genome_part = jnp.sum(
        jnp.where(
            segments[:, None] == genome_index[None, :],
            logprob[:, None],
            jnp.zeros((row_count, genome_lengths.shape[0]), jnp.float32),
        ),
        axis=0,
    )
    totals = lax.psum(genome_part, "seq")
    return (logprob, totals / genome_lengths.astype(jnp.float32))


def solution(mesh):
    return jax.shard_map(
        per_device,
        mesh=mesh,
        in_specs=(
            P(("groups", "seq"), ("chan", "rep")),
            P(("groups", "seq"), ("chan", "rep")),
            P(("groups", "seq"), ("chan", "rep")),
            P(None, ("chan", "rep")),
            P(None, ("chan", "rep")),
            P(None, ("chan", "rep"), None),
            P(("chan", "rep")),
            P(("chan", "rep")),
            P(("chan", "rep"), None),
            P(("groups", "seq")),
            P("groups"),
        ),
        out_specs=(P(("groups", "seq")), P("groups")),
        check_vma=False,
    )
```

```python
import jax
import jax.numpy as jnp
from jax import lax
from jax.sharding import PartitionSpec as P

D = 8192
GROUP = 16


tile_rows = 128
short_margin = 8
norm_eps = 1e-05


def from_behind(shard, axis, by):
    count = lax.axis_size(axis)
    pairs = [(i, i + by) for i in range(count) if 0 <= i + by < count]
    return lax.ppermute(shard, axis, pairs)


def entering_2(part, axis, combine, identity):
    place = lax.axis_index(axis)
    count = lax.axis_size(axis)
    lead = part[0].shape[0]
    widths = [a.size // lead for a in part]

    def pack(t):
        return jnp.concatenate([a.reshape(lead, -1) for a in t], axis=1)

    def unpack(flat):
        pieces = []
        offset = 0
        for a, width in zip(part, widths):
            pieces.append(flat[:, offset : offset + width].reshape(a.shape))
            offset += width
        return tuple(pieces)

    ident = tuple(jnp.zeros_like(a) + jnp.asarray(e, a.dtype) for a, e in zip(part, identity))
    before = ident
    upto = tuple(part)
    shift = 1
    while shift < count:
        arrived = unpack(from_behind(pack(upto), axis, shift))
        arrived = tuple(jnp.where(place >= shift, r, i) for r, i in zip(arrived, ident))
        before = combine(arrived, before)
        upto = combine(arrived, upto)
        shift *= 2
    return before


def segment_ids(positions, genome_lengths):
    starts = jnp.cumsum(genome_lengths) - genome_lengths
    at_or_past = (positions[:, None] >= starts[None, :]).astype(jnp.int32)
    return jnp.sum(at_or_past, axis=1) - 1


def short_filter(keys_in, values_in, seg_list, out_rows, short_taps):
    gated = keys_in.astype(jnp.float32) * values_in.astype(jnp.float32)
    total_rows = keys_in.shape[0]
    lead_rows = total_rows - out_rows
    own_segs = seg_list[lead_rows:]
    result = jnp.zeros((out_rows, keys_in.shape[1]), jnp.float32)
    for lag_index in range(short_taps.shape[0]):
        shifted = gated[lead_rows - lag_index : total_rows - lag_index]
        same_genome = (seg_list[lead_rows - lag_index : total_rows - lag_index] == own_segs).astype(
            jnp.float32
        )
        result = (
            result
            + short_taps[lag_index].astype(jnp.float32)[None, :] * shifted * same_genome[:, None]
        )
    return result.astype(jnp.bfloat16)


def lag_select(table, rows, cols, shift):
    lag_count = table.shape[0]
    lag_ids = lax.optimization_barrier(jnp.arange(lag_count, dtype=jnp.int32))
    out_pos = jnp.arange(rows, dtype=jnp.int32)[:, None]
    in_pos = jnp.arange(cols, dtype=jnp.int32)[None, :]
    lag_grid = out_pos + shift - in_pos
    one_hot = (lag_grid.reshape(1, rows * cols) == lag_ids[:, None]).astype(table.dtype)
    width = table.shape[1]
    lead = jnp.concatenate((table.T, jnp.zeros((max(256 - width, 0), lag_count), table.dtype)))
    picked = jnp.dot(lead, one_hot, preferred_element_type=jnp.float32)[:width]
    return picked.astype(table.dtype).reshape(width, rows, cols)


def medium_toeplitz(medium_taps):
    return lag_select(medium_taps, tile_rows, 2 * tile_rows, tile_rows)


def modal_tables(modal_poles):
    decay_rate = modal_poles[0]
    angles = modal_poles[1]
    residue_re = modal_poles[2]
    residue_im = modal_poles[3]
    powers = jnp.arange(tile_rows + 1).astype(jnp.float32)[:, None, None]
    magnitude = jnp.exp(-powers * decay_rate[None])
    power_re = magnitude * jnp.cos(powers * angles[None])
    power_im = magnitude * jnp.sin(powers * angles[None])
    kernel_re = residue_re[None] * power_re - residue_im[None] * power_im
    kernel_im = residue_re[None] * power_im + residue_im[None] * power_re
    kernel = jnp.sum(kernel_re[:tile_rows], axis=2)
    upper, lower = split_table(kernel)
    group_count = kernel.shape[1]
    both = lag_select(jnp.concatenate((upper, lower), axis=1), tile_rows, tile_rows, 0)
    toeplitz = (both[:group_count], both[group_count:])
    outward = jnp.transpose(jnp.concatenate((kernel_re[1:], -kernel_im[1:]), axis=2), (1, 0, 2))
    inward = jnp.transpose(
        jnp.concatenate((power_re[tile_rows - 1 :: -1], power_im[tile_rows - 1 :: -1]), axis=2),
        (1, 0, 2),
    )
    return (toeplitz, outward, inward, power_re[tile_rows], power_im[tile_rows])


def split_table(table):
    upper = table.astype(jnp.bfloat16)
    lower = (table - upper.astype(jnp.float32)).astype(jnp.bfloat16)
    return (upper, lower)


def complex_link(earlier, later):
    early_are, early_aim, early_sre, early_sim = earlier
    late_are, late_aim, late_sre, late_sim = later
    lead_re = late_are[..., None, :]
    lead_im = late_aim[..., None, :]
    return (
        late_are * early_are - late_aim * early_aim,
        late_are * early_aim + late_aim * early_are,
        lead_re * early_sre - lead_im * early_sim + late_sre,
        lead_re * early_sim + lead_im * early_sre + late_sim,
    )


def log_probs(logits, targets):
    vocab_ids = jnp.arange(logits.shape[1], dtype=jnp.int32)
    picked = jnp.sum(
        jnp.where(targets[:, None] == vocab_ids[None, :], logits, jnp.zeros_like(logits)), axis=1
    )
    return picked - jnp.log(jnp.sum(jnp.exp(logits), axis=1))


def channel_logits(normed_cols, unembed):
    return lax.dot_general(
        normed_cols, unembed, (((0,), (0,)), ((), ())), preferred_element_type=jnp.float32
    )


def per_device(
    query_proj,
    key_proj,
    value_proj,
    short_taps,
    medium_taps,
    modal_poles,
    skip_gain,
    norm_gain,
    unembed,
    token_ids,
    genome_lengths,
):
    highest = lax.Precision.HIGHEST
    row_count, chan_count = query_proj.shape
    group_count = chan_count // GROUP
    mode_count = modal_poles.shape[2]
    tile_count = row_count // tile_rows
    first_row = lax.axis_index("seq") * row_count
    segments = segment_ids(first_row + jnp.arange(row_count, dtype=jnp.int32), genome_lengths)
    halo = tile_rows + short_margin
    edge_pair = from_behind(
        jnp.stack((key_proj[row_count - halo :], value_proj[row_count - halo :])),
        "seq",
        1,
    )
    ext_segs = segment_ids(
        first_row - halo + jnp.arange(row_count + halo, dtype=jnp.int32),
        genome_lengths,
    )
    filtered = short_filter(
        jnp.concatenate((edge_pair[0], key_proj)),
        jnp.concatenate((edge_pair[1], value_proj)),
        ext_segs,
        row_count + tile_rows,
        short_taps,
    )
    ext_short = filtered.T.reshape(group_count, GROUP, row_count + tile_rows)
    medium_segs = segment_ids(
        first_row - tile_rows + jnp.arange(row_count + tile_rows, dtype=jnp.int32), genome_lengths
    )
    toeplitz = medium_toeplitz(medium_taps)

    def medium_block(tile_index):
        start = tile_index * tile_rows
        window = lax.dynamic_slice_in_dim(ext_short, start, 2 * tile_rows, 2)
        window_segs = lax.dynamic_slice_in_dim(medium_segs, start, 2 * tile_rows, 0)
        own_segs = lax.dynamic_slice_in_dim(segments, start, tile_rows, 0)
        same_genome = own_segs[:, None] == window_segs[None, :]
        matrix = jnp.where(same_genome[None], toeplitz, jnp.zeros_like(toeplitz))
        return jnp.einsum(
            "gts,gis->git", matrix, window, preferred_element_type=jnp.float32
        ).astype(jnp.bfloat16)

    signal = lax.map(medium_block, jnp.arange(tile_count, dtype=jnp.int32))
    long_toeplitz, outward, inward, decay_re, decay_im = modal_tables(modal_poles)
    toeplitz_upper, toeplitz_lower = long_toeplitz
    inward_upper, inward_lower = split_table(inward)
    tile_segs = segments.reshape(tile_count, tile_rows)
    before = segment_ids(
        first_row + jnp.arange(tile_count, dtype=jnp.int32) * tile_rows - 1, genome_lengths
    )

    def intra_block(inputs):
        block_in, own_segs = inputs
        same_genome = (own_segs[:, None] == own_segs[None, :])[None]
        upper = jnp.where(same_genome, toeplitz_upper, jnp.zeros_like(toeplitz_upper))
        lower = jnp.where(same_genome, toeplitz_lower, jnp.zeros_like(toeplitz_lower))
        return jnp.einsum(
            "gts,gis->git", upper, block_in, preferred_element_type=jnp.float32
        ) + jnp.einsum("gts,gis->git", lower, block_in, preferred_element_type=jnp.float32)

    local_part = lax.map(intra_block, (signal, tile_segs))
    end_keep = (tile_segs == tile_segs[:, -1:])[:, None, None, :]
    masked_signal = jnp.where(end_keep, signal, jnp.zeros_like(signal))
    states = jnp.einsum(
        "gsm,jgis->jgim", inward_upper, masked_signal, preferred_element_type=jnp.float32
    ) + jnp.einsum(
        "gsm,jgis->jgim", inward_lower, masked_signal, preferred_element_type=jnp.float32
    )
    carried = (tile_segs[:, -1] == before).astype(jnp.float32)

    def chain_link(carry_in, inputs):
        block_states, kept_flag = inputs
        step = (
            decay_re * kept_flag,
            decay_im * kept_flag,
            block_states[..., :mode_count],
            block_states[..., mode_count:],
        )
        return (complex_link(carry_in, step), carry_in)

    state_zero = jnp.zeros((group_count, GROUP, mode_count), jnp.float32)
    start_carry = (
        jnp.ones((group_count, mode_count), jnp.float32),
        jnp.zeros((group_count, mode_count), jnp.float32),
        state_zero,
        state_zero,
    )
    summary, entering = lax.scan(chain_link, start_carry, (states, carried))
    incoming = entering_2(
        (summary[0], summary[1], summary[2], summary[3]),
        "seq",
        complex_link,
        (start_carry[0], start_carry[1], start_carry[2], start_carry[3]),
    )
    incoming_re = incoming[2]
    incoming_im = incoming[3]
    reach_re = entering[0][:, :, None, :]
    reach_im = entering[1][:, :, None, :]
    full_re = entering[2] + reach_re * incoming_re - reach_im * incoming_im
    full_im = entering[3] + reach_re * incoming_im + reach_im * incoming_re
    keep_mask = (tile_segs == before[:, None]).astype(jnp.float32)
    carried_part = (
        jnp.einsum(
            "gtm,jgim->jgit",
            outward,
            jnp.concatenate((full_re, full_im), axis=3),
            precision=highest,
        )
        * keep_mask[:, None, None, :]
    )
    longconv = (
        local_part
        + carried_part
        + skip_gain.reshape(group_count, GROUP)[None, :, :, None] * signal.astype(jnp.float32)
    )
    long_cols = jnp.transpose(longconv, (1, 2, 0, 3)).reshape(chan_count, row_count)
    mixed = (query_proj.T.astype(jnp.float32) * long_cols).astype(jnp.bfloat16)
    mixed_wide = mixed.astype(jnp.float32)
    squares = lax.psum(jnp.sum(mixed_wide * mixed_wide, axis=0), ("chan", "rep"))
    normed = (mixed_wide * lax.rsqrt(squares / D + norm_eps)[None, :] * norm_gain[:, None]).astype(
        jnp.bfloat16
    )
    partial_value = channel_logits(normed, unembed)
    lanes = ("chan", "rep")
    lane_count = lax.axis_size(lanes)
    piece = row_count // lane_count
    piece_at = lax.axis_index(lanes) * piece
    logits = lax.psum_scatter(partial_value, lanes, scatter_dimension=0, tiled=True)
    logprob_piece = log_probs(logits, lax.dynamic_slice_in_dim(token_ids, piece_at, piece, 0))
    logprob = lax.all_gather(logprob_piece, lanes, tiled=True)
    genome_index = jnp.arange(genome_lengths.shape[0], dtype=jnp.int32)
    genome_part = jnp.sum(
        jnp.where(
            segments[:, None] == genome_index[None, :],
            logprob[:, None],
            jnp.zeros((row_count, genome_lengths.shape[0]), jnp.float32),
        ),
        axis=0,
    )
    totals = lax.psum(genome_part, "seq")
    return (logprob, totals / genome_lengths.astype(jnp.float32))


def solution(mesh):
    return jax.shard_map(
        per_device,
        mesh=mesh,
        in_specs=(
            P(("groups", "seq"), ("chan", "rep")),
            P(("groups", "seq"), ("chan", "rep")),
            P(("groups", "seq"), ("chan", "rep")),
            P(None, ("chan", "rep")),
            P(None, ("chan", "rep")),
            P(None, ("chan", "rep"), None),
            P(("chan", "rep")),
            P(("chan", "rep")),
            P(("chan", "rep"), None),
            P(("groups", "seq")),
            P("groups"),
        ),
        out_specs=(P(("groups", "seq")), P("groups")),
        check_vma=False,
    )
```

```python
import jax
import jax.numpy as jnp
from jax import lax
from jax.sharding import PartitionSpec as P

D = 8192
GROUP = 16


tile_rows = 128
short_margin = 8
norm_eps = 1e-05


def from_behind(shard, axis, by):
    count = lax.axis_size(axis)
    pairs = [(i, i + by) for i in range(count) if 0 <= i + by < count]
    return lax.ppermute(shard, axis, pairs)


def entering_2(part, axis, combine, identity):
    place = lax.axis_index(axis)
    count = lax.axis_size(axis)
    lead = part[0].shape[0]
    widths = [a.size // lead for a in part]

    def pack(t):
        return jnp.concatenate([a.reshape(lead, -1) for a in t], axis=1)

    def unpack(flat):
        pieces = []
        offset = 0
        for a, width in zip(part, widths):
            pieces.append(flat[:, offset : offset + width].reshape(a.shape))
            offset += width
        return tuple(pieces)

    ident = tuple(jnp.zeros_like(a) + jnp.asarray(e, a.dtype) for a, e in zip(part, identity))
    before = ident
    upto = tuple(part)
    shift = 1
    while shift < count:
        arrived = unpack(from_behind(pack(upto), axis, shift))
        arrived = tuple(jnp.where(place >= shift, r, i) for r, i in zip(arrived, ident))
        before = combine(arrived, before)
        upto = combine(arrived, upto)
        shift *= 2
    return before


def segment_ids(positions, genome_lengths):
    starts = jnp.cumsum(genome_lengths) - genome_lengths
    at_or_past = (positions[:, None] >= starts[None, :]).astype(jnp.int32)
    return jnp.sum(at_or_past, axis=1) - 1


def short_filter(keys_in, values_in, seg_list, out_rows, short_taps):
    gated = keys_in.astype(jnp.float32) * values_in.astype(jnp.float32)
    total_rows = keys_in.shape[0]
    lead_rows = total_rows - out_rows
    own_segs = seg_list[lead_rows:]
    result = jnp.zeros((out_rows, keys_in.shape[1]), jnp.float32)
    for lag_index in range(short_taps.shape[0]):
        shifted = gated[lead_rows - lag_index : total_rows - lag_index]
        same_genome = (seg_list[lead_rows - lag_index : total_rows - lag_index] == own_segs).astype(
            jnp.float32
        )
        result = (
            result
            + short_taps[lag_index].astype(jnp.float32)[None, :] * shifted * same_genome[:, None]
        )
    return result.astype(jnp.bfloat16)


def circulants(table):
    lag_count, width = table.shape
    lag_ids = lax.optimization_barrier(jnp.arange(lag_count, dtype=jnp.int32))
    out_pos = jnp.arange(tile_rows, dtype=jnp.int32)[:, None]
    in_pos = jnp.arange(tile_rows, dtype=jnp.int32)[None, :]
    lag_grid = (out_pos - in_pos + tile_rows) % tile_rows
    one_hot = (lag_grid.reshape(1, tile_rows * tile_rows) == lag_ids[:, None]).astype(table.dtype)
    picked = jnp.dot(table.T, one_hot, preferred_element_type=jnp.float32)
    return picked.astype(table.dtype).reshape(width, tile_rows, tile_rows)


def modal_tables(modal_poles):
    decay_rate = modal_poles[0]
    angles = modal_poles[1]
    residue_re = modal_poles[2]
    residue_im = modal_poles[3]
    powers = jnp.arange(tile_rows + 1).astype(jnp.float32)[:, None, None]
    magnitude = jnp.exp(-powers * decay_rate[None])
    power_re = magnitude * jnp.cos(powers * angles[None])
    power_im = magnitude * jnp.sin(powers * angles[None])
    kernel_re = residue_re[None] * power_re - residue_im[None] * power_im
    kernel_im = residue_re[None] * power_im + residue_im[None] * power_re
    kernel = jnp.sum(kernel_re[:tile_rows], axis=2)
    toeplitz = split_table(kernel)
    outward = jnp.transpose(jnp.concatenate((kernel_re[1:], -kernel_im[1:]), axis=2), (1, 0, 2))
    inward = jnp.transpose(
        jnp.concatenate((power_re[tile_rows - 1 :: -1], power_im[tile_rows - 1 :: -1]), axis=2),
        (1, 0, 2),
    )
    return (toeplitz, outward, inward, power_re[tile_rows], power_im[tile_rows])


def split_table(table):
    upper = table.astype(jnp.bfloat16)
    lower = (table - upper.astype(jnp.float32)).astype(jnp.bfloat16)
    return (upper, lower)


def complex_link(earlier, later):
    early_are, early_aim, early_sre, early_sim = earlier
    late_are, late_aim, late_sre, late_sim = later
    lead_re = late_are[..., None, :]
    lead_im = late_aim[..., None, :]
    return (
        late_are * early_are - late_aim * early_aim,
        late_are * early_aim + late_aim * early_are,
        lead_re * early_sre - lead_im * early_sim + late_sre,
        lead_re * early_sim + lead_im * early_sre + late_sim,
    )


def log_probs(logits, targets):
    vocab_ids = jnp.arange(logits.shape[1], dtype=jnp.int32)
    picked = jnp.sum(
        jnp.where(targets[:, None] == vocab_ids[None, :], logits, jnp.zeros_like(logits)), axis=1
    )
    return picked - jnp.log(jnp.sum(jnp.exp(logits), axis=1))


def channel_logits(normed_cols, unembed):
    return lax.dot_general(
        normed_cols, unembed, (((0,), (0,)), ((), ())), preferred_element_type=jnp.float32
    )


def per_device(
    query_proj,
    key_proj,
    value_proj,
    short_taps,
    medium_taps,
    modal_poles,
    skip_gain,
    norm_gain,
    unembed,
    token_ids,
    genome_lengths,
):
    highest = lax.Precision.HIGHEST
    row_count, chan_count = query_proj.shape
    group_count = chan_count // GROUP
    mode_count = modal_poles.shape[2]
    tile_count = row_count // tile_rows
    first_row = lax.axis_index("seq") * row_count
    segments = segment_ids(first_row + jnp.arange(row_count, dtype=jnp.int32), genome_lengths)
    halo = tile_rows + short_margin
    edge_pair = from_behind(
        jnp.stack((key_proj[row_count - halo :], value_proj[row_count - halo :])),
        "seq",
        1,
    )
    ext_segs = segment_ids(
        first_row - halo + jnp.arange(row_count + halo, dtype=jnp.int32),
        genome_lengths,
    )
    filtered = short_filter(
        jnp.concatenate((edge_pair[0], key_proj)),
        jnp.concatenate((edge_pair[1], value_proj)),
        ext_segs,
        row_count + tile_rows,
        short_taps,
    )
    ext_short = filtered.T.reshape(group_count, GROUP, row_count + tile_rows)
    medium_segs = segment_ids(
        first_row - tile_rows + jnp.arange(row_count + tile_rows, dtype=jnp.int32), genome_lengths
    )

    long_toeplitz, outward, inward, decay_re, decay_im = modal_tables(modal_poles)
    circ = circulants(jnp.concatenate((medium_taps, long_toeplitz[0], long_toeplitz[1]), axis=1))
    circ_medium = jnp.concatenate((circ[:group_count], circ[:group_count]), axis=2)
    toeplitz_upper = circ[group_count : 2 * group_count]
    toeplitz_lower = circ[2 * group_count :]
    lag_band = (
        jnp.arange(tile_rows, dtype=jnp.int32)[:, None] + tile_rows
        - jnp.arange(2 * tile_rows, dtype=jnp.int32)[None, :]
    )
    medium_band = (lag_band >= 0) & (lag_band < medium_taps.shape[0])
    long_band = lag_band[:, tile_rows:] >= 0

    def medium_block(tile_index):
        start = tile_index * tile_rows
        window = lax.dynamic_slice_in_dim(ext_short, start, 2 * tile_rows, 2)
        window_segs = lax.dynamic_slice_in_dim(medium_segs, start, 2 * tile_rows, 0)
        own_segs = lax.dynamic_slice_in_dim(segments, start, tile_rows, 0)
        same_genome = (own_segs[:, None] == window_segs[None, :]) & medium_band
        matrix = jnp.where(same_genome[None], circ_medium, jnp.zeros_like(circ_medium))
        return jnp.einsum(
            "gts,gis->git", matrix, window, preferred_element_type=jnp.float32
        ).astype(jnp.bfloat16)

    signal = lax.map(medium_block, jnp.arange(tile_count, dtype=jnp.int32))
    inward_upper, inward_lower = split_table(inward)
    tile_segs = segments.reshape(tile_count, tile_rows)
    before = segment_ids(
        first_row + jnp.arange(tile_count, dtype=jnp.int32) * tile_rows - 1, genome_lengths
    )

    def intra_block(inputs):
        block_in, own_segs = inputs
        same_genome = ((own_segs[:, None] == own_segs[None, :]) & long_band)[None]
        upper = jnp.where(same_genome, toeplitz_upper, jnp.zeros_like(toeplitz_upper))
        lower = jnp.where(same_genome, toeplitz_lower, jnp.zeros_like(toeplitz_lower))
        return jnp.einsum(
            "gts,gis->git", upper, block_in, preferred_element_type=jnp.float32
        ) + jnp.einsum("gts,gis->git", lower, block_in, preferred_element_type=jnp.float32)

    local_part = lax.map(intra_block, (signal, tile_segs))
    end_keep = (tile_segs == tile_segs[:, -1:])[:, None, None, :]
    masked_signal = jnp.where(end_keep, signal, jnp.zeros_like(signal))
    states = jnp.einsum(
        "gsm,jgis->jgim", inward_upper, masked_signal, preferred_element_type=jnp.float32
    ) + jnp.einsum(
        "gsm,jgis->jgim", inward_lower, masked_signal, preferred_element_type=jnp.float32
    )
    carried = (tile_segs[:, -1] == before).astype(jnp.float32)

    def chain_link(carry_in, inputs):
        block_states, kept_flag = inputs
        step = (
            decay_re * kept_flag,
            decay_im * kept_flag,
            block_states[..., :mode_count],
            block_states[..., mode_count:],
        )
        return (complex_link(carry_in, step), carry_in)

    state_zero = jnp.zeros((group_count, GROUP, mode_count), jnp.float32)
    start_carry = (
        jnp.ones((group_count, mode_count), jnp.float32),
        jnp.zeros((group_count, mode_count), jnp.float32),
        state_zero,
        state_zero,
    )
    summary, entering = lax.scan(chain_link, start_carry, (states, carried))
    incoming = entering_2(
        (summary[0], summary[1], summary[2], summary[3]),
        "seq",
        complex_link,
        (start_carry[0], start_carry[1], start_carry[2], start_carry[3]),
    )
    incoming_re = incoming[2]
    incoming_im = incoming[3]
    reach_re = entering[0][:, :, None, :]
    reach_im = entering[1][:, :, None, :]
    full_re = entering[2] + reach_re * incoming_re - reach_im * incoming_im
    full_im = entering[3] + reach_re * incoming_im + reach_im * incoming_re
    keep_mask = (tile_segs == before[:, None]).astype(jnp.float32)
    carried_part = (
        jnp.einsum(
            "gtm,jgim->jgit",
            outward,
            jnp.concatenate((full_re, full_im), axis=3),
            precision=highest,
        )
        * keep_mask[:, None, None, :]
    )
    longconv = (
        local_part
        + carried_part
        + skip_gain.reshape(group_count, GROUP)[None, :, :, None] * signal.astype(jnp.float32)
    )
    long_cols = jnp.transpose(longconv, (1, 2, 0, 3)).reshape(chan_count, row_count)
    mixed = (query_proj.T.astype(jnp.float32) * long_cols).astype(jnp.bfloat16)
    mixed_wide = mixed.astype(jnp.float32)
    squares = lax.psum(jnp.sum(mixed_wide * mixed_wide, axis=0), ("chan", "rep"))
    normed = (mixed_wide * lax.rsqrt(squares / D + norm_eps)[None, :] * norm_gain[:, None]).astype(
        jnp.bfloat16
    )
    partial_value = channel_logits(normed, unembed)
    lanes = ("chan", "rep")
    lane_count = lax.axis_size(lanes)
    piece = row_count // lane_count
    piece_at = lax.axis_index(lanes) * piece
    logits = lax.psum_scatter(partial_value, lanes, scatter_dimension=0, tiled=True)
    logprob_piece = log_probs(logits, lax.dynamic_slice_in_dim(token_ids, piece_at, piece, 0))
    logprob = lax.all_gather(logprob_piece, lanes, tiled=True)
    genome_index = jnp.arange(genome_lengths.shape[0], dtype=jnp.int32)
    genome_part = jnp.sum(
        jnp.where(
            segments[:, None] == genome_index[None, :],
            logprob[:, None],
            jnp.zeros((row_count, genome_lengths.shape[0]), jnp.float32),
        ),
        axis=0,
    )
    totals = lax.psum(genome_part, "seq")
    return (logprob, totals / genome_lengths.astype(jnp.float32))


def solution(mesh):
    return jax.shard_map(
        per_device,
        mesh=mesh,
        in_specs=(
            P(("groups", "seq"), ("chan", "rep")),
            P(("groups", "seq"), ("chan", "rep")),
            P(("groups", "seq"), ("chan", "rep")),
            P(None, ("chan", "rep")),
            P(None, ("chan", "rep")),
            P(None, ("chan", "rep"), None),
            P(("chan", "rep")),
            P(("chan", "rep")),
            P(("chan", "rep"), None),
            P(("groups", "seq")),
            P("groups"),
        ),
        out_specs=(P(("groups", "seq")), P("groups")),
        check_vma=False,
    )
```

```python
import jax
import jax.numpy as jnp
from jax import lax
from jax.sharding import PartitionSpec as P

D = 8192
GROUP = 16


tile_rows = 128
short_margin = 8
norm_eps = 1e-05


def from_behind(shard, axis, by):
    count = lax.axis_size(axis)
    pairs = [(i, i + by) for i in range(count) if 0 <= i + by < count]
    return lax.ppermute(shard, axis, pairs)


def entering_2(part, axis, combine, identity):
    place = lax.axis_index(axis)
    count = lax.axis_size(axis)
    lead = part[0].shape[0]
    widths = [a.size // lead for a in part]

    def pack(t):
        return jnp.concatenate([a.reshape(lead, -1) for a in t], axis=1)

    def unpack(flat):
        pieces = []
        offset = 0
        for a, width in zip(part, widths):
            pieces.append(flat[:, offset : offset + width].reshape(a.shape))
            offset += width
        return tuple(pieces)

    ident = tuple(jnp.zeros_like(a) + jnp.asarray(e, a.dtype) for a, e in zip(part, identity))
    before = ident
    upto = tuple(part)
    shift = 1
    while shift < count:
        arrived = unpack(from_behind(pack(upto), axis, shift))
        arrived = tuple(jnp.where(place >= shift, r, i) for r, i in zip(arrived, ident))
        before = combine(arrived, before)
        upto = combine(arrived, upto)
        shift *= 2
    return before


def segment_ids(positions, genome_lengths):
    starts = jnp.cumsum(genome_lengths) - genome_lengths
    at_or_past = (positions[:, None] >= starts[None, :]).astype(jnp.int32)
    return jnp.sum(at_or_past, axis=1) - 1


def short_filter(keys_in, values_in, seg_list, out_rows, short_taps):
    gated = keys_in.astype(jnp.float32) * values_in.astype(jnp.float32)
    total_rows = keys_in.shape[0]
    lead_rows = total_rows - out_rows
    own_segs = seg_list[lead_rows:]
    result = jnp.zeros((out_rows, keys_in.shape[1]), jnp.float32)
    for lag_index in range(short_taps.shape[0]):
        shifted = gated[lead_rows - lag_index : total_rows - lag_index]
        same_genome = (seg_list[lead_rows - lag_index : total_rows - lag_index] == own_segs).astype(
            jnp.float32
        )
        result = (
            result
            + short_taps[lag_index].astype(jnp.float32)[None, :] * shifted * same_genome[:, None]
        )
    return result.astype(jnp.bfloat16)


def circulants(table):
    lag_count, width = table.shape
    lag_ids = lax.optimization_barrier(jnp.arange(lag_count, dtype=jnp.int32))
    out_pos = jnp.arange(tile_rows, dtype=jnp.int32)[:, None]
    in_pos = jnp.arange(tile_rows, dtype=jnp.int32)[None, :]
    lag_grid = (out_pos - in_pos + tile_rows) % tile_rows
    one_hot = (lag_grid.reshape(1, tile_rows * tile_rows) == lag_ids[:, None]).astype(table.dtype)
    picked = jnp.dot(table.T, one_hot, preferred_element_type=jnp.float32)
    return picked.astype(table.dtype).reshape(width, tile_rows, tile_rows)


def modal_tables(modal_poles):
    decay_rate = modal_poles[0]
    angles = modal_poles[1]
    residue_re = modal_poles[2]
    residue_im = modal_poles[3]
    powers = jnp.arange(tile_rows + 1).astype(jnp.float32)[:, None, None]
    magnitude = jnp.exp(-powers * decay_rate[None])
    power_re = magnitude * jnp.cos(powers * angles[None])
    power_im = magnitude * jnp.sin(powers * angles[None])
    kernel_re = residue_re[None] * power_re - residue_im[None] * power_im
    kernel_im = residue_re[None] * power_im + residue_im[None] * power_re
    kernel = jnp.sum(kernel_re[:tile_rows], axis=2)
    toeplitz = split_table(kernel)
    outward = jnp.transpose(jnp.concatenate((kernel_re[1:], -kernel_im[1:]), axis=2), (1, 0, 2))
    inward = jnp.transpose(
        jnp.concatenate((power_re[tile_rows - 1 :: -1], power_im[tile_rows - 1 :: -1]), axis=2),
        (1, 0, 2),
    )
    return (toeplitz, outward, inward, power_re[tile_rows], power_im[tile_rows])


def split_table(table):
    upper = table.astype(jnp.bfloat16)
    lower = (table - upper.astype(jnp.float32)).astype(jnp.bfloat16)
    return (upper, lower)


def complex_link(earlier, later):
    early_are, early_aim, early_sre, early_sim = earlier
    late_are, late_aim, late_sre, late_sim = later
    lead_re = late_are[..., None, :]
    lead_im = late_aim[..., None, :]
    return (
        late_are * early_are - late_aim * early_aim,
        late_are * early_aim + late_aim * early_are,
        lead_re * early_sre - lead_im * early_sim + late_sre,
        lead_re * early_sim + lead_im * early_sre + late_sim,
    )


def log_probs(logits, targets):
    vocab_ids = jnp.arange(logits.shape[1], dtype=jnp.int32)
    picked = jnp.sum(
        jnp.where(targets[:, None] == vocab_ids[None, :], logits, jnp.zeros_like(logits)), axis=1
    )
    return picked - jnp.log(jnp.sum(jnp.exp(logits), axis=1))


def channel_logits(normed_cols, unembed):
    return lax.dot_general(
        normed_cols, unembed, (((0,), (0,)), ((), ())), preferred_element_type=jnp.float32
    )


def per_device(
    query_proj,
    key_proj,
    value_proj,
    short_taps,
    medium_taps,
    modal_poles,
    skip_gain,
    norm_gain,
    unembed,
    token_ids,
    genome_lengths,
):
    highest = lax.Precision.HIGHEST
    row_count, chan_count = query_proj.shape
    group_count = chan_count // GROUP
    mode_count = modal_poles.shape[2]
    tile_count = row_count // tile_rows
    first_row = lax.axis_index("seq") * row_count
    segments = segment_ids(first_row + jnp.arange(row_count, dtype=jnp.int32), genome_lengths)
    halo = tile_rows + short_margin
    edge_pair = from_behind(
        jnp.stack((key_proj[row_count - halo :], value_proj[row_count - halo :])),
        "seq",
        1,
    )
    ext_segs = segment_ids(
        first_row - halo + jnp.arange(row_count + halo, dtype=jnp.int32),
        genome_lengths,
    )
    filtered = short_filter(
        jnp.concatenate((edge_pair[0], key_proj)),
        jnp.concatenate((edge_pair[1], value_proj)),
        ext_segs,
        row_count + tile_rows,
        short_taps,
    )
    ext_short = filtered.T.reshape(group_count, GROUP, row_count + tile_rows)
    medium_segs = segment_ids(
        first_row - tile_rows + jnp.arange(row_count + tile_rows, dtype=jnp.int32), genome_lengths
    )

    long_toeplitz, outward, inward, decay_re, decay_im = modal_tables(modal_poles)
    circ_medium = circulants(medium_taps)
    circ_long = circulants(jnp.concatenate(long_toeplitz, axis=1))
    toeplitz_upper = circ_long[:group_count]
    toeplitz_lower = circ_long[group_count:]
    lag_band = (
        jnp.arange(tile_rows, dtype=jnp.int32)[:, None] + tile_rows
        - jnp.arange(2 * tile_rows, dtype=jnp.int32)[None, :]
    )
    medium_band = (lag_band >= 0) & (lag_band < medium_taps.shape[0])
    long_band = lag_band[:, tile_rows:] >= 0

    def medium_block(tile_index):
        start = tile_index * tile_rows
        window = lax.dynamic_slice_in_dim(ext_short, start, 2 * tile_rows, 2)
        window_segs = lax.dynamic_slice_in_dim(medium_segs, start, 2 * tile_rows, 0)
        own_segs = lax.dynamic_slice_in_dim(segments, start, tile_rows, 0)
        same_genome = (own_segs[:, None] == window_segs[None, :]) & medium_band
        halves = []
        for half in range(2):
            cols = slice(half * tile_rows, (half + 1) * tile_rows)
            matrix = jnp.where(same_genome[None, :, cols], circ_medium, jnp.zeros_like(circ_medium))
            halves.append(
                jnp.einsum(
                    "gts,gis->git", matrix, window[:, :, cols], preferred_element_type=jnp.float32
                )
            )
        return (halves[0] + halves[1]).astype(jnp.bfloat16)

    signal = lax.map(medium_block, jnp.arange(tile_count, dtype=jnp.int32))
    inward_upper, inward_lower = split_table(inward)
    tile_segs = segments.reshape(tile_count, tile_rows)
    before = segment_ids(
        first_row + jnp.arange(tile_count, dtype=jnp.int32) * tile_rows - 1, genome_lengths
    )

    def intra_block(inputs):
        block_in, own_segs = inputs
        same_genome = ((own_segs[:, None] == own_segs[None, :]) & long_band)[None]
        upper = jnp.where(same_genome, toeplitz_upper, jnp.zeros_like(toeplitz_upper))
        lower = jnp.where(same_genome, toeplitz_lower, jnp.zeros_like(toeplitz_lower))
        return jnp.einsum(
            "gts,gis->git", upper, block_in, preferred_element_type=jnp.float32
        ) + jnp.einsum("gts,gis->git", lower, block_in, preferred_element_type=jnp.float32)

    local_part = lax.map(intra_block, (signal, tile_segs))
    end_keep = (tile_segs == tile_segs[:, -1:])[:, None, None, :]
    masked_signal = jnp.where(end_keep, signal, jnp.zeros_like(signal))
    states = jnp.einsum(
        "gsm,jgis->jgim", inward_upper, masked_signal, preferred_element_type=jnp.float32
    ) + jnp.einsum(
        "gsm,jgis->jgim", inward_lower, masked_signal, preferred_element_type=jnp.float32
    )
    carried = (tile_segs[:, -1] == before).astype(jnp.float32)

    def chain_link(carry_in, inputs):
        block_states, kept_flag = inputs
        step = (
            decay_re * kept_flag,
            decay_im * kept_flag,
            block_states[..., :mode_count],
            block_states[..., mode_count:],
        )
        return (complex_link(carry_in, step), carry_in)

    state_zero = jnp.zeros((group_count, GROUP, mode_count), jnp.float32)
    start_carry = (
        jnp.ones((group_count, mode_count), jnp.float32),
        jnp.zeros((group_count, mode_count), jnp.float32),
        state_zero,
        state_zero,
    )
    summary, entering = lax.scan(chain_link, start_carry, (states, carried))
    incoming = entering_2(
        (summary[0], summary[1], summary[2], summary[3]),
        "seq",
        complex_link,
        (start_carry[0], start_carry[1], start_carry[2], start_carry[3]),
    )
    incoming_re = incoming[2]
    incoming_im = incoming[3]
    reach_re = entering[0][:, :, None, :]
    reach_im = entering[1][:, :, None, :]
    full_re = entering[2] + reach_re * incoming_re - reach_im * incoming_im
    full_im = entering[3] + reach_re * incoming_im + reach_im * incoming_re
    keep_mask = (tile_segs == before[:, None]).astype(jnp.float32)
    carried_part = (
        jnp.einsum(
            "gtm,jgim->jgit",
            outward,
            jnp.concatenate((full_re, full_im), axis=3),
            precision=highest,
        )
        * keep_mask[:, None, None, :]
    )
    longconv = (
        local_part
        + carried_part
        + skip_gain.reshape(group_count, GROUP)[None, :, :, None] * signal.astype(jnp.float32)
    )
    long_cols = jnp.transpose(longconv, (1, 2, 0, 3)).reshape(chan_count, row_count)
    mixed = (query_proj.T.astype(jnp.float32) * long_cols).astype(jnp.bfloat16)
    mixed_wide = mixed.astype(jnp.float32)
    squares = lax.psum(jnp.sum(mixed_wide * mixed_wide, axis=0), ("chan", "rep"))
    normed = (mixed_wide * lax.rsqrt(squares / D + norm_eps)[None, :] * norm_gain[:, None]).astype(
        jnp.bfloat16
    )
    partial_value = channel_logits(normed, unembed)
    lanes = ("chan", "rep")
    lane_count = lax.axis_size(lanes)
    piece = row_count // lane_count
    piece_at = lax.axis_index(lanes) * piece
    logits = lax.psum_scatter(partial_value, lanes, scatter_dimension=0, tiled=True)
    logprob_piece = log_probs(logits, lax.dynamic_slice_in_dim(token_ids, piece_at, piece, 0))
    logprob = lax.all_gather(logprob_piece, lanes, tiled=True)
    genome_index = jnp.arange(genome_lengths.shape[0], dtype=jnp.int32)
    genome_part = jnp.sum(
        jnp.where(
            segments[:, None] == genome_index[None, :],
            logprob[:, None],
            jnp.zeros((row_count, genome_lengths.shape[0]), jnp.float32),
        ),
        axis=0,
    )
    totals = lax.psum(genome_part, "seq")
    return (logprob, totals / genome_lengths.astype(jnp.float32))


def solution(mesh):
    return jax.shard_map(
        per_device,
        mesh=mesh,
        in_specs=(
            P(("groups", "seq"), ("chan", "rep")),
            P(("groups", "seq"), ("chan", "rep")),
            P(("groups", "seq"), ("chan", "rep")),
            P(None, ("chan", "rep")),
            P(None, ("chan", "rep")),
            P(None, ("chan", "rep"), None),
            P(("chan", "rep")),
            P(("chan", "rep")),
            P(("chan", "rep"), None),
            P(("groups", "seq")),
            P("groups"),
        ),
        out_specs=(P(("groups", "seq")), P("groups")),
        check_vma=False,
    )
```

```python
import jax
import jax.numpy as jnp
from jax import lax
from jax.sharding import PartitionSpec as P

D = 8192
GROUP = 16


tile_rows = 128
short_margin = 8
norm_eps = 1e-05


def from_behind(shard, axis, by):
    count = lax.axis_size(axis)
    pairs = [(i, i + by) for i in range(count) if 0 <= i + by < count]
    return lax.ppermute(shard, axis, pairs)


def entering_2(part, axis, combine, identity):
    place = lax.axis_index(axis)
    count = lax.axis_size(axis)
    lead = part[0].shape[0]
    widths = [a.size // lead for a in part]

    def pack(t):
        return jnp.concatenate([a.reshape(lead, -1) for a in t], axis=1)

    def unpack(flat):
        pieces = []
        offset = 0
        for a, width in zip(part, widths):
            pieces.append(flat[:, offset : offset + width].reshape(a.shape))
            offset += width
        return tuple(pieces)

    ident = tuple(jnp.zeros_like(a) + jnp.asarray(e, a.dtype) for a, e in zip(part, identity))
    before = ident
    upto = tuple(part)
    shift = 1
    while shift < count:
        arrived = unpack(from_behind(pack(upto), axis, shift))
        arrived = tuple(jnp.where(place >= shift, r, i) for r, i in zip(arrived, ident))
        before = combine(arrived, before)
        upto = combine(arrived, upto)
        shift *= 2
    return before


def segment_ids(positions, genome_lengths):
    starts = jnp.cumsum(genome_lengths) - genome_lengths
    at_or_past = (positions[:, None] >= starts[None, :]).astype(jnp.int32)
    return jnp.sum(at_or_past, axis=1) - 1


def short_filter(keys_in, values_in, seg_list, out_rows, short_taps):
    gated = keys_in.astype(jnp.float32) * values_in.astype(jnp.float32)
    total_rows = keys_in.shape[0]
    lead_rows = total_rows - out_rows
    own_segs = seg_list[lead_rows:]
    result = jnp.zeros((out_rows, keys_in.shape[1]), jnp.float32)
    for lag_index in range(short_taps.shape[0]):
        shifted = gated[lead_rows - lag_index : total_rows - lag_index]
        same_genome = (seg_list[lead_rows - lag_index : total_rows - lag_index] == own_segs).astype(
            jnp.float32
        )
        result = (
            result
            + short_taps[lag_index].astype(jnp.float32)[None, :] * shifted * same_genome[:, None]
        )
    return result.astype(jnp.bfloat16)


def circulants(table):
    lag_count, width = table.shape
    lag_ids = lax.optimization_barrier(jnp.arange(lag_count, dtype=jnp.int32))
    out_pos = jnp.arange(tile_rows, dtype=jnp.int32)[:, None]
    in_pos = jnp.arange(tile_rows, dtype=jnp.int32)[None, :]
    lag_grid = (out_pos - in_pos + tile_rows) % tile_rows
    one_hot = (lag_grid.reshape(1, tile_rows * tile_rows) == lag_ids[:, None]).astype(table.dtype)
    picked = jnp.dot(table.T, one_hot, preferred_element_type=jnp.float32)
    return picked.astype(table.dtype).reshape(width, tile_rows, tile_rows)


def pole_powers(decay_rate, angles, exponents):
    e = exponents.astype(jnp.float32)[:, None, None]
    magnitude = jnp.exp(-e * decay_rate[None])
    return (magnitude * jnp.cos(e * angles[None]), magnitude * jnp.sin(e * angles[None]))


def power_products(high, low):
    high_re, high_im = high[0][:, None], high[1][:, None]
    low_re, low_im = low[0][None], low[1][None]
    out_re = high_re * low_re - high_im * low_im
    out_im = high_re * low_im + high_im * low_re
    return (out_re.reshape((-1,) + out_re.shape[2:]), out_im.reshape((-1,) + out_im.shape[2:]))


def modal_tables(modal_poles):
    decay_rate = modal_poles[0]
    angles = modal_poles[1]
    residue_re = modal_poles[2]
    residue_im = modal_poles[3]
    step = 16
    spans = tile_rows // step
    low = pole_powers(decay_rate, angles, jnp.arange(step))
    high = pole_powers(decay_rate, angles, jnp.arange(spans + 1) * step)
    forward = power_products(high, low)
    power_re = forward[0][: tile_rows + 1]
    power_im = forward[1][: tile_rows + 1]
    backward = power_products(
        (high[0][spans - 1 :: -1], high[1][spans - 1 :: -1]), (low[0][::-1], low[1][::-1])
    )
    kernel_re = residue_re[None] * power_re - residue_im[None] * power_im
    kernel_im = residue_re[None] * power_im + residue_im[None] * power_re
    kernel = jnp.sum(kernel_re[:tile_rows], axis=2)
    toeplitz = split_table(kernel)
    outward = jnp.transpose(jnp.concatenate((kernel_re[1:], -kernel_im[1:]), axis=2), (1, 0, 2))
    inward = jnp.transpose(jnp.concatenate(backward, axis=2), (1, 0, 2))
    return (toeplitz, outward, inward, power_re[tile_rows], power_im[tile_rows])


def split_table(table):
    upper = table.astype(jnp.bfloat16)
    lower = (table - upper.astype(jnp.float32)).astype(jnp.bfloat16)
    return (upper, lower)


def complex_link(earlier, later):
    early_are, early_aim, early_sre, early_sim = earlier
    late_are, late_aim, late_sre, late_sim = later
    lead_re = late_are[..., None, :]
    lead_im = late_aim[..., None, :]
    return (
        late_are * early_are - late_aim * early_aim,
        late_are * early_aim + late_aim * early_are,
        lead_re * early_sre - lead_im * early_sim + late_sre,
        lead_re * early_sim + lead_im * early_sre + late_sim,
    )


def log_probs(logits, targets):
    vocab_ids = jnp.arange(logits.shape[1], dtype=jnp.int32)
    picked = jnp.sum(
        jnp.where(targets[:, None] == vocab_ids[None, :], logits, jnp.zeros_like(logits)), axis=1
    )
    return picked - jnp.log(jnp.sum(jnp.exp(logits), axis=1))


def channel_logits(normed_cols, unembed):
    return lax.dot_general(
        normed_cols, unembed, (((0,), (0,)), ((), ())), preferred_element_type=jnp.float32
    )


def per_device(
    query_proj,
    key_proj,
    value_proj,
    short_taps,
    medium_taps,
    modal_poles,
    skip_gain,
    norm_gain,
    unembed,
    token_ids,
    genome_lengths,
):
    highest = lax.Precision.HIGHEST
    row_count, chan_count = query_proj.shape
    group_count = chan_count // GROUP
    mode_count = modal_poles.shape[2]
    tile_count = row_count // tile_rows
    first_row = lax.axis_index("seq") * row_count
    segments = segment_ids(first_row + jnp.arange(row_count, dtype=jnp.int32), genome_lengths)
    halo = tile_rows + short_margin
    edge_pair = from_behind(
        jnp.stack((key_proj[row_count - halo :], value_proj[row_count - halo :])),
        "seq",
        1,
    )
    ext_segs = segment_ids(
        first_row - halo + jnp.arange(row_count + halo, dtype=jnp.int32),
        genome_lengths,
    )
    filtered = short_filter(
        jnp.concatenate((edge_pair[0], key_proj)),
        jnp.concatenate((edge_pair[1], value_proj)),
        ext_segs,
        row_count + tile_rows,
        short_taps,
    )
    ext_short = filtered.T.reshape(group_count, GROUP, row_count + tile_rows)
    medium_segs = segment_ids(
        first_row - tile_rows + jnp.arange(row_count + tile_rows, dtype=jnp.int32), genome_lengths
    )

    long_toeplitz, outward, inward, decay_re, decay_im = modal_tables(modal_poles)
    circ = circulants(jnp.concatenate((medium_taps, long_toeplitz[0], long_toeplitz[1]), axis=1))
    circ_medium = jnp.concatenate((circ[:group_count], circ[:group_count]), axis=2)
    toeplitz_upper = circ[group_count : 2 * group_count]
    toeplitz_lower = circ[2 * group_count :]
    lag_band = (
        jnp.arange(tile_rows, dtype=jnp.int32)[:, None] + tile_rows
        - jnp.arange(2 * tile_rows, dtype=jnp.int32)[None, :]
    )
    medium_band = (lag_band >= 0) & (lag_band < medium_taps.shape[0])
    long_band = lag_band[:, tile_rows:] >= 0

    def medium_block(tile_index):
        start = tile_index * tile_rows
        window = lax.dynamic_slice_in_dim(ext_short, start, 2 * tile_rows, 2)
        window_segs = lax.dynamic_slice_in_dim(medium_segs, start, 2 * tile_rows, 0)
        own_segs = lax.dynamic_slice_in_dim(segments, start, tile_rows, 0)
        same_genome = (own_segs[:, None] == window_segs[None, :]) & medium_band
        matrix = jnp.where(same_genome[None], circ_medium, jnp.zeros_like(circ_medium))
        return jnp.einsum(
            "gts,gis->git", matrix, window, preferred_element_type=jnp.float32
        ).astype(jnp.bfloat16)

    signal = lax.map(medium_block, jnp.arange(tile_count, dtype=jnp.int32))
    inward_upper, inward_lower = split_table(inward)
    tile_segs = segments.reshape(tile_count, tile_rows)
    before = segment_ids(
        first_row + jnp.arange(tile_count, dtype=jnp.int32) * tile_rows - 1, genome_lengths
    )

    def intra_block(inputs):
        block_in, own_segs = inputs
        same_genome = ((own_segs[:, None] == own_segs[None, :]) & long_band)[None]
        upper = jnp.where(same_genome, toeplitz_upper, jnp.zeros_like(toeplitz_upper))
        lower = jnp.where(same_genome, toeplitz_lower, jnp.zeros_like(toeplitz_lower))
        return jnp.einsum(
            "gts,gis->git", upper, block_in, preferred_element_type=jnp.float32
        ) + jnp.einsum("gts,gis->git", lower, block_in, preferred_element_type=jnp.float32)

    local_part = lax.map(intra_block, (signal, tile_segs))
    end_keep = (tile_segs == tile_segs[:, -1:])[:, None, None, :]
    masked_signal = jnp.where(end_keep, signal, jnp.zeros_like(signal))
    states = jnp.einsum(
        "gsm,jgis->jgim", inward_upper, masked_signal, preferred_element_type=jnp.float32
    ) + jnp.einsum(
        "gsm,jgis->jgim", inward_lower, masked_signal, preferred_element_type=jnp.float32
    )
    carried = (tile_segs[:, -1] == before).astype(jnp.float32)

    def chain_link(carry_in, inputs):
        block_states, kept_flag = inputs
        step = (
            decay_re * kept_flag,
            decay_im * kept_flag,
            block_states[..., :mode_count],
            block_states[..., mode_count:],
        )
        return (complex_link(carry_in, step), carry_in)

    state_zero = jnp.zeros((group_count, GROUP, mode_count), jnp.float32)
    start_carry = (
        jnp.ones((group_count, mode_count), jnp.float32),
        jnp.zeros((group_count, mode_count), jnp.float32),
        state_zero,
        state_zero,
    )
    summary, entering = lax.scan(chain_link, start_carry, (states, carried))
    incoming = entering_2(
        (summary[0], summary[1], summary[2], summary[3]),
        "seq",
        complex_link,
        (start_carry[0], start_carry[1], start_carry[2], start_carry[3]),
    )
    incoming_re = incoming[2]
    incoming_im = incoming[3]
    reach_re = entering[0][:, :, None, :]
    reach_im = entering[1][:, :, None, :]
    full_re = entering[2] + reach_re * incoming_re - reach_im * incoming_im
    full_im = entering[3] + reach_re * incoming_im + reach_im * incoming_re
    keep_mask = (tile_segs == before[:, None]).astype(jnp.float32)
    carried_part = (
        jnp.einsum(
            "gtm,jgim->jgit",
            outward,
            jnp.concatenate((full_re, full_im), axis=3),
            precision=highest,
        )
        * keep_mask[:, None, None, :]
    )
    longconv = (
        local_part
        + carried_part
        + skip_gain.reshape(group_count, GROUP)[None, :, :, None] * signal.astype(jnp.float32)
    )
    long_cols = jnp.transpose(longconv, (1, 2, 0, 3)).reshape(chan_count, row_count)
    mixed = (query_proj.T.astype(jnp.float32) * long_cols).astype(jnp.bfloat16)
    mixed_wide = mixed.astype(jnp.float32)
    squares = lax.psum(jnp.sum(mixed_wide * mixed_wide, axis=0), ("chan", "rep"))
    normed = (mixed_wide * lax.rsqrt(squares / D + norm_eps)[None, :] * norm_gain[:, None]).astype(
        jnp.bfloat16
    )
    partial_value = channel_logits(normed, unembed)
    lanes = ("chan", "rep")
    lane_count = lax.axis_size(lanes)
    piece = row_count // lane_count
    piece_at = lax.axis_index(lanes) * piece
    logits = lax.psum_scatter(partial_value, lanes, scatter_dimension=0, tiled=True)
    logprob_piece = log_probs(logits, lax.dynamic_slice_in_dim(token_ids, piece_at, piece, 0))
    logprob = lax.all_gather(logprob_piece, lanes, tiled=True)
    genome_index = jnp.arange(genome_lengths.shape[0], dtype=jnp.int32)
    genome_part = jnp.sum(
        jnp.where(
            segments[:, None] == genome_index[None, :],
            logprob[:, None],
            jnp.zeros((row_count, genome_lengths.shape[0]), jnp.float32),
        ),
        axis=0,
    )
    totals = lax.psum(genome_part, "seq")
    return (logprob, totals / genome_lengths.astype(jnp.float32))


def solution(mesh):
    return jax.shard_map(
        per_device,
        mesh=mesh,
        in_specs=(
            P(("groups", "seq"), ("chan", "rep")),
            P(("groups", "seq"), ("chan", "rep")),
            P(("groups", "seq"), ("chan", "rep")),
            P(None, ("chan", "rep")),
            P(None, ("chan", "rep")),
            P(None, ("chan", "rep"), None),
            P(("chan", "rep")),
            P(("chan", "rep")),
            P(("chan", "rep"), None),
            P(("groups", "seq")),
            P("groups"),
        ),
        out_specs=(P(("groups", "seq")), P("groups")),
        check_vma=False,
    )
```

```python
import jax
import jax.numpy as jnp
from jax import lax
from jax.sharding import PartitionSpec as P

D = 8192
GROUP = 16


tile_rows = 128
short_margin = 8
norm_eps = 1e-05


def from_behind(shard, axis, by):
    count = lax.axis_size(axis)
    pairs = [(i, i + by) for i in range(count) if 0 <= i + by < count]
    return lax.ppermute(shard, axis, pairs)


def sum_over(part, axis):
    count = lax.axis_size(axis)
    if count & (count - 1):
        return lax.psum(part, axis)
    bit = 1
    while bit < count:
        part = part + lax.ppermute(part, axis, [(i, i ^ bit) for i in range(count)])
        bit *= 2
    return part


def entering_2(part, axis, combine, identity):
    place = lax.axis_index(axis)
    count = lax.axis_size(axis)
    lead = part[0].shape[0]
    widths = [a.size // lead for a in part]

    def pack(t):
        return jnp.concatenate([a.reshape(lead, -1) for a in t], axis=1)

    def unpack(flat):
        pieces = []
        offset = 0
        for a, width in zip(part, widths):
            pieces.append(flat[:, offset : offset + width].reshape(a.shape))
            offset += width
        return tuple(pieces)

    ident = tuple(jnp.zeros_like(a) + jnp.asarray(e, a.dtype) for a, e in zip(part, identity))
    before = ident
    upto = tuple(part)
    shift = 1
    while shift < count:
        arrived = unpack(from_behind(pack(upto), axis, shift))
        arrived = tuple(jnp.where(place >= shift, r, i) for r, i in zip(arrived, ident))
        before = combine(arrived, before)
        upto = combine(arrived, upto)
        shift *= 2
    return before


def segment_ids(positions, genome_lengths):
    starts = jnp.cumsum(genome_lengths) - genome_lengths
    at_or_past = (positions[:, None] >= starts[None, :]).astype(jnp.int32)
    return jnp.sum(at_or_past, axis=1) - 1


def short_filter(keys_in, values_in, seg_list, out_rows, short_taps):
    gated = keys_in.astype(jnp.float32) * values_in.astype(jnp.float32)
    total_rows = keys_in.shape[0]
    lead_rows = total_rows - out_rows
    own_segs = seg_list[lead_rows:]
    result = jnp.zeros((out_rows, keys_in.shape[1]), jnp.float32)
    for lag_index in range(short_taps.shape[0]):
        shifted = gated[lead_rows - lag_index : total_rows - lag_index]
        same_genome = (seg_list[lead_rows - lag_index : total_rows - lag_index] == own_segs).astype(
            jnp.float32
        )
        result = (
            result
            + short_taps[lag_index].astype(jnp.float32)[None, :] * shifted * same_genome[:, None]
        )
    return result.astype(jnp.bfloat16)


def circulants(table):
    lag_count, width = table.shape
    lag_ids = lax.optimization_barrier(jnp.arange(lag_count, dtype=jnp.int32))
    out_pos = jnp.arange(tile_rows, dtype=jnp.int32)[:, None]
    in_pos = jnp.arange(tile_rows, dtype=jnp.int32)[None, :]
    lag_grid = (out_pos - in_pos + tile_rows) % tile_rows
    one_hot = (lag_grid.reshape(1, tile_rows * tile_rows) == lag_ids[:, None]).astype(table.dtype)
    picked = jnp.dot(table.T, one_hot, preferred_element_type=jnp.float32)
    return picked.astype(table.dtype).reshape(width, tile_rows, tile_rows)


def modal_tables(modal_poles):
    decay_rate = modal_poles[0]
    angles = modal_poles[1]
    residue_re = modal_poles[2]
    residue_im = modal_poles[3]
    powers = jnp.arange(tile_rows + 1).astype(jnp.float32)[:, None, None]
    magnitude = jnp.exp(-powers * decay_rate[None])
    power_re = magnitude * jnp.cos(powers * angles[None])
    power_im = magnitude * jnp.sin(powers * angles[None])
    kernel_re = residue_re[None] * power_re - residue_im[None] * power_im
    kernel_im = residue_re[None] * power_im + residue_im[None] * power_re
    kernel = jnp.sum(kernel_re[:tile_rows], axis=2)
    toeplitz = split_table(kernel)
    outward = jnp.transpose(jnp.concatenate((kernel_re[1:], -kernel_im[1:]), axis=2), (1, 0, 2))
    inward = jnp.transpose(
        jnp.concatenate((power_re[tile_rows - 1 :: -1], power_im[tile_rows - 1 :: -1]), axis=2),
        (1, 0, 2),
    )
    return (toeplitz, outward, inward, power_re[tile_rows], power_im[tile_rows])


def split_table(table):
    upper = table.astype(jnp.bfloat16)
    lower = (table - upper.astype(jnp.float32)).astype(jnp.bfloat16)
    return (upper, lower)


def complex_link(earlier, later):
    early_are, early_aim, early_sre, early_sim = earlier
    late_are, late_aim, late_sre, late_sim = later
    lead_re = late_are[..., None, :]
    lead_im = late_aim[..., None, :]
    return (
        late_are * early_are - late_aim * early_aim,
        late_are * early_aim + late_aim * early_are,
        lead_re * early_sre - lead_im * early_sim + late_sre,
        lead_re * early_sim + lead_im * early_sre + late_sim,
    )


def log_probs(logits, targets):
    vocab_ids = jnp.arange(logits.shape[1], dtype=jnp.int32)
    picked = jnp.sum(
        jnp.where(targets[:, None] == vocab_ids[None, :], logits, jnp.zeros_like(logits)), axis=1
    )
    return picked - jnp.log(jnp.sum(jnp.exp(logits), axis=1))


def channel_logits(normed_cols, unembed):
    return lax.dot_general(
        normed_cols, unembed, (((0,), (0,)), ((), ())), preferred_element_type=jnp.float32
    )


def per_device(
    query_proj,
    key_proj,
    value_proj,
    short_taps,
    medium_taps,
    modal_poles,
    skip_gain,
    norm_gain,
    unembed,
    token_ids,
    genome_lengths,
):
    highest = lax.Precision.HIGHEST
    row_count, chan_count = query_proj.shape
    group_count = chan_count // GROUP
    mode_count = modal_poles.shape[2]
    tile_count = row_count // tile_rows
    first_row = lax.axis_index("seq") * row_count
    segments = segment_ids(first_row + jnp.arange(row_count, dtype=jnp.int32), genome_lengths)
    halo = tile_rows + short_margin
    edge_pair = from_behind(
        jnp.stack((key_proj[row_count - halo :], value_proj[row_count - halo :])),
        "seq",
        1,
    )
    ext_segs = segment_ids(
        first_row - halo + jnp.arange(row_count + halo, dtype=jnp.int32),
        genome_lengths,
    )
    filtered = short_filter(
        jnp.concatenate((edge_pair[0], key_proj)),
        jnp.concatenate((edge_pair[1], value_proj)),
        ext_segs,
        row_count + tile_rows,
        short_taps,
    )
    ext_short = filtered.T.reshape(group_count, GROUP, row_count + tile_rows)
    medium_segs = segment_ids(
        first_row - tile_rows + jnp.arange(row_count + tile_rows, dtype=jnp.int32), genome_lengths
    )

    long_toeplitz, outward, inward, decay_re, decay_im = modal_tables(modal_poles)
    circ = circulants(jnp.concatenate((medium_taps, long_toeplitz[0], long_toeplitz[1]), axis=1))
    circ_medium = jnp.concatenate((circ[:group_count], circ[:group_count]), axis=2)
    toeplitz_upper = circ[group_count : 2 * group_count]
    toeplitz_lower = circ[2 * group_count :]
    lag_band = (
        jnp.arange(tile_rows, dtype=jnp.int32)[:, None] + tile_rows
        - jnp.arange(2 * tile_rows, dtype=jnp.int32)[None, :]
    )
    medium_band = (lag_band >= 0) & (lag_band < medium_taps.shape[0])
    long_band = lag_band[:, tile_rows:] >= 0

    def medium_block(tile_index):
        start = tile_index * tile_rows
        window = lax.dynamic_slice_in_dim(ext_short, start, 2 * tile_rows, 2)
        window_segs = lax.dynamic_slice_in_dim(medium_segs, start, 2 * tile_rows, 0)
        own_segs = lax.dynamic_slice_in_dim(segments, start, tile_rows, 0)
        same_genome = (own_segs[:, None] == window_segs[None, :]) & medium_band
        matrix = jnp.where(same_genome[None], circ_medium, jnp.zeros_like(circ_medium))
        return jnp.einsum(
            "gts,gis->git", matrix, window, preferred_element_type=jnp.float32
        ).astype(jnp.bfloat16)

    signal = jnp.stack([medium_block(tile_index) for tile_index in range(tile_count)])
    inward_upper, inward_lower = split_table(inward)
    tile_segs = segments.reshape(tile_count, tile_rows)
    before = segment_ids(
        first_row + jnp.arange(tile_count, dtype=jnp.int32) * tile_rows - 1, genome_lengths
    )

    def intra_block(inputs):
        block_in, own_segs = inputs
        same_genome = ((own_segs[:, None] == own_segs[None, :]) & long_band)[None]
        upper = jnp.where(same_genome, toeplitz_upper, jnp.zeros_like(toeplitz_upper))
        lower = jnp.where(same_genome, toeplitz_lower, jnp.zeros_like(toeplitz_lower))
        return jnp.einsum(
            "gts,gis->git", upper, block_in, preferred_element_type=jnp.float32
        ) + jnp.einsum("gts,gis->git", lower, block_in, preferred_element_type=jnp.float32)

    local_part = jnp.stack([intra_block((signal[j], tile_segs[j])) for j in range(tile_count)])
    end_keep = (tile_segs == tile_segs[:, -1:])[:, None, None, :]
    masked_signal = jnp.where(end_keep, signal, jnp.zeros_like(signal))
    states = jnp.einsum(
        "gsm,jgis->jgim", inward_upper, masked_signal, preferred_element_type=jnp.float32
    ) + jnp.einsum(
        "gsm,jgis->jgim", inward_lower, masked_signal, preferred_element_type=jnp.float32
    )
    carried = (tile_segs[:, -1] == before).astype(jnp.float32)

    def chain_link(carry_in, inputs):
        block_states, kept_flag = inputs
        step = (
            decay_re * kept_flag,
            decay_im * kept_flag,
            block_states[..., :mode_count],
            block_states[..., mode_count:],
        )
        return (complex_link(carry_in, step), carry_in)

    state_zero = jnp.zeros((group_count, GROUP, mode_count), jnp.float32)
    start_carry = (
        jnp.ones((group_count, mode_count), jnp.float32),
        jnp.zeros((group_count, mode_count), jnp.float32),
        state_zero,
        state_zero,
    )
    summary, entering = lax.scan(chain_link, start_carry, (states, carried))
    incoming = entering_2(
        (summary[0], summary[1], summary[2], summary[3]),
        "seq",
        complex_link,
        (start_carry[0], start_carry[1], start_carry[2], start_carry[3]),
    )
    incoming_re = incoming[2]
    incoming_im = incoming[3]
    reach_re = entering[0][:, :, None, :]
    reach_im = entering[1][:, :, None, :]
    full_re = entering[2] + reach_re * incoming_re - reach_im * incoming_im
    full_im = entering[3] + reach_re * incoming_im + reach_im * incoming_re
    keep_mask = (tile_segs == before[:, None]).astype(jnp.float32)
    carried_part = (
        jnp.einsum(
            "gtm,jgim->jgit",
            outward,
            jnp.concatenate((full_re, full_im), axis=3),
            precision=highest,
        )
        * keep_mask[:, None, None, :]
    )
    longconv = (
        local_part
        + carried_part
        + skip_gain.reshape(group_count, GROUP)[None, :, :, None] * signal.astype(jnp.float32)
    )
    long_cols = jnp.transpose(longconv, (1, 2, 0, 3)).reshape(chan_count, row_count)
    mixed = (query_proj.T.astype(jnp.float32) * long_cols).astype(jnp.bfloat16)
    mixed_wide = mixed.astype(jnp.float32)
    squares = lax.psum(jnp.sum(mixed_wide * mixed_wide, axis=0), ("chan", "rep"))
    normed = (mixed_wide * lax.rsqrt(squares / D + norm_eps)[None, :] * norm_gain[:, None]).astype(
        jnp.bfloat16
    )
    partial_value = channel_logits(normed, unembed)
    lanes = ("chan", "rep")
    lane_count = lax.axis_size(lanes)
    piece = row_count // lane_count
    piece_at = lax.axis_index(lanes) * piece
    logits = lax.psum_scatter(partial_value, lanes, scatter_dimension=0, tiled=True)
    logprob_piece = log_probs(logits, lax.dynamic_slice_in_dim(token_ids, piece_at, piece, 0))
    logprob = lax.all_gather(logprob_piece, lanes, tiled=True)
    genome_index = jnp.arange(genome_lengths.shape[0], dtype=jnp.int32)
    genome_part = jnp.sum(
        jnp.where(
            segments[:, None] == genome_index[None, :],
            logprob[:, None],
            jnp.zeros((row_count, genome_lengths.shape[0]), jnp.float32),
        ),
        axis=0,
    )
    totals = sum_over(genome_part, "seq")
    return (logprob, totals / genome_lengths.astype(jnp.float32))


def solution(mesh):
    return jax.shard_map(
        per_device,
        mesh=mesh,
        in_specs=(
            P(("groups", "seq"), ("chan", "rep")),
            P(("groups", "seq"), ("chan", "rep")),
            P(("groups", "seq"), ("chan", "rep")),
            P(None, ("chan", "rep")),
            P(None, ("chan", "rep")),
            P(None, ("chan", "rep"), None),
            P(("chan", "rep")),
            P(("chan", "rep")),
            P(("chan", "rep"), None),
            P(("groups", "seq")),
            P("groups"),
        ),
        out_specs=(P(("groups", "seq")), P("groups")),
        check_vma=False,
    )
```

```python
import jax
import jax.numpy as jnp
from jax import lax
from jax.sharding import PartitionSpec as P

D = 8192
GROUP = 16


tile_rows = 128
short_margin = 8
norm_eps = 1e-05


def from_behind(shard, axis, by):
    count = lax.axis_size(axis)
    pairs = [(i, i + by) for i in range(count) if 0 <= i + by < count]
    return lax.ppermute(shard, axis, pairs)


def scatter_sum(part, axes):
    count = lax.axis_size(axes)
    if count & (count - 1):
        return lax.psum_scatter(part, axes, scatter_dimension=0, tiled=True)
    place = lax.axis_index(axes)
    bit = count // 2
    while bit >= 1:
        half = part.shape[0] // 2
        upper = (place & bit) != 0
        keep = jnp.where(upper, part[half:], part[:half])
        give = jnp.where(upper, part[:half], part[half:])
        part = keep + lax.ppermute(give, axes, [(i, i ^ bit) for i in range(count)])
        bit //= 2
    return part


def sum_over(part, axis):
    count = lax.axis_size(axis)
    if count & (count - 1):
        return lax.psum(part, axis)
    bit = 1
    while bit < count:
        part = part + lax.ppermute(part, axis, [(i, i ^ bit) for i in range(count)])
        bit *= 2
    return part


def entering_2(part, axis, combine, identity):
    place = lax.axis_index(axis)
    count = lax.axis_size(axis)
    lead = part[0].shape[0]
    widths = [a.size // lead for a in part]

    def pack(t):
        return jnp.concatenate([a.reshape(lead, -1) for a in t], axis=1)

    def unpack(flat):
        pieces = []
        offset = 0
        for a, width in zip(part, widths):
            pieces.append(flat[:, offset : offset + width].reshape(a.shape))
            offset += width
        return tuple(pieces)

    ident = tuple(jnp.zeros_like(a) + jnp.asarray(e, a.dtype) for a, e in zip(part, identity))
    before = ident
    upto = tuple(part)
    shift = 1
    while shift < count:
        arrived = unpack(from_behind(pack(upto), axis, shift))
        arrived = tuple(jnp.where(place >= shift, r, i) for r, i in zip(arrived, ident))
        before = combine(arrived, before)
        upto = combine(arrived, upto)
        shift *= 2
    return before


def segment_ids(positions, genome_lengths):
    starts = jnp.cumsum(genome_lengths) - genome_lengths
    at_or_past = (positions[:, None] >= starts[None, :]).astype(jnp.int32)
    return jnp.sum(at_or_past, axis=1) - 1


def short_filter(keys_in, values_in, seg_list, out_rows, short_taps):
    gated = keys_in.astype(jnp.float32) * values_in.astype(jnp.float32)
    total_rows = keys_in.shape[0]
    lead_rows = total_rows - out_rows
    own_segs = seg_list[lead_rows:]
    result = jnp.zeros((out_rows, keys_in.shape[1]), jnp.float32)
    for lag_index in range(short_taps.shape[0]):
        shifted = gated[lead_rows - lag_index : total_rows - lag_index]
        same_genome = (seg_list[lead_rows - lag_index : total_rows - lag_index] == own_segs).astype(
            jnp.float32
        )
        result = (
            result
            + short_taps[lag_index].astype(jnp.float32)[None, :] * shifted * same_genome[:, None]
        )
    return result.astype(jnp.bfloat16)


def circulants(table):
    lag_count, width = table.shape
    lag_ids = lax.optimization_barrier(jnp.arange(lag_count, dtype=jnp.int32))
    out_pos = jnp.arange(tile_rows, dtype=jnp.int32)[:, None]
    in_pos = jnp.arange(tile_rows, dtype=jnp.int32)[None, :]
    lag_grid = (out_pos - in_pos + tile_rows) % tile_rows
    one_hot = (lag_grid.reshape(1, tile_rows * tile_rows) == lag_ids[:, None]).astype(table.dtype)
    picked = jnp.dot(table.T, one_hot, preferred_element_type=jnp.float32)
    return picked.astype(table.dtype).reshape(width, tile_rows, tile_rows)


def modal_tables(modal_poles):
    decay_rate = modal_poles[0]
    angles = modal_poles[1]
    residue_re = modal_poles[2]
    residue_im = modal_poles[3]
    powers = jnp.arange(tile_rows + 1).astype(jnp.float32)[:, None, None]
    magnitude = jnp.exp(-powers * decay_rate[None])
    power_re = magnitude * jnp.cos(powers * angles[None])
    power_im = magnitude * jnp.sin(powers * angles[None])
    kernel_re = residue_re[None] * power_re - residue_im[None] * power_im
    kernel_im = residue_re[None] * power_im + residue_im[None] * power_re
    kernel = jnp.sum(kernel_re[:tile_rows], axis=2)
    toeplitz = split_table(kernel)
    outward = jnp.transpose(jnp.concatenate((kernel_re[1:], -kernel_im[1:]), axis=2), (1, 0, 2))
    inward = jnp.transpose(
        jnp.concatenate((power_re[tile_rows - 1 :: -1], power_im[tile_rows - 1 :: -1]), axis=2),
        (1, 0, 2),
    )
    return (toeplitz, outward, inward, power_re[tile_rows], power_im[tile_rows])


def split_table(table):
    upper = table.astype(jnp.bfloat16)
    lower = (table - upper.astype(jnp.float32)).astype(jnp.bfloat16)
    return (upper, lower)


def complex_link(earlier, later):
    early_are, early_aim, early_sre, early_sim = earlier
    late_are, late_aim, late_sre, late_sim = later
    lead_re = late_are[..., None, :]
    lead_im = late_aim[..., None, :]
    return (
        late_are * early_are - late_aim * early_aim,
        late_are * early_aim + late_aim * early_are,
        lead_re * early_sre - lead_im * early_sim + late_sre,
        lead_re * early_sim + lead_im * early_sre + late_sim,
    )


def log_probs(logits, targets):
    vocab_ids = jnp.arange(logits.shape[1], dtype=jnp.int32)
    picked = jnp.sum(
        jnp.where(targets[:, None] == vocab_ids[None, :], logits, jnp.zeros_like(logits)), axis=1
    )
    return picked - jnp.log(jnp.sum(jnp.exp(logits), axis=1))


def channel_logits(normed_cols, unembed):
    return lax.dot_general(
        normed_cols, unembed, (((0,), (0,)), ((), ())), preferred_element_type=jnp.float32
    )


def per_device(
    query_proj,
    key_proj,
    value_proj,
    short_taps,
    medium_taps,
    modal_poles,
    skip_gain,
    norm_gain,
    unembed,
    token_ids,
    genome_lengths,
):
    highest = lax.Precision.HIGHEST
    row_count, chan_count = query_proj.shape
    group_count = chan_count // GROUP
    mode_count = modal_poles.shape[2]
    tile_count = row_count // tile_rows
    first_row = lax.axis_index("seq") * row_count
    segments = segment_ids(first_row + jnp.arange(row_count, dtype=jnp.int32), genome_lengths)
    halo = tile_rows + short_margin
    edge_pair = from_behind(
        jnp.stack((key_proj[row_count - halo :], value_proj[row_count - halo :])),
        "seq",
        1,
    )
    ext_segs = segment_ids(
        first_row - halo + jnp.arange(row_count + halo, dtype=jnp.int32),
        genome_lengths,
    )
    filtered = short_filter(
        jnp.concatenate((edge_pair[0], key_proj)),
        jnp.concatenate((edge_pair[1], value_proj)),
        ext_segs,
        row_count + tile_rows,
        short_taps,
    )
    ext_short = filtered.T.reshape(group_count, GROUP, row_count + tile_rows)
    medium_segs = segment_ids(
        first_row - tile_rows + jnp.arange(row_count + tile_rows, dtype=jnp.int32), genome_lengths
    )

    long_toeplitz, outward, inward, decay_re, decay_im = modal_tables(modal_poles)
    circ = circulants(jnp.concatenate((medium_taps, long_toeplitz[0], long_toeplitz[1]), axis=1))
    circ_medium = jnp.concatenate((circ[:group_count], circ[:group_count]), axis=2)
    toeplitz_upper = circ[group_count : 2 * group_count]
    toeplitz_lower = circ[2 * group_count :]
    lag_band = (
        jnp.arange(tile_rows, dtype=jnp.int32)[:, None] + tile_rows
        - jnp.arange(2 * tile_rows, dtype=jnp.int32)[None, :]
    )
    medium_band = (lag_band >= 0) & (lag_band < medium_taps.shape[0])
    long_band = lag_band[:, tile_rows:] >= 0

    def medium_block(tile_index):
        start = tile_index * tile_rows
        window = lax.dynamic_slice_in_dim(ext_short, start, 2 * tile_rows, 2)
        window_segs = lax.dynamic_slice_in_dim(medium_segs, start, 2 * tile_rows, 0)
        own_segs = lax.dynamic_slice_in_dim(segments, start, tile_rows, 0)
        same_genome = (own_segs[:, None] == window_segs[None, :]) & medium_band
        matrix = jnp.where(same_genome[None], circ_medium, jnp.zeros_like(circ_medium))
        return jnp.einsum(
            "gts,gis->git", matrix, window, preferred_element_type=jnp.float32
        ).astype(jnp.bfloat16)

    signal = jnp.stack([medium_block(tile_index) for tile_index in range(tile_count)])
    inward_upper, inward_lower = split_table(inward)
    tile_segs = segments.reshape(tile_count, tile_rows)
    before = segment_ids(
        first_row + jnp.arange(tile_count, dtype=jnp.int32) * tile_rows - 1, genome_lengths
    )

    def intra_block(inputs):
        block_in, own_segs = inputs
        same_genome = ((own_segs[:, None] == own_segs[None, :]) & long_band)[None]
        upper = jnp.where(same_genome, toeplitz_upper, jnp.zeros_like(toeplitz_upper))
        lower = jnp.where(same_genome, toeplitz_lower, jnp.zeros_like(toeplitz_lower))
        return jnp.einsum(
            "gts,gis->git", upper, block_in, preferred_element_type=jnp.float32
        ) + jnp.einsum("gts,gis->git", lower, block_in, preferred_element_type=jnp.float32)

    local_part = jnp.stack([intra_block((signal[j], tile_segs[j])) for j in range(tile_count)])
    end_keep = (tile_segs == tile_segs[:, -1:])[:, None, None, :]
    masked_signal = jnp.where(end_keep, signal, jnp.zeros_like(signal))
    states = jnp.einsum(
        "gsm,jgis->jgim", inward_upper, masked_signal, preferred_element_type=jnp.float32
    ) + jnp.einsum(
        "gsm,jgis->jgim", inward_lower, masked_signal, preferred_element_type=jnp.float32
    )
    carried = (tile_segs[:, -1] == before).astype(jnp.float32)

    def chain_link(carry_in, inputs):
        block_states, kept_flag = inputs
        step = (
            decay_re * kept_flag,
            decay_im * kept_flag,
            block_states[..., :mode_count],
            block_states[..., mode_count:],
        )
        return (complex_link(carry_in, step), carry_in)

    state_zero = jnp.zeros((group_count, GROUP, mode_count), jnp.float32)
    start_carry = (
        jnp.ones((group_count, mode_count), jnp.float32),
        jnp.zeros((group_count, mode_count), jnp.float32),
        state_zero,
        state_zero,
    )
    summary, entering = lax.scan(chain_link, start_carry, (states, carried))
    incoming = entering_2(
        (summary[0], summary[1], summary[2], summary[3]),
        "seq",
        complex_link,
        (start_carry[0], start_carry[1], start_carry[2], start_carry[3]),
    )
    incoming_re = incoming[2]
    incoming_im = incoming[3]
    reach_re = entering[0][:, :, None, :]
    reach_im = entering[1][:, :, None, :]
    full_re = entering[2] + reach_re * incoming_re - reach_im * incoming_im
    full_im = entering[3] + reach_re * incoming_im + reach_im * incoming_re
    keep_mask = (tile_segs == before[:, None]).astype(jnp.float32)
    carried_part = (
        jnp.einsum(
            "gtm,jgim->jgit",
            outward,
            jnp.concatenate((full_re, full_im), axis=3),
            precision=highest,
        )
        * keep_mask[:, None, None, :]
    )
    longconv = (
        local_part
        + carried_part
        + skip_gain.reshape(group_count, GROUP)[None, :, :, None] * signal.astype(jnp.float32)
    )
    long_cols = jnp.transpose(longconv, (1, 2, 0, 3)).reshape(chan_count, row_count)
    mixed = (query_proj.T.astype(jnp.float32) * long_cols).astype(jnp.bfloat16)
    mixed_wide = mixed.astype(jnp.float32)
    squares = lax.psum(jnp.sum(mixed_wide * mixed_wide, axis=0), ("chan", "rep"))
    normed = (mixed_wide * lax.rsqrt(squares / D + norm_eps)[None, :] * norm_gain[:, None]).astype(
        jnp.bfloat16
    )
    partial_value = channel_logits(normed, unembed)
    lanes = ("chan", "rep")
    lane_count = lax.axis_size(lanes)
    piece = row_count // lane_count
    piece_at = lax.axis_index(lanes) * piece
    logits = scatter_sum(partial_value, lanes)
    logprob_piece = log_probs(logits, lax.dynamic_slice_in_dim(token_ids, piece_at, piece, 0))
    logprob = lax.all_gather(logprob_piece, lanes, tiled=True)
    genome_index = jnp.arange(genome_lengths.shape[0], dtype=jnp.int32)
    genome_part = jnp.sum(
        jnp.where(
            segments[:, None] == genome_index[None, :],
            logprob[:, None],
            jnp.zeros((row_count, genome_lengths.shape[0]), jnp.float32),
        ),
        axis=0,
    )
    totals = sum_over(genome_part, "seq")
    return (logprob, totals / genome_lengths.astype(jnp.float32))


def solution(mesh):
    return jax.shard_map(
        per_device,
        mesh=mesh,
        in_specs=(
            P(("groups", "seq"), ("chan", "rep")),
            P(("groups", "seq"), ("chan", "rep")),
            P(("groups", "seq"), ("chan", "rep")),
            P(None, ("chan", "rep")),
            P(None, ("chan", "rep")),
            P(None, ("chan", "rep"), None),
            P(("chan", "rep")),
            P(("chan", "rep")),
            P(("chan", "rep"), None),
            P(("groups", "seq")),
            P("groups"),
        ),
        out_specs=(P(("groups", "seq")), P("groups")),
        check_vma=False,
    )
```

```python
import jax
import jax.numpy as jnp
from jax import lax
from jax.sharding import PartitionSpec as P

D = 8192
GROUP = 16


tile_rows = 128
short_margin = 8
norm_eps = 1e-05


def from_behind(shard, axis, by):
    count = lax.axis_size(axis)
    pairs = [(i, i + by) for i in range(count) if 0 <= i + by < count]
    return lax.ppermute(shard, axis, pairs)


def scatter_sum(part, axes):
    count = lax.axis_size(axes)
    if count & (count - 1):
        return lax.psum_scatter(part, axes, scatter_dimension=0, tiled=True)
    place = lax.axis_index(axes)
    bit = count // 2
    while bit >= 1:
        half = part.shape[0] // 2
        upper = (place & bit) != 0
        keep = jnp.where(upper, part[half:], part[:half])
        give = jnp.where(upper, part[:half], part[half:])
        part = keep + lax.ppermute(give, axes, [(i, i ^ bit) for i in range(count)])
        bit //= 2
    return part


def sum_over(part, axis):
    count = lax.axis_size(axis)
    if count & (count - 1):
        return lax.psum(part, axis)
    bit = 1
    while bit < count:
        part = part + lax.ppermute(part, axis, [(i, i ^ bit) for i in range(count)])
        bit *= 2
    return part


def entering_2(part, axis, combine, identity):
    place = lax.axis_index(axis)
    count = lax.axis_size(axis)
    lead = part[0].shape[0]
    widths = [a.size // lead for a in part]

    def pack(t):
        return jnp.concatenate([a.reshape(lead, -1) for a in t], axis=1)

    def unpack(flat):
        pieces = []
        offset = 0
        for a, width in zip(part, widths):
            pieces.append(flat[:, offset : offset + width].reshape(a.shape))
            offset += width
        return tuple(pieces)

    ident = tuple(jnp.zeros_like(a) + jnp.asarray(e, a.dtype) for a, e in zip(part, identity))
    before = ident
    upto = tuple(part)
    shift = 1
    while shift < count:
        arrived = unpack(from_behind(pack(upto), axis, shift))
        arrived = tuple(jnp.where(place >= shift, r, i) for r, i in zip(arrived, ident))
        before = combine(arrived, before)
        upto = combine(arrived, upto)
        shift *= 2
    return before


def segment_ids(positions, genome_lengths):
    starts = jnp.cumsum(genome_lengths) - genome_lengths
    at_or_past = (positions[:, None] >= starts[None, :]).astype(jnp.int32)
    return jnp.sum(at_or_past, axis=1) - 1


def short_filter(keys_in, values_in, seg_list, out_rows, short_taps):
    gated = keys_in.astype(jnp.float32) * values_in.astype(jnp.float32)
    total_rows = keys_in.shape[0]
    lead_rows = total_rows - out_rows
    own_segs = seg_list[lead_rows:]
    result = jnp.zeros((out_rows, keys_in.shape[1]), jnp.float32)
    for lag_index in range(short_taps.shape[0]):
        shifted = gated[lead_rows - lag_index : total_rows - lag_index]
        same_genome = (seg_list[lead_rows - lag_index : total_rows - lag_index] == own_segs).astype(
            jnp.float32
        )
        result = (
            result
            + short_taps[lag_index].astype(jnp.float32)[None, :] * shifted * same_genome[:, None]
        )
    return result.astype(jnp.bfloat16)


def circulants(table):
    lag_count, width = table.shape
    lag_ids = lax.optimization_barrier(jnp.arange(lag_count, dtype=jnp.int32))
    out_pos = jnp.arange(tile_rows, dtype=jnp.int32)[:, None]
    in_pos = jnp.arange(tile_rows, dtype=jnp.int32)[None, :]
    lag_grid = (out_pos - in_pos + tile_rows) % tile_rows
    one_hot = (lag_grid.reshape(1, tile_rows * tile_rows) == lag_ids[:, None]).astype(table.dtype)
    picked = jnp.dot(table.T, one_hot, preferred_element_type=jnp.float32)
    return picked.astype(table.dtype).reshape(width, tile_rows, tile_rows)


def modal_tables(modal_poles):
    decay_rate = modal_poles[0]
    angles = modal_poles[1]
    residue_re = modal_poles[2]
    residue_im = modal_poles[3]

    def pole_powers(exponents):
        magnitude = jnp.exp(-exponents * decay_rate[None])
        return (
            magnitude * jnp.cos(exponents * angles[None]),
            magnitude * jnp.sin(exponents * angles[None]),
        )

    power_re, power_im = pole_powers(jnp.arange(tile_rows).astype(jnp.float32)[:, None, None])
    last_re, last_im = pole_powers(jnp.full((1, 1, 1), tile_rows, jnp.float32))
    kernel_re = residue_re[None] * power_re - residue_im[None] * power_im
    kernel_im = residue_re[None] * power_im + residue_im[None] * power_re
    end_re = residue_re[None] * last_re - residue_im[None] * last_im
    end_im = residue_re[None] * last_im + residue_im[None] * last_re
    kernel = jnp.sum(kernel_re, axis=2)
    toeplitz = split_table(kernel)
    outward = jnp.transpose(
        jnp.concatenate(
            (
                jnp.concatenate((kernel_re[1:], end_re), axis=0),
                -jnp.concatenate((kernel_im[1:], end_im), axis=0),
            ),
            axis=2,
        ),
        (1, 0, 2),
    )
    inward = jnp.transpose(
        jnp.concatenate((power_re[tile_rows - 1 :: -1], power_im[tile_rows - 1 :: -1]), axis=2),
        (1, 0, 2),
    )
    return (toeplitz, outward, inward, last_re[0], last_im[0])


def split_table(table):
    upper = table.astype(jnp.bfloat16)
    lower = (table - upper.astype(jnp.float32)).astype(jnp.bfloat16)
    return (upper, lower)


def complex_link(earlier, later):
    early_are, early_aim, early_sre, early_sim = earlier
    late_are, late_aim, late_sre, late_sim = later
    lead_re = late_are[..., None, :]
    lead_im = late_aim[..., None, :]
    return (
        late_are * early_are - late_aim * early_aim,
        late_are * early_aim + late_aim * early_are,
        lead_re * early_sre - lead_im * early_sim + late_sre,
        lead_re * early_sim + lead_im * early_sre + late_sim,
    )


def log_probs(logits, targets):
    vocab_ids = jnp.arange(logits.shape[1], dtype=jnp.int32)
    picked = jnp.sum(
        jnp.where(targets[:, None] == vocab_ids[None, :], logits, jnp.zeros_like(logits)), axis=1
    )
    return picked - jnp.log(jnp.sum(jnp.exp(logits), axis=1))


def channel_logits(normed_cols, unembed):
    return lax.dot_general(
        normed_cols, unembed, (((0,), (0,)), ((), ())), preferred_element_type=jnp.float32
    )


def per_device(
    query_proj,
    key_proj,
    value_proj,
    short_taps,
    medium_taps,
    modal_poles,
    skip_gain,
    norm_gain,
    unembed,
    token_ids,
    genome_lengths,
):
    highest = lax.Precision.HIGHEST
    row_count, chan_count = query_proj.shape
    group_count = chan_count // GROUP
    mode_count = modal_poles.shape[2]
    tile_count = row_count // tile_rows
    first_row = lax.axis_index("seq") * row_count
    segments = segment_ids(first_row + jnp.arange(row_count, dtype=jnp.int32), genome_lengths)
    halo = tile_rows + short_margin
    edge_pair = from_behind(
        jnp.stack((key_proj[row_count - halo :], value_proj[row_count - halo :])),
        "seq",
        1,
    )
    ext_segs = segment_ids(
        first_row - halo + jnp.arange(row_count + halo, dtype=jnp.int32),
        genome_lengths,
    )
    filtered = short_filter(
        jnp.concatenate((edge_pair[0], key_proj)),
        jnp.concatenate((edge_pair[1], value_proj)),
        ext_segs,
        row_count + tile_rows,
        short_taps,
    )
    ext_short = filtered.T.reshape(group_count, GROUP, row_count + tile_rows)
    medium_segs = segment_ids(
        first_row - tile_rows + jnp.arange(row_count + tile_rows, dtype=jnp.int32), genome_lengths
    )

    long_toeplitz, outward, inward, decay_re, decay_im = modal_tables(modal_poles)
    circ = circulants(jnp.concatenate((medium_taps, long_toeplitz[0], long_toeplitz[1]), axis=1))
    circ_medium = jnp.concatenate((circ[:group_count], circ[:group_count]), axis=2)
    toeplitz_upper = circ[group_count : 2 * group_count]
    toeplitz_lower = circ[2 * group_count :]
    lag_band = (
        jnp.arange(tile_rows, dtype=jnp.int32)[:, None] + tile_rows
        - jnp.arange(2 * tile_rows, dtype=jnp.int32)[None, :]
    )
    medium_band = (lag_band >= 0) & (lag_band < medium_taps.shape[0])
    long_band = lag_band[:, tile_rows:] >= 0

    def medium_block(tile_index):
        start = tile_index * tile_rows
        window = lax.dynamic_slice_in_dim(ext_short, start, 2 * tile_rows, 2)
        window_segs = lax.dynamic_slice_in_dim(medium_segs, start, 2 * tile_rows, 0)
        own_segs = lax.dynamic_slice_in_dim(segments, start, tile_rows, 0)
        same_genome = (own_segs[:, None] == window_segs[None, :]) & medium_band
        matrix = jnp.where(same_genome[None], circ_medium, jnp.zeros_like(circ_medium))
        return jnp.einsum(
            "gts,gis->git", matrix, window, preferred_element_type=jnp.float32
        ).astype(jnp.bfloat16)

    signal = jnp.stack([medium_block(tile_index) for tile_index in range(tile_count)])
    inward_upper, inward_lower = split_table(inward)
    tile_segs = segments.reshape(tile_count, tile_rows)
    before = segment_ids(
        first_row + jnp.arange(tile_count, dtype=jnp.int32) * tile_rows - 1, genome_lengths
    )

    def intra_block(inputs):
        block_in, own_segs = inputs
        same_genome = ((own_segs[:, None] == own_segs[None, :]) & long_band)[None]
        upper = jnp.where(same_genome, toeplitz_upper, jnp.zeros_like(toeplitz_upper))
        lower = jnp.where(same_genome, toeplitz_lower, jnp.zeros_like(toeplitz_lower))
        return jnp.einsum(
            "gts,gis->git", upper, block_in, preferred_element_type=jnp.float32
        ) + jnp.einsum("gts,gis->git", lower, block_in, preferred_element_type=jnp.float32)

    local_part = jnp.stack([intra_block((signal[j], tile_segs[j])) for j in range(tile_count)])
    end_keep = (tile_segs == tile_segs[:, -1:])[:, None, None, :]
    masked_signal = jnp.where(end_keep, signal, jnp.zeros_like(signal))
    states = jnp.einsum(
        "gsm,jgis->jgim", inward_upper, masked_signal, preferred_element_type=jnp.float32
    ) + jnp.einsum(
        "gsm,jgis->jgim", inward_lower, masked_signal, preferred_element_type=jnp.float32
    )
    carried = (tile_segs[:, -1] == before).astype(jnp.float32)

    def chain_link(carry_in, inputs):
        block_states, kept_flag = inputs
        step = (
            decay_re * kept_flag,
            decay_im * kept_flag,
            block_states[..., :mode_count],
            block_states[..., mode_count:],
        )
        return (complex_link(carry_in, step), carry_in)

    state_zero = jnp.zeros((group_count, GROUP, mode_count), jnp.float32)
    start_carry = (
        jnp.ones((group_count, mode_count), jnp.float32),
        jnp.zeros((group_count, mode_count), jnp.float32),
        state_zero,
        state_zero,
    )
    summary, entering = lax.scan(chain_link, start_carry, (states, carried))
    incoming = entering_2(
        (summary[0], summary[1], summary[2], summary[3]),
        "seq",
        complex_link,
        (start_carry[0], start_carry[1], start_carry[2], start_carry[3]),
    )
    incoming_re = incoming[2]
    incoming_im = incoming[3]
    reach_re = entering[0][:, :, None, :]
    reach_im = entering[1][:, :, None, :]
    full_re = entering[2] + reach_re * incoming_re - reach_im * incoming_im
    full_im = entering[3] + reach_re * incoming_im + reach_im * incoming_re
    keep_mask = (tile_segs == before[:, None]).astype(jnp.float32)
    carried_part = (
        jnp.einsum(
            "gtm,jgim->jgit",
            outward,
            jnp.concatenate((full_re, full_im), axis=3),
            precision=highest,
        )
        * keep_mask[:, None, None, :]
    )
    longconv = (
        local_part
        + carried_part
        + skip_gain.reshape(group_count, GROUP)[None, :, :, None] * signal.astype(jnp.float32)
    )
    long_cols = jnp.transpose(longconv, (1, 2, 0, 3)).reshape(chan_count, row_count)
    mixed = (query_proj.T.astype(jnp.float32) * long_cols).astype(jnp.bfloat16)
    mixed_wide = mixed.astype(jnp.float32)
    squares = lax.psum(jnp.sum(mixed_wide * mixed_wide, axis=0), ("chan", "rep"))
    normed = (mixed_wide * lax.rsqrt(squares / D + norm_eps)[None, :] * norm_gain[:, None]).astype(
        jnp.bfloat16
    )
    partial_value = channel_logits(normed, unembed)
    lanes = ("chan", "rep")
    lane_count = lax.axis_size(lanes)
    piece = row_count // lane_count
    piece_at = lax.axis_index(lanes) * piece
    logits = scatter_sum(partial_value, lanes)
    logprob_piece = log_probs(logits, lax.dynamic_slice_in_dim(token_ids, piece_at, piece, 0))
    logprob = lax.all_gather(logprob_piece, lanes, tiled=True)
    genome_index = jnp.arange(genome_lengths.shape[0], dtype=jnp.int32)
    genome_part = jnp.sum(
        jnp.where(
            segments[:, None] == genome_index[None, :],
            logprob[:, None],
            jnp.zeros((row_count, genome_lengths.shape[0]), jnp.float32),
        ),
        axis=0,
    )
    totals = sum_over(genome_part, "seq")
    return (logprob, totals / genome_lengths.astype(jnp.float32))


def solution(mesh):
    return jax.shard_map(
        per_device,
        mesh=mesh,
        in_specs=(
            P(("groups", "seq"), ("chan", "rep")),
            P(("groups", "seq"), ("chan", "rep")),
            P(("groups", "seq"), ("chan", "rep")),
            P(None, ("chan", "rep")),
            P(None, ("chan", "rep")),
            P(None, ("chan", "rep"), None),
            P(("chan", "rep")),
            P(("chan", "rep")),
            P(("chan", "rep"), None),
            P(("groups", "seq")),
            P("groups"),
        ),
        out_specs=(P(("groups", "seq")), P("groups")),
        check_vma=False,
    )
```

```python
import jax
import jax.numpy as jnp
from jax import lax
from jax.sharding import PartitionSpec as P

D = 8192
GROUP = 16


tile_rows = 128
short_margin = 8
norm_eps = 1e-05


def from_behind(shard, axis, by):
    count = lax.axis_size(axis)
    pairs = [(i, i + by) for i in range(count) if 0 <= i + by < count]
    return lax.ppermute(shard, axis, pairs)


def scatter_sum(part, axes):
    count = lax.axis_size(axes)
    place = lax.axis_index(axes)
    bit = 1
    piece_index = 0
    while bit < count:
        half = part.shape[0] // 2
        upper = (place & bit) != 0
        keep = jnp.where(upper, part[half:], part[:half])
        give = jnp.where(upper, part[:half], part[half:])
        part = keep + lax.ppermute(give, axes, [(i, i ^ bit) for i in range(count)])
        piece_index = piece_index * 2 + upper.astype(jnp.int32)
        bit *= 2
    return part, piece_index


def sum_over(part, axis):
    count = lax.axis_size(axis)
    if count & (count - 1):
        return lax.psum(part, axis)
    bit = 1
    while bit < count:
        part = part + lax.ppermute(part, axis, [(i, i ^ bit) for i in range(count)])
        bit *= 2
    return part


def entering_2(part, axis, combine, identity):
    place = lax.axis_index(axis)
    count = lax.axis_size(axis)
    lead = part[0].shape[0]
    widths = [a.size // lead for a in part]

    def pack(t):
        return jnp.concatenate([a.reshape(lead, -1) for a in t], axis=1)

    def unpack(flat):
        pieces = []
        offset = 0
        for a, width in zip(part, widths):
            pieces.append(flat[:, offset : offset + width].reshape(a.shape))
            offset += width
        return tuple(pieces)

    ident = tuple(jnp.zeros_like(a) + jnp.asarray(e, a.dtype) for a, e in zip(part, identity))
    before = ident
    upto = tuple(part)
    shift = 1
    while shift < count:
        arrived = unpack(from_behind(pack(upto), axis, shift))
        arrived = tuple(jnp.where(place >= shift, r, i) for r, i in zip(arrived, ident))
        before = combine(arrived, before)
        upto = combine(arrived, upto)
        shift *= 2
    return before


def segment_ids(positions, genome_lengths):
    starts = jnp.cumsum(genome_lengths) - genome_lengths
    at_or_past = (positions[:, None] >= starts[None, :]).astype(jnp.int32)
    return jnp.sum(at_or_past, axis=1) - 1


def short_filter(keys_in, values_in, seg_list, out_rows, short_taps):
    gated = keys_in.astype(jnp.float32) * values_in.astype(jnp.float32)
    total_rows = keys_in.shape[0]
    lead_rows = total_rows - out_rows
    own_segs = seg_list[lead_rows:]
    result = jnp.zeros((out_rows, keys_in.shape[1]), jnp.float32)
    for lag_index in range(short_taps.shape[0]):
        shifted = gated[lead_rows - lag_index : total_rows - lag_index]
        same_genome = (seg_list[lead_rows - lag_index : total_rows - lag_index] == own_segs).astype(
            jnp.float32
        )
        result = (
            result
            + short_taps[lag_index].astype(jnp.float32)[None, :] * shifted * same_genome[:, None]
        )
    return result.astype(jnp.bfloat16)


def circulants(table):
    lag_count, width = table.shape
    lag_ids = lax.optimization_barrier(jnp.arange(lag_count, dtype=jnp.int32))
    out_pos = jnp.arange(tile_rows, dtype=jnp.int32)[:, None]
    in_pos = jnp.arange(tile_rows, dtype=jnp.int32)[None, :]
    lag_grid = (out_pos - in_pos + tile_rows) % tile_rows
    one_hot = (lag_grid.reshape(1, tile_rows * tile_rows) == lag_ids[:, None]).astype(table.dtype)
    picked = jnp.dot(table.T, one_hot, preferred_element_type=jnp.float32)
    return picked.astype(table.dtype).reshape(width, tile_rows, tile_rows)


def modal_tables(modal_poles):
    decay_rate = modal_poles[0]
    angles = modal_poles[1]
    residue_re = modal_poles[2]
    residue_im = modal_poles[3]
    powers = jnp.arange(tile_rows + 1).astype(jnp.float32)[:, None, None]
    magnitude = jnp.exp(-powers * decay_rate[None])
    power_re = magnitude * jnp.cos(powers * angles[None])
    power_im = magnitude * jnp.sin(powers * angles[None])
    kernel_re = residue_re[None] * power_re - residue_im[None] * power_im
    kernel_im = residue_re[None] * power_im + residue_im[None] * power_re
    kernel = jnp.sum(kernel_re[:tile_rows], axis=2)
    toeplitz = split_table(kernel)
    outward = jnp.transpose(jnp.concatenate((kernel_re[1:], -kernel_im[1:]), axis=2), (1, 0, 2))
    inward = jnp.transpose(
        jnp.concatenate((power_re[tile_rows - 1 :: -1], power_im[tile_rows - 1 :: -1]), axis=2),
        (1, 0, 2),
    )
    return (toeplitz, outward, inward, power_re[tile_rows], power_im[tile_rows])


def split_table(table):
    upper = table.astype(jnp.bfloat16)
    lower = (table - upper.astype(jnp.float32)).astype(jnp.bfloat16)
    return (upper, lower)


def complex_link(earlier, later):
    early_are, early_aim, early_sre, early_sim = earlier
    late_are, late_aim, late_sre, late_sim = later
    lead_re = late_are[..., None, :]
    lead_im = late_aim[..., None, :]
    return (
        late_are * early_are - late_aim * early_aim,
        late_are * early_aim + late_aim * early_are,
        lead_re * early_sre - lead_im * early_sim + late_sre,
        lead_re * early_sim + lead_im * early_sre + late_sim,
    )


def log_probs(logits, targets):
    vocab_ids = jnp.arange(logits.shape[1], dtype=jnp.int32)
    picked = jnp.sum(
        jnp.where(targets[:, None] == vocab_ids[None, :], logits, jnp.zeros_like(logits)), axis=1
    )
    return picked - jnp.log(jnp.sum(jnp.exp(logits), axis=1))


def channel_logits(normed_cols, unembed):
    return lax.dot_general(
        normed_cols, unembed, (((0,), (0,)), ((), ())), preferred_element_type=jnp.float32
    )


def per_device(
    query_proj,
    key_proj,
    value_proj,
    short_taps,
    medium_taps,
    modal_poles,
    skip_gain,
    norm_gain,
    unembed,
    token_ids,
    genome_lengths,
):
    highest = lax.Precision.HIGHEST
    row_count, chan_count = query_proj.shape
    group_count = chan_count // GROUP
    mode_count = modal_poles.shape[2]
    tile_count = row_count // tile_rows
    first_row = lax.axis_index("seq") * row_count
    segments = segment_ids(first_row + jnp.arange(row_count, dtype=jnp.int32), genome_lengths)
    halo = tile_rows + short_margin
    edge_pair = from_behind(
        jnp.stack((key_proj[row_count - halo :], value_proj[row_count - halo :])),
        "seq",
        1,
    )
    ext_segs = segment_ids(
        first_row - halo + jnp.arange(row_count + halo, dtype=jnp.int32),
        genome_lengths,
    )
    filtered = short_filter(
        jnp.concatenate((edge_pair[0], key_proj)),
        jnp.concatenate((edge_pair[1], value_proj)),
        ext_segs,
        row_count + tile_rows,
        short_taps,
    )
    ext_short = filtered.T.reshape(group_count, GROUP, row_count + tile_rows)
    medium_segs = segment_ids(
        first_row - tile_rows + jnp.arange(row_count + tile_rows, dtype=jnp.int32), genome_lengths
    )

    long_toeplitz, outward, inward, decay_re, decay_im = modal_tables(modal_poles)
    circ = circulants(jnp.concatenate((medium_taps, long_toeplitz[0], long_toeplitz[1]), axis=1))
    circ_medium = jnp.concatenate((circ[:group_count], circ[:group_count]), axis=2)
    toeplitz_upper = circ[group_count : 2 * group_count]
    toeplitz_lower = circ[2 * group_count :]
    lag_band = (
        jnp.arange(tile_rows, dtype=jnp.int32)[:, None] + tile_rows
        - jnp.arange(2 * tile_rows, dtype=jnp.int32)[None, :]
    )
    medium_band = (lag_band >= 0) & (lag_band < medium_taps.shape[0])
    long_band = lag_band[:, tile_rows:] >= 0

    def medium_block(tile_index):
        start = tile_index * tile_rows
        window = lax.dynamic_slice_in_dim(ext_short, start, 2 * tile_rows, 2)
        window_segs = lax.dynamic_slice_in_dim(medium_segs, start, 2 * tile_rows, 0)
        own_segs = lax.dynamic_slice_in_dim(segments, start, tile_rows, 0)
        same_genome = (own_segs[:, None] == window_segs[None, :]) & medium_band
        matrix = jnp.where(same_genome[None], circ_medium, jnp.zeros_like(circ_medium))
        return jnp.einsum(
            "gts,gis->git", matrix, window, preferred_element_type=jnp.float32
        ).astype(jnp.bfloat16)

    signal = jnp.stack([medium_block(tile_index) for tile_index in range(tile_count)])
    inward_upper, inward_lower = split_table(inward)
    tile_segs = segments.reshape(tile_count, tile_rows)
    before = segment_ids(
        first_row + jnp.arange(tile_count, dtype=jnp.int32) * tile_rows - 1, genome_lengths
    )

    def intra_block(inputs):
        block_in, own_segs = inputs
        same_genome = ((own_segs[:, None] == own_segs[None, :]) & long_band)[None]
        upper = jnp.where(same_genome, toeplitz_upper, jnp.zeros_like(toeplitz_upper))
        lower = jnp.where(same_genome, toeplitz_lower, jnp.zeros_like(toeplitz_lower))
        return jnp.einsum(
            "gts,gis->git", upper, block_in, preferred_element_type=jnp.float32
        ) + jnp.einsum("gts,gis->git", lower, block_in, preferred_element_type=jnp.float32)

    local_part = jnp.stack([intra_block((signal[j], tile_segs[j])) for j in range(tile_count)])
    end_keep = (tile_segs == tile_segs[:, -1:])[:, None, None, :]
    masked_signal = jnp.where(end_keep, signal, jnp.zeros_like(signal))
    states = jnp.einsum(
        "gsm,jgis->jgim", inward_upper, masked_signal, preferred_element_type=jnp.float32
    ) + jnp.einsum(
        "gsm,jgis->jgim", inward_lower, masked_signal, preferred_element_type=jnp.float32
    )
    carried = (tile_segs[:, -1] == before).astype(jnp.float32)

    def chain_link(carry_in, inputs):
        block_states, kept_flag = inputs
        step = (
            decay_re * kept_flag,
            decay_im * kept_flag,
            block_states[..., :mode_count],
            block_states[..., mode_count:],
        )
        return (complex_link(carry_in, step), carry_in)

    state_zero = jnp.zeros((group_count, GROUP, mode_count), jnp.float32)
    start_carry = (
        jnp.ones((group_count, mode_count), jnp.float32),
        jnp.zeros((group_count, mode_count), jnp.float32),
        state_zero,
        state_zero,
    )
    summary, entering = lax.scan(chain_link, start_carry, (states, carried))
    incoming = entering_2(
        (summary[0], summary[1], summary[2], summary[3]),
        "seq",
        complex_link,
        (start_carry[0], start_carry[1], start_carry[2], start_carry[3]),
    )
    incoming_re = incoming[2]
    incoming_im = incoming[3]
    reach_re = entering[0][:, :, None, :]
    reach_im = entering[1][:, :, None, :]
    full_re = entering[2] + reach_re * incoming_re - reach_im * incoming_im
    full_im = entering[3] + reach_re * incoming_im + reach_im * incoming_re
    keep_mask = (tile_segs == before[:, None]).astype(jnp.float32)
    carried_part = (
        jnp.einsum(
            "gtm,jgim->jgit",
            outward,
            jnp.concatenate((full_re, full_im), axis=3),
            precision=highest,
        )
        * keep_mask[:, None, None, :]
    )
    longconv = (
        local_part
        + carried_part
        + skip_gain.reshape(group_count, GROUP)[None, :, :, None] * signal.astype(jnp.float32)
    )
    long_cols = jnp.transpose(longconv, (1, 2, 0, 3)).reshape(chan_count, row_count)
    mixed = (query_proj.T.astype(jnp.float32) * long_cols).astype(jnp.bfloat16)
    mixed_wide = mixed.astype(jnp.float32)
    squares = sum_over(jnp.sum(mixed_wide * mixed_wide, axis=0), ("chan", "rep"))
    normed = (mixed_wide * lax.rsqrt(squares / D + norm_eps)[None, :] * norm_gain[:, None]).astype(
        jnp.bfloat16
    )
    partial_value = channel_logits(normed, unembed)
    lanes = ("chan", "rep")
    lane_count = lax.axis_size(lanes)
    piece = row_count // lane_count
    logits, piece_index = scatter_sum(partial_value, lanes)
    piece_at = piece_index * piece
    logprob_piece = log_probs(logits, lax.dynamic_slice_in_dim(token_ids, piece_at, piece, 0))
    logprob = sum_over(
        lax.dynamic_update_slice_in_dim(
            jnp.zeros((row_count,), jnp.float32), logprob_piece, piece_at, 0
        ),
        lanes,
    )
    genome_index = jnp.arange(genome_lengths.shape[0], dtype=jnp.int32)
    genome_part = jnp.sum(
        jnp.where(
            segments[:, None] == genome_index[None, :],
            logprob[:, None],
            jnp.zeros((row_count, genome_lengths.shape[0]), jnp.float32),
        ),
        axis=0,
    )
    totals = sum_over(genome_part, "seq")
    return (logprob, totals / genome_lengths.astype(jnp.float32))


def solution(mesh):
    return jax.shard_map(
        per_device,
        mesh=mesh,
        in_specs=(
            P(("groups", "seq"), ("chan", "rep")),
            P(("groups", "seq"), ("chan", "rep")),
            P(("groups", "seq"), ("chan", "rep")),
            P(None, ("chan", "rep")),
            P(None, ("chan", "rep")),
            P(None, ("chan", "rep"), None),
            P(("chan", "rep")),
            P(("chan", "rep")),
            P(("chan", "rep"), None),
            P(("groups", "seq")),
            P("groups"),
        ),
        out_specs=(P(("groups", "seq")), P("groups")),
        check_vma=False,
    )
```

```python
import jax
import jax.numpy as jnp
from jax import lax
from jax.sharding import PartitionSpec as P

D = 8192
GROUP = 16


tile_rows = 128
short_margin = 8
norm_eps = 1e-05


def from_behind(shard, axis, by):
    count = lax.axis_size(axis)
    pairs = [(i, i + by) for i in range(count) if 0 <= i + by < count]
    return lax.ppermute(shard, axis, pairs)


def scatter_sum(part, axes):
    count = lax.axis_size(axes)
    place = lax.axis_index(axes)
    bit = 1
    piece_index = 0
    while bit < count:
        half = part.shape[0] // 2
        upper = (place & bit) != 0
        keep = jnp.where(upper, part[half:], part[:half])
        give = jnp.where(upper, part[:half], part[half:])
        part = keep + lax.ppermute(give, axes, [(i, i ^ bit) for i in range(count)])
        piece_index = piece_index * 2 + upper.astype(jnp.int32)
        bit *= 2
    return part, piece_index


def sum_over(part, axis):
    count = lax.axis_size(axis)
    if count & (count - 1):
        return lax.psum(part, axis)
    bit = 1
    while bit < count:
        part = part + lax.ppermute(part, axis, [(i, i ^ bit) for i in range(count)])
        bit *= 2
    return part


def entering_2(part, axis, combine, identity):
    place = lax.axis_index(axis)
    count = lax.axis_size(axis)
    lead = part[0].shape[0]
    widths = [a.size // lead for a in part]

    def pack(t):
        return jnp.concatenate([a.reshape(lead, -1) for a in t], axis=1)

    def unpack(flat):
        pieces = []
        offset = 0
        for a, width in zip(part, widths):
            pieces.append(flat[:, offset : offset + width].reshape(a.shape))
            offset += width
        return tuple(pieces)

    ident = tuple(jnp.zeros_like(a) + jnp.asarray(e, a.dtype) for a, e in zip(part, identity))
    before = ident
    upto = tuple(part)
    shift = 1
    while shift < count:
        arrived = unpack(from_behind(pack(upto), axis, shift))
        arrived = tuple(jnp.where(place >= shift, r, i) for r, i in zip(arrived, ident))
        before = combine(arrived, before)
        upto = combine(arrived, upto)
        shift *= 2
    return before


def segment_ids(positions, genome_lengths):
    starts = jnp.cumsum(genome_lengths) - genome_lengths
    at_or_past = (positions[:, None] >= starts[None, :]).astype(jnp.int32)
    return jnp.sum(at_or_past, axis=1) - 1


def short_filter(keys_in, values_in, seg_list, out_rows, short_taps):
    gated = keys_in.astype(jnp.float32) * values_in.astype(jnp.float32)
    total_rows = keys_in.shape[0]
    lead_rows = total_rows - out_rows
    own_segs = seg_list[lead_rows:]
    result = jnp.zeros((out_rows, keys_in.shape[1]), jnp.float32)
    for lag_index in range(short_taps.shape[0]):
        shifted = gated[lead_rows - lag_index : total_rows - lag_index]
        same_genome = (seg_list[lead_rows - lag_index : total_rows - lag_index] == own_segs).astype(
            jnp.float32
        )
        result = (
            result
            + short_taps[lag_index].astype(jnp.float32)[None, :] * shifted * same_genome[:, None]
        )
    return result.astype(jnp.bfloat16)


def circulants(table):
    lag_count, width = table.shape
    lag_ids = lax.optimization_barrier(jnp.arange(lag_count, dtype=jnp.int32))
    out_pos = jnp.arange(tile_rows, dtype=jnp.int32)[:, None]
    in_pos = jnp.arange(tile_rows, dtype=jnp.int32)[None, :]
    lag_grid = (out_pos - in_pos + tile_rows) % tile_rows
    one_hot = (lag_grid.reshape(1, tile_rows * tile_rows) == lag_ids[:, None]).astype(table.dtype)
    picked = jnp.dot(table.T, one_hot, preferred_element_type=jnp.float32)
    return picked.astype(table.dtype).reshape(width, tile_rows, tile_rows)


def modal_tables(modal_poles):
    decay_rate = modal_poles[0]
    angles = modal_poles[1]
    residue_re = modal_poles[2]
    residue_im = modal_poles[3]
    powers = jnp.arange(tile_rows + 1).astype(jnp.float32)[:, None, None]
    magnitude = jnp.exp(-powers * decay_rate[None])
    power_re = magnitude * jnp.cos(powers * angles[None])
    power_im = magnitude * jnp.sin(powers * angles[None])
    kernel_re = residue_re[None] * power_re - residue_im[None] * power_im
    kernel_im = residue_re[None] * power_im + residue_im[None] * power_re
    kernel = jnp.sum(kernel_re[:tile_rows], axis=2)
    toeplitz = split_table(kernel)
    outward = jnp.transpose(jnp.concatenate((kernel_re[1:], -kernel_im[1:]), axis=2), (1, 0, 2))
    inward = jnp.transpose(
        jnp.concatenate((power_re[tile_rows - 1 :: -1], power_im[tile_rows - 1 :: -1]), axis=2),
        (1, 0, 2),
    )
    return (toeplitz, outward, inward, power_re[tile_rows], power_im[tile_rows])


def split_table(table):
    upper = table.astype(jnp.bfloat16)
    lower = (table - upper.astype(jnp.float32)).astype(jnp.bfloat16)
    return (upper, lower)


def complex_link(earlier, later):
    early_are, early_aim, early_sre, early_sim = earlier
    late_are, late_aim, late_sre, late_sim = later
    lead_re = late_are[..., None, :]
    lead_im = late_aim[..., None, :]
    return (
        late_are * early_are - late_aim * early_aim,
        late_are * early_aim + late_aim * early_are,
        lead_re * early_sre - lead_im * early_sim + late_sre,
        lead_re * early_sim + lead_im * early_sre + late_sim,
    )


def log_probs(logits, targets):
    vocab_ids = jnp.arange(logits.shape[1], dtype=jnp.int32)
    picked = jnp.sum(
        jnp.where(targets[:, None] == vocab_ids[None, :], logits, jnp.zeros_like(logits)), axis=1
    )
    return picked - jnp.log(jnp.sum(jnp.exp(logits), axis=1))


def channel_logits(normed_cols, unembed):
    return lax.dot_general(
        normed_cols, unembed, (((0,), (0,)), ((), ())), preferred_element_type=jnp.float32
    )


def per_device(
    query_proj,
    key_proj,
    value_proj,
    short_taps,
    medium_taps,
    modal_poles,
    skip_gain,
    norm_gain,
    unembed,
    token_ids,
    genome_lengths,
):
    highest = lax.Precision.HIGHEST
    row_count, chan_count = query_proj.shape
    group_count = chan_count // GROUP
    mode_count = modal_poles.shape[2]
    tile_count = row_count // tile_rows
    first_row = lax.axis_index("seq") * row_count
    segments = segment_ids(first_row + jnp.arange(row_count, dtype=jnp.int32), genome_lengths)
    halo = tile_rows + short_margin
    edge_pair = from_behind(
        jnp.stack((key_proj[row_count - halo :], value_proj[row_count - halo :])),
        "seq",
        1,
    )
    ext_segs = segment_ids(
        first_row - halo + jnp.arange(row_count + halo, dtype=jnp.int32),
        genome_lengths,
    )
    filtered = short_filter(
        jnp.concatenate((edge_pair[0], key_proj)),
        jnp.concatenate((edge_pair[1], value_proj)),
        ext_segs,
        row_count + tile_rows,
        short_taps,
    )
    ext_short = filtered.T.reshape(group_count, GROUP, row_count + tile_rows)
    medium_segs = segment_ids(
        first_row - tile_rows + jnp.arange(row_count + tile_rows, dtype=jnp.int32), genome_lengths
    )

    long_toeplitz, outward, inward, decay_re, decay_im = modal_tables(modal_poles)
    circ = circulants(jnp.concatenate((medium_taps, long_toeplitz[0], long_toeplitz[1]), axis=1))
    circ_medium = circ[:group_count]
    toeplitz_upper = circ[group_count : 2 * group_count]
    toeplitz_lower = circ[2 * group_count :]
    lag_band = (
        jnp.arange(tile_rows, dtype=jnp.int32)[:, None] + tile_rows
        - jnp.arange(2 * tile_rows, dtype=jnp.int32)[None, :]
    )
    medium_band = (lag_band >= 0) & (lag_band < medium_taps.shape[0])
    long_band = lag_band[:, tile_rows:] >= 0

    def medium_block(tile_index):
        start = tile_index * tile_rows
        window = lax.dynamic_slice_in_dim(ext_short, start, 2 * tile_rows, 2)
        window_segs = lax.dynamic_slice_in_dim(medium_segs, start, 2 * tile_rows, 0)
        own_segs = lax.dynamic_slice_in_dim(segments, start, tile_rows, 0)
        same_genome = (own_segs[:, None] == window_segs[None, :]) & medium_band
        halves = same_genome.reshape(tile_rows, 2, tile_rows).transpose(1, 0, 2)
        matrix = jnp.where(halves[:, None], circ_medium[None], jnp.zeros_like(circ_medium)[None])
        window2 = window.reshape(group_count, GROUP, 2, tile_rows)
        return jnp.einsum(
            "hgts,gihs->git", matrix, window2, preferred_element_type=jnp.float32
        ).astype(jnp.bfloat16)

    signal = jnp.stack([medium_block(tile_index) for tile_index in range(tile_count)])
    inward_upper, inward_lower = split_table(inward)
    tile_segs = segments.reshape(tile_count, tile_rows)
    before = segment_ids(
        first_row + jnp.arange(tile_count, dtype=jnp.int32) * tile_rows - 1, genome_lengths
    )

    def intra_block(inputs):
        block_in, own_segs = inputs
        same_genome = ((own_segs[:, None] == own_segs[None, :]) & long_band)[None]
        upper = jnp.where(same_genome, toeplitz_upper, jnp.zeros_like(toeplitz_upper))
        lower = jnp.where(same_genome, toeplitz_lower, jnp.zeros_like(toeplitz_lower))
        return jnp.einsum(
            "gts,gis->git", upper, block_in, preferred_element_type=jnp.float32
        ) + jnp.einsum("gts,gis->git", lower, block_in, preferred_element_type=jnp.float32)

    local_part = jnp.stack([intra_block((signal[j], tile_segs[j])) for j in range(tile_count)])
    end_keep = (tile_segs == tile_segs[:, -1:])[:, None, None, :]
    masked_signal = jnp.where(end_keep, signal, jnp.zeros_like(signal))
    states = jnp.einsum(
        "gsm,jgis->jgim", inward_upper, masked_signal, preferred_element_type=jnp.float32
    ) + jnp.einsum(
        "gsm,jgis->jgim", inward_lower, masked_signal, preferred_element_type=jnp.float32
    )
    carried = (tile_segs[:, -1] == before).astype(jnp.float32)

    def chain_link(carry_in, inputs):
        block_states, kept_flag = inputs
        step = (
            decay_re * kept_flag,
            decay_im * kept_flag,
            block_states[..., :mode_count],
            block_states[..., mode_count:],
        )
        return (complex_link(carry_in, step), carry_in)

    state_zero = jnp.zeros((group_count, GROUP, mode_count), jnp.float32)
    start_carry = (
        jnp.ones((group_count, mode_count), jnp.float32),
        jnp.zeros((group_count, mode_count), jnp.float32),
        state_zero,
        state_zero,
    )
    summary, entering = lax.scan(chain_link, start_carry, (states, carried))
    incoming = entering_2(
        (summary[0], summary[1], summary[2], summary[3]),
        "seq",
        complex_link,
        (start_carry[0], start_carry[1], start_carry[2], start_carry[3]),
    )
    incoming_re = incoming[2]
    incoming_im = incoming[3]
    reach_re = entering[0][:, :, None, :]
    reach_im = entering[1][:, :, None, :]
    full_re = entering[2] + reach_re * incoming_re - reach_im * incoming_im
    full_im = entering[3] + reach_re * incoming_im + reach_im * incoming_re
    keep_mask = (tile_segs == before[:, None]).astype(jnp.float32)
    carried_part = (
        jnp.einsum(
            "gtm,jgim->jgit",
            outward,
            jnp.concatenate((full_re, full_im), axis=3),
            precision=highest,
        )
        * keep_mask[:, None, None, :]
    )
    longconv = (
        local_part
        + carried_part
        + skip_gain.reshape(group_count, GROUP)[None, :, :, None] * signal.astype(jnp.float32)
    )
    long_cols = jnp.transpose(longconv, (1, 2, 0, 3)).reshape(chan_count, row_count)
    mixed = (query_proj.T.astype(jnp.float32) * long_cols).astype(jnp.bfloat16)
    mixed_wide = mixed.astype(jnp.float32)
    squares = sum_over(jnp.sum(mixed_wide * mixed_wide, axis=0), ("chan", "rep"))
    normed = (mixed_wide * lax.rsqrt(squares / D + norm_eps)[None, :] * norm_gain[:, None]).astype(
        jnp.bfloat16
    )
    partial_value = channel_logits(normed, unembed)
    lanes = ("chan", "rep")
    lane_count = lax.axis_size(lanes)
    piece = row_count // lane_count
    logits, piece_index = scatter_sum(partial_value, lanes)
    piece_at = piece_index * piece
    logprob_piece = log_probs(logits, lax.dynamic_slice_in_dim(token_ids, piece_at, piece, 0))
    logprob = sum_over(
        lax.dynamic_update_slice_in_dim(
            jnp.zeros((row_count,), jnp.float32), logprob_piece, piece_at, 0
        ),
        lanes,
    )
    genome_index = jnp.arange(genome_lengths.shape[0], dtype=jnp.int32)
    genome_part = jnp.sum(
        jnp.where(
            segments[:, None] == genome_index[None, :],
            logprob[:, None],
            jnp.zeros((row_count, genome_lengths.shape[0]), jnp.float32),
        ),
        axis=0,
    )
    totals = sum_over(genome_part, "seq")
    return (logprob, totals / genome_lengths.astype(jnp.float32))


def solution(mesh):
    return jax.shard_map(
        per_device,
        mesh=mesh,
        in_specs=(
            P(("groups", "seq"), ("chan", "rep")),
            P(("groups", "seq"), ("chan", "rep")),
            P(("groups", "seq"), ("chan", "rep")),
            P(None, ("chan", "rep")),
            P(None, ("chan", "rep")),
            P(None, ("chan", "rep"), None),
            P(("chan", "rep")),
            P(("chan", "rep")),
            P(("chan", "rep"), None),
            P(("groups", "seq")),
            P("groups"),
        ),
        out_specs=(P(("groups", "seq")), P("groups")),
        check_vma=False,
    )
```

```python
import jax
import jax.numpy as jnp
from jax import lax
from jax.sharding import PartitionSpec as P

D = 8192
GROUP = 16


tile_rows = 128
short_margin = 8
norm_eps = 1e-05


def from_behind(shard, axis, by):
    count = lax.axis_size(axis)
    pairs = [(i, i + by) for i in range(count) if 0 <= i + by < count]
    return lax.ppermute(shard, axis, pairs)


def scatter_sum(part, axes):
    count = lax.axis_size(axes)
    place = lax.axis_index(axes)
    bit = 1
    piece_index = 0
    while bit < count:
        half = part.shape[0] // 2
        upper = (place & bit) != 0
        keep = jnp.where(upper, part[half:], part[:half])
        give = jnp.where(upper, part[:half], part[half:])
        part = keep + lax.ppermute(give, axes, [(i, i ^ bit) for i in range(count)])
        piece_index = piece_index * 2 + upper.astype(jnp.int32)
        bit *= 2
    return part, piece_index


def sum_over(part, axis):
    count = lax.axis_size(axis)
    if count & (count - 1):
        return lax.psum(part, axis)
    bit = 1
    while bit < count:
        part = part + lax.ppermute(part, axis, [(i, i ^ bit) for i in range(count)])
        bit *= 2
    return part


def entering_2(part, axis, combine, identity):
    place = lax.axis_index(axis)
    count = lax.axis_size(axis)
    lead = part[0].shape[0]
    widths = [a.size // lead for a in part]

    def pack(t):
        return jnp.concatenate([a.reshape(lead, -1) for a in t], axis=1)

    def unpack(flat):
        pieces = []
        offset = 0
        for a, width in zip(part, widths):
            pieces.append(flat[:, offset : offset + width].reshape(a.shape))
            offset += width
        return tuple(pieces)

    ident = tuple(jnp.zeros_like(a) + jnp.asarray(e, a.dtype) for a, e in zip(part, identity))
    before = ident
    upto = tuple(part)
    shift = 1
    while shift < count:
        arrived = unpack(from_behind(pack(upto), axis, shift))
        arrived = tuple(jnp.where(place >= shift, r, i) for r, i in zip(arrived, ident))
        before = combine(arrived, before)
        upto = combine(arrived, upto)
        shift *= 2
    return before


def segment_ids(positions, genome_lengths):
    starts = jnp.cumsum(genome_lengths) - genome_lengths
    at_or_past = (positions[:, None] >= starts[None, :]).astype(jnp.int32)
    return jnp.sum(at_or_past, axis=1) - 1


def short_filter(keys_in, values_in, seg_list, out_rows, short_taps):
    gated = keys_in.astype(jnp.float32) * values_in.astype(jnp.float32)
    total_rows = keys_in.shape[0]
    lead_rows = total_rows - out_rows
    own_segs = seg_list[lead_rows:]
    result = jnp.zeros((out_rows, keys_in.shape[1]), jnp.float32)
    for lag_index in range(short_taps.shape[0]):
        shifted = gated[lead_rows - lag_index : total_rows - lag_index]
        same_genome = (seg_list[lead_rows - lag_index : total_rows - lag_index] == own_segs).astype(
            jnp.float32
        )
        result = (
            result
            + short_taps[lag_index].astype(jnp.float32)[None, :] * shifted * same_genome[:, None]
        )
    return result.astype(jnp.bfloat16)


def circulants(table):
    lag_count, width = table.shape
    lag_ids = lax.optimization_barrier(jnp.arange(lag_count, dtype=jnp.int32))
    out_pos = jnp.arange(tile_rows, dtype=jnp.int32)[:, None]
    in_pos = jnp.arange(tile_rows, dtype=jnp.int32)[None, :]
    lag_grid = (out_pos - in_pos + tile_rows) % tile_rows
    one_hot = (lag_grid.reshape(1, tile_rows * tile_rows) == lag_ids[:, None]).astype(table.dtype)
    picked = jnp.dot(table.T, one_hot, preferred_element_type=jnp.float32)
    return picked.astype(table.dtype).reshape(width, tile_rows, tile_rows)


def modal_tables(modal_poles):
    decay_rate = modal_poles[0]
    angles = modal_poles[1]
    residue_re = modal_poles[2]
    residue_im = modal_poles[3]
    powers = jnp.arange(tile_rows + 1).astype(jnp.float32)[:, None, None]
    magnitude = jnp.exp(-powers * decay_rate[None])
    power_re = magnitude * jnp.cos(powers * angles[None])
    power_im = magnitude * jnp.sin(powers * angles[None])
    kernel_re = residue_re[None] * power_re - residue_im[None] * power_im
    kernel_im = residue_re[None] * power_im + residue_im[None] * power_re
    kernel = jnp.sum(kernel_re[:tile_rows], axis=2)
    toeplitz = split_table(kernel)
    outward = jnp.transpose(jnp.concatenate((kernel_re[1:], -kernel_im[1:]), axis=2), (1, 0, 2))
    inward = jnp.transpose(
        jnp.concatenate((power_re[tile_rows - 1 :: -1], power_im[tile_rows - 1 :: -1]), axis=2),
        (1, 0, 2),
    )
    return (toeplitz, outward, inward, power_re[tile_rows], power_im[tile_rows])


def split_table(table):
    upper = table.astype(jnp.bfloat16)
    lower = (table - upper.astype(jnp.float32)).astype(jnp.bfloat16)
    return (upper, lower)


def complex_link(earlier, later):
    early_are, early_aim, early_sre, early_sim = earlier
    late_are, late_aim, late_sre, late_sim = later
    lead_re = late_are[..., None, :]
    lead_im = late_aim[..., None, :]
    return (
        late_are * early_are - late_aim * early_aim,
        late_are * early_aim + late_aim * early_are,
        lead_re * early_sre - lead_im * early_sim + late_sre,
        lead_re * early_sim + lead_im * early_sre + late_sim,
    )


def log_probs(logits, targets):
    vocab_ids = jnp.arange(logits.shape[1], dtype=jnp.int32)
    picked = jnp.sum(
        jnp.where(targets[:, None] == vocab_ids[None, :], logits, jnp.zeros_like(logits)), axis=1
    )
    return picked - jnp.log(jnp.sum(jnp.exp(logits), axis=1))


def channel_logits(normed_cols, unembed):
    return lax.dot_general(
        normed_cols, unembed, (((0,), (0,)), ((), ())), preferred_element_type=jnp.float32
    )


def per_device(
    query_proj,
    key_proj,
    value_proj,
    short_taps,
    medium_taps,
    modal_poles,
    skip_gain,
    norm_gain,
    unembed,
    token_ids,
    genome_lengths,
):
    highest = lax.Precision.HIGHEST
    row_count, chan_count = query_proj.shape
    group_count = chan_count // GROUP
    mode_count = modal_poles.shape[2]
    tile_count = row_count // tile_rows
    first_row = lax.axis_index("seq") * row_count
    segments = segment_ids(first_row + jnp.arange(row_count, dtype=jnp.int32), genome_lengths)
    halo = tile_rows + short_margin
    edge_pair = from_behind(
        jnp.stack((key_proj[row_count - halo :], value_proj[row_count - halo :])),
        "seq",
        1,
    )
    ext_segs = segment_ids(
        first_row - halo + jnp.arange(row_count + halo, dtype=jnp.int32),
        genome_lengths,
    )
    filtered = short_filter(
        jnp.concatenate((edge_pair[0], key_proj)),
        jnp.concatenate((edge_pair[1], value_proj)),
        ext_segs,
        row_count + tile_rows,
        short_taps,
    )
    ext_short = filtered.T.reshape(group_count, GROUP, row_count + tile_rows)
    medium_segs = segment_ids(
        first_row - tile_rows + jnp.arange(row_count + tile_rows, dtype=jnp.int32), genome_lengths
    )

    long_toeplitz, outward, inward, decay_re, decay_im = modal_tables(modal_poles)
    circ = circulants(jnp.concatenate((medium_taps, long_toeplitz[0], long_toeplitz[1]), axis=1))
    circ_medium = jnp.concatenate((circ[:group_count], circ[:group_count]), axis=2)
    toeplitz_upper = circ[group_count : 2 * group_count]
    toeplitz_lower = circ[2 * group_count :]
    lag_band = (
        jnp.arange(tile_rows, dtype=jnp.int32)[:, None] + tile_rows
        - jnp.arange(2 * tile_rows, dtype=jnp.int32)[None, :]
    )
    medium_band = (lag_band >= 0) & (lag_band < medium_taps.shape[0])
    long_band = lag_band[:, tile_rows:] >= 0

    def medium_block(tile_index):
        start = tile_index * tile_rows
        window = lax.dynamic_slice_in_dim(ext_short, start, 2 * tile_rows, 2)
        window_segs = lax.dynamic_slice_in_dim(medium_segs, start, 2 * tile_rows, 0)
        own_segs = lax.dynamic_slice_in_dim(segments, start, tile_rows, 0)
        same_genome = (own_segs[:, None] == window_segs[None, :]) & medium_band
        matrix = jnp.where(same_genome[None], circ_medium, jnp.zeros_like(circ_medium))
        return jnp.einsum(
            "gts,gis->git", matrix, window, preferred_element_type=jnp.float32
        ).astype(jnp.bfloat16)

    signal = jnp.stack([medium_block(tile_index) for tile_index in range(tile_count)])
    inward_upper, inward_lower = split_table(inward)
    tile_segs = segments.reshape(tile_count, tile_rows)
    before = segment_ids(
        first_row + jnp.arange(tile_count, dtype=jnp.int32) * tile_rows - 1, genome_lengths
    )

    def intra_block(inputs):
        block_in, own_segs = inputs
        same_genome = ((own_segs[:, None] == own_segs[None, :]) & long_band)[None]
        upper = jnp.where(same_genome, toeplitz_upper, jnp.zeros_like(toeplitz_upper))
        lower = jnp.where(same_genome, toeplitz_lower, jnp.zeros_like(toeplitz_lower))
        return jnp.einsum(
            "gts,gis->git", upper, block_in, preferred_element_type=jnp.float32
        ) + jnp.einsum("gts,gis->git", lower, block_in, preferred_element_type=jnp.float32)

    local_part = jnp.stack([intra_block((signal[j], tile_segs[j])) for j in range(tile_count)])
    end_keep = (tile_segs == tile_segs[:, -1:])[:, None, None, :]
    masked_signal = jnp.where(end_keep, signal, jnp.zeros_like(signal))
    states = jnp.einsum(
        "gsm,jgis->jgim", inward_upper, masked_signal, preferred_element_type=jnp.float32
    ) + jnp.einsum(
        "gsm,jgis->jgim", inward_lower, masked_signal, preferred_element_type=jnp.float32
    )
    carried = (tile_segs[:, -1] == before).astype(jnp.float32)

    def chain_link(carry_in, inputs):
        block_states, kept_flag = inputs
        step = (
            decay_re * kept_flag,
            decay_im * kept_flag,
            block_states[..., :mode_count],
            block_states[..., mode_count:],
        )
        return (complex_link(carry_in, step), carry_in)

    state_zero = jnp.zeros((group_count, GROUP, mode_count), jnp.float32)
    start_carry = (
        jnp.ones((group_count, mode_count), jnp.float32),
        jnp.zeros((group_count, mode_count), jnp.float32),
        state_zero,
        state_zero,
    )
    carry = start_carry
    entering_steps = []
    for j in range(tile_count):
        carry, seen = chain_link(carry, (states[j], carried[j]))
        entering_steps.append(seen)
    summary = carry
    entering = tuple(jnp.stack(parts) for parts in zip(*entering_steps))
    incoming = entering_2(
        (summary[0], summary[1], summary[2], summary[3]),
        "seq",
        complex_link,
        (start_carry[0], start_carry[1], start_carry[2], start_carry[3]),
    )
    incoming_re = incoming[2]
    incoming_im = incoming[3]
    reach_re = entering[0][:, :, None, :]
    reach_im = entering[1][:, :, None, :]
    full_re = entering[2] + reach_re * incoming_re - reach_im * incoming_im
    full_im = entering[3] + reach_re * incoming_im + reach_im * incoming_re
    keep_mask = (tile_segs == before[:, None]).astype(jnp.float32)
    carried_part = (
        jnp.einsum(
            "gtm,jgim->jgit",
            outward,
            jnp.concatenate((full_re, full_im), axis=3),
            precision=highest,
        )
        * keep_mask[:, None, None, :]
    )
    longconv = (
        local_part
        + carried_part
        + skip_gain.reshape(group_count, GROUP)[None, :, :, None] * signal.astype(jnp.float32)
    )
    long_cols = jnp.transpose(longconv, (1, 2, 0, 3)).reshape(chan_count, row_count)
    mixed = (query_proj.T.astype(jnp.float32) * long_cols).astype(jnp.bfloat16)
    mixed_wide = mixed.astype(jnp.float32)
    squares = sum_over(jnp.sum(mixed_wide * mixed_wide, axis=0), ("chan", "rep"))
    normed = (mixed_wide * lax.rsqrt(squares / D + norm_eps)[None, :] * norm_gain[:, None]).astype(
        jnp.bfloat16
    )
    partial_value = channel_logits(normed, unembed)
    lanes = ("chan", "rep")
    lane_count = lax.axis_size(lanes)
    piece = row_count // lane_count
    logits, piece_index = scatter_sum(partial_value, lanes)
    piece_at = piece_index * piece
    logprob_piece = log_probs(logits, lax.dynamic_slice_in_dim(token_ids, piece_at, piece, 0))
    logprob = sum_over(
        lax.dynamic_update_slice_in_dim(
            jnp.zeros((row_count,), jnp.float32), logprob_piece, piece_at, 0
        ),
        lanes,
    )
    genome_index = jnp.arange(genome_lengths.shape[0], dtype=jnp.int32)
    genome_part = jnp.sum(
        jnp.where(
            segments[:, None] == genome_index[None, :],
            logprob[:, None],
            jnp.zeros((row_count, genome_lengths.shape[0]), jnp.float32),
        ),
        axis=0,
    )
    totals = sum_over(genome_part, "seq")
    return (logprob, totals / genome_lengths.astype(jnp.float32))


def solution(mesh):
    return jax.shard_map(
        per_device,
        mesh=mesh,
        in_specs=(
            P(("groups", "seq"), ("chan", "rep")),
            P(("groups", "seq"), ("chan", "rep")),
            P(("groups", "seq"), ("chan", "rep")),
            P(None, ("chan", "rep")),
            P(None, ("chan", "rep")),
            P(None, ("chan", "rep"), None),
            P(("chan", "rep")),
            P(("chan", "rep")),
            P(("chan", "rep"), None),
            P(("groups", "seq")),
            P("groups"),
        ),
        out_specs=(P(("groups", "seq")), P("groups")),
        check_vma=False,
    )
```

```python
import jax
import jax.numpy as jnp
from jax import lax
from jax.sharding import PartitionSpec as P

D = 8192
GROUP = 16


tile_rows = 128
short_margin = 8
norm_eps = 1e-05


def from_behind(shard, axis, by):
    count = lax.axis_size(axis)
    pairs = [(i, i + by) for i in range(count) if 0 <= i + by < count]
    return lax.ppermute(shard, axis, pairs)


def scatter_sum(part, axes):
    count = lax.axis_size(axes)
    place = lax.axis_index(axes)
    bit = 1
    piece_index = 0
    while bit < count:
        half = part.shape[0] // 2
        upper = (place & bit) != 0
        keep = jnp.where(upper, part[half:], part[:half])
        give = jnp.where(upper, part[:half], part[half:])
        part = keep + lax.ppermute(give, axes, [(i, i ^ bit) for i in range(count)])
        piece_index = piece_index * 2 + upper.astype(jnp.int32)
        bit *= 2
    return part, piece_index


def sum_over(part, axis):
    count = lax.axis_size(axis)
    if count & (count - 1):
        return lax.psum(part, axis)
    bit = 1
    while bit < count:
        part = part + lax.ppermute(part, axis, [(i, i ^ bit) for i in range(count)])
        bit *= 2
    return part


def entering_2(part, axis, combine, identity):
    place = lax.axis_index(axis)
    count = lax.axis_size(axis)
    lead = part[0].shape[0]
    widths = [a.size // lead for a in part]

    def pack(t):
        return jnp.concatenate([a.reshape(lead, -1) for a in t], axis=1)

    def unpack(flat):
        pieces = []
        offset = 0
        for a, width in zip(part, widths):
            pieces.append(flat[:, offset : offset + width].reshape(a.shape))
            offset += width
        return tuple(pieces)

    ident = tuple(jnp.zeros_like(a) + jnp.asarray(e, a.dtype) for a, e in zip(part, identity))
    before = ident
    upto = tuple(part)
    shift = 1
    while shift < count:
        arrived = unpack(from_behind(pack(upto), axis, shift))
        arrived = tuple(jnp.where(place >= shift, r, i) for r, i in zip(arrived, ident))
        before = combine(arrived, before)
        upto = combine(arrived, upto)
        shift *= 2
    return before


def segment_ids(positions, genome_lengths):
    starts = jnp.cumsum(genome_lengths) - genome_lengths
    at_or_past = (positions[:, None] >= starts[None, :]).astype(jnp.int32)
    return jnp.sum(at_or_past, axis=1) - 1


def short_filter(keys_in, values_in, seg_list, out_rows, short_taps):
    gated = keys_in.astype(jnp.float32) * values_in.astype(jnp.float32)
    total_rows = keys_in.shape[0]
    lead_rows = total_rows - out_rows
    own_segs = seg_list[lead_rows:]
    result = jnp.zeros((out_rows, keys_in.shape[1]), jnp.float32)
    for lag_index in range(short_taps.shape[0]):
        shifted = gated[lead_rows - lag_index : total_rows - lag_index]
        same_genome = (seg_list[lead_rows - lag_index : total_rows - lag_index] == own_segs).astype(
            jnp.float32
        )
        result = (
            result
            + short_taps[lag_index].astype(jnp.float32)[None, :] * shifted * same_genome[:, None]
        )
    return result.astype(jnp.bfloat16)


def circulants(table, cols):
    lag_count, width = table.shape
    lag_ids = lax.optimization_barrier(jnp.arange(lag_count, dtype=jnp.int32))
    out_pos = jnp.arange(tile_rows, dtype=jnp.int32)[:, None]
    in_pos = jnp.arange(cols, dtype=jnp.int32)[None, :]
    lag_grid = (out_pos - in_pos + cols) % tile_rows
    one_hot = (lag_grid.reshape(1, tile_rows * cols) == lag_ids[:, None]).astype(table.dtype)
    picked = jnp.dot(table.T, one_hot, preferred_element_type=jnp.float32)
    return picked.astype(table.dtype).reshape(width, tile_rows, cols)


def modal_tables(modal_poles):
    decay_rate = modal_poles[0]
    angles = modal_poles[1]
    residue_re = modal_poles[2]
    residue_im = modal_poles[3]
    powers = jnp.arange(tile_rows + 1).astype(jnp.float32)[:, None, None]
    magnitude = jnp.exp(-powers * decay_rate[None])
    power_re = magnitude * jnp.cos(powers * angles[None])
    power_im = magnitude * jnp.sin(powers * angles[None])
    kernel_re = residue_re[None] * power_re - residue_im[None] * power_im
    kernel_im = residue_re[None] * power_im + residue_im[None] * power_re
    kernel = jnp.sum(kernel_re[:tile_rows], axis=2)
    toeplitz = split_table(kernel)
    outward = jnp.transpose(jnp.concatenate((kernel_re[1:], -kernel_im[1:]), axis=2), (1, 0, 2))
    inward = jnp.transpose(
        jnp.concatenate((power_re[tile_rows - 1 :: -1], power_im[tile_rows - 1 :: -1]), axis=2),
        (1, 0, 2),
    )
    return (toeplitz, outward, inward, power_re[tile_rows], power_im[tile_rows])


def split_table(table):
    upper = table.astype(jnp.bfloat16)
    lower = (table - upper.astype(jnp.float32)).astype(jnp.bfloat16)
    return (upper, lower)


def complex_link(earlier, later):
    early_are, early_aim, early_sre, early_sim = earlier
    late_are, late_aim, late_sre, late_sim = later
    lead_re = late_are[..., None, :]
    lead_im = late_aim[..., None, :]
    return (
        late_are * early_are - late_aim * early_aim,
        late_are * early_aim + late_aim * early_are,
        lead_re * early_sre - lead_im * early_sim + late_sre,
        lead_re * early_sim + lead_im * early_sre + late_sim,
    )


def log_probs(logits, targets):
    vocab_ids = jnp.arange(logits.shape[1], dtype=jnp.int32)
    picked = jnp.sum(
        jnp.where(targets[:, None] == vocab_ids[None, :], logits, jnp.zeros_like(logits)), axis=1
    )
    return picked - jnp.log(jnp.sum(jnp.exp(logits), axis=1))


def channel_logits(normed_cols, unembed):
    return lax.dot_general(
        normed_cols, unembed, (((0,), (0,)), ((), ())), preferred_element_type=jnp.float32
    )


def per_device(
    query_proj,
    key_proj,
    value_proj,
    short_taps,
    medium_taps,
    modal_poles,
    skip_gain,
    norm_gain,
    unembed,
    token_ids,
    genome_lengths,
):
    highest = lax.Precision.HIGHEST
    row_count, chan_count = query_proj.shape
    group_count = chan_count // GROUP
    mode_count = modal_poles.shape[2]
    tile_count = row_count // tile_rows
    first_row = lax.axis_index("seq") * row_count
    segments = segment_ids(first_row + jnp.arange(row_count, dtype=jnp.int32), genome_lengths)
    halo = tile_rows + short_margin
    edge_pair = from_behind(
        jnp.stack((key_proj[row_count - halo :], value_proj[row_count - halo :])),
        "seq",
        1,
    )
    ext_segs = segment_ids(
        first_row - halo + jnp.arange(row_count + halo, dtype=jnp.int32),
        genome_lengths,
    )
    filtered = short_filter(
        jnp.concatenate((edge_pair[0], key_proj)),
        jnp.concatenate((edge_pair[1], value_proj)),
        ext_segs,
        row_count + tile_rows,
        short_taps,
    )
    ext_short = filtered.T.reshape(group_count, GROUP, row_count + tile_rows)
    medium_segs = segment_ids(
        first_row - tile_rows + jnp.arange(row_count + tile_rows, dtype=jnp.int32), genome_lengths
    )

    long_toeplitz, outward, inward, decay_re, decay_im = modal_tables(modal_poles)
    circ = circulants(
        jnp.concatenate((medium_taps, long_toeplitz[0], long_toeplitz[1]), axis=1), 2 * tile_rows
    )
    circ_medium = circ[:group_count]
    toeplitz_upper = circ[group_count : 2 * group_count, :, :tile_rows]
    toeplitz_lower = circ[2 * group_count :, :, :tile_rows]
    lag_band = (
        jnp.arange(tile_rows, dtype=jnp.int32)[:, None] + tile_rows
        - jnp.arange(2 * tile_rows, dtype=jnp.int32)[None, :]
    )
    medium_band = (lag_band >= 0) & (lag_band < medium_taps.shape[0])
    long_band = lag_band[:, tile_rows:] >= 0

    def medium_block(tile_index):
        start = tile_index * tile_rows
        window = lax.dynamic_slice_in_dim(ext_short, start, 2 * tile_rows, 2)
        window_segs = lax.dynamic_slice_in_dim(medium_segs, start, 2 * tile_rows, 0)
        own_segs = lax.dynamic_slice_in_dim(segments, start, tile_rows, 0)
        same_genome = (own_segs[:, None] == window_segs[None, :]) & medium_band
        matrix = jnp.where(same_genome[None], circ_medium, jnp.zeros_like(circ_medium))
        return jnp.einsum(
            "gts,gis->git", matrix, window, preferred_element_type=jnp.float32
        ).astype(jnp.bfloat16)

    signal = jnp.stack([medium_block(tile_index) for tile_index in range(tile_count)])
    inward_upper, inward_lower = split_table(inward)
    tile_segs = segments.reshape(tile_count, tile_rows)
    before = segment_ids(
        first_row + jnp.arange(tile_count, dtype=jnp.int32) * tile_rows - 1, genome_lengths
    )

    def intra_block(inputs):
        block_in, own_segs = inputs
        same_genome = ((own_segs[:, None] == own_segs[None, :]) & long_band)[None]
        upper = jnp.where(same_genome, toeplitz_upper, jnp.zeros_like(toeplitz_upper))
        lower = jnp.where(same_genome, toeplitz_lower, jnp.zeros_like(toeplitz_lower))
        return jnp.einsum(
            "gts,gis->git", upper, block_in, preferred_element_type=jnp.float32
        ) + jnp.einsum("gts,gis->git", lower, block_in, preferred_element_type=jnp.float32)

    local_part = jnp.stack([intra_block((signal[j], tile_segs[j])) for j in range(tile_count)])
    end_keep = (tile_segs == tile_segs[:, -1:])[:, None, None, :]
    masked_signal = jnp.where(end_keep, signal, jnp.zeros_like(signal))
    states = jnp.einsum(
        "gsm,jgis->jgim", inward_upper, masked_signal, preferred_element_type=jnp.float32
    ) + jnp.einsum(
        "gsm,jgis->jgim", inward_lower, masked_signal, preferred_element_type=jnp.float32
    )
    carried = (tile_segs[:, -1] == before).astype(jnp.float32)

    def chain_link(carry_in, inputs):
        block_states, kept_flag = inputs
        step = (
            decay_re * kept_flag,
            decay_im * kept_flag,
            block_states[..., :mode_count],
            block_states[..., mode_count:],
        )
        return (complex_link(carry_in, step), carry_in)

    state_zero = jnp.zeros((group_count, GROUP, mode_count), jnp.float32)
    start_carry = (
        jnp.ones((group_count, mode_count), jnp.float32),
        jnp.zeros((group_count, mode_count), jnp.float32),
        state_zero,
        state_zero,
    )
    summary, entering = lax.scan(chain_link, start_carry, (states, carried))
    incoming = entering_2(
        (summary[0], summary[1], summary[2], summary[3]),
        "seq",
        complex_link,
        (start_carry[0], start_carry[1], start_carry[2], start_carry[3]),
    )
    incoming_re = incoming[2]
    incoming_im = incoming[3]
    reach_re = entering[0][:, :, None, :]
    reach_im = entering[1][:, :, None, :]
    full_re = entering[2] + reach_re * incoming_re - reach_im * incoming_im
    full_im = entering[3] + reach_re * incoming_im + reach_im * incoming_re
    keep_mask = (tile_segs == before[:, None]).astype(jnp.float32)
    carried_part = (
        jnp.einsum(
            "gtm,jgim->jgit",
            outward,
            jnp.concatenate((full_re, full_im), axis=3),
            precision=highest,
        )
        * keep_mask[:, None, None, :]
    )
    longconv = (
        local_part
        + carried_part
        + skip_gain.reshape(group_count, GROUP)[None, :, :, None] * signal.astype(jnp.float32)
    )
    long_cols = jnp.transpose(longconv, (1, 2, 0, 3)).reshape(chan_count, row_count)
    mixed = (query_proj.T.astype(jnp.float32) * long_cols).astype(jnp.bfloat16)
    mixed_wide = mixed.astype(jnp.float32)
    squares = sum_over(jnp.sum(mixed_wide * mixed_wide, axis=0), ("chan", "rep"))
    normed = (mixed_wide * lax.rsqrt(squares / D + norm_eps)[None, :] * norm_gain[:, None]).astype(
        jnp.bfloat16
    )
    partial_value = channel_logits(normed, unembed)
    lanes = ("chan", "rep")
    lane_count = lax.axis_size(lanes)
    piece = row_count // lane_count
    logits, piece_index = scatter_sum(partial_value, lanes)
    piece_at = piece_index * piece
    logprob_piece = log_probs(logits, lax.dynamic_slice_in_dim(token_ids, piece_at, piece, 0))
    logprob = sum_over(
        lax.dynamic_update_slice_in_dim(
            jnp.zeros((row_count,), jnp.float32), logprob_piece, piece_at, 0
        ),
        lanes,
    )
    genome_index = jnp.arange(genome_lengths.shape[0], dtype=jnp.int32)
    genome_part = jnp.sum(
        jnp.where(
            segments[:, None] == genome_index[None, :],
            logprob[:, None],
            jnp.zeros((row_count, genome_lengths.shape[0]), jnp.float32),
        ),
        axis=0,
    )
    totals = sum_over(genome_part, "seq")
    return (logprob, totals / genome_lengths.astype(jnp.float32))


def solution(mesh):
    return jax.shard_map(
        per_device,
        mesh=mesh,
        in_specs=(
            P(("groups", "seq"), ("chan", "rep")),
            P(("groups", "seq"), ("chan", "rep")),
            P(("groups", "seq"), ("chan", "rep")),
            P(None, ("chan", "rep")),
            P(None, ("chan", "rep")),
            P(None, ("chan", "rep"), None),
            P(("chan", "rep")),
            P(("chan", "rep")),
            P(("chan", "rep"), None),
            P(("groups", "seq")),
            P("groups"),
        ),
        out_specs=(P(("groups", "seq")), P("groups")),
        check_vma=False,
    )
```

```python
import jax
import jax.numpy as jnp
from jax import lax
from jax.sharding import PartitionSpec as P

D = 8192
GROUP = 16


tile_rows = 128
short_margin = 8
norm_eps = 1e-05


def from_behind(shard, axis, by):
    count = lax.axis_size(axis)
    pairs = [(i, i + by) for i in range(count) if 0 <= i + by < count]
    return lax.ppermute(shard, axis, pairs)


def scatter_sum(part, axes):
    count = lax.axis_size(axes)
    place = lax.axis_index(axes)
    bit = 1
    piece_index = 0
    while bit < count:
        half = part.shape[0] // 2
        upper = (place & bit) != 0
        keep = jnp.where(upper, part[half:], part[:half])
        give = jnp.where(upper, part[:half], part[half:])
        part = keep + lax.ppermute(give, axes, [(i, i ^ bit) for i in range(count)])
        piece_index = piece_index * 2 + upper.astype(jnp.int32)
        bit *= 2
    return part, piece_index


def sum_over(part, axis):
    count = lax.axis_size(axis)
    if count & (count - 1):
        return lax.psum(part, axis)
    bit = 1
    while bit < count:
        part = part + lax.ppermute(part, axis, [(i, i ^ bit) for i in range(count)])
        bit *= 2
    return part


def entering_2(part, axis, combine, identity):
    place = lax.axis_index(axis)
    count = lax.axis_size(axis)
    lead = part[0].shape[0]
    widths = [a.size // lead for a in part]

    def pack(t):
        return jnp.concatenate([a.reshape(lead, -1) for a in t], axis=1)

    def unpack(flat):
        pieces = []
        offset = 0
        for a, width in zip(part, widths):
            pieces.append(flat[:, offset : offset + width].reshape(a.shape))
            offset += width
        return tuple(pieces)

    ident = tuple(jnp.zeros_like(a) + jnp.asarray(e, a.dtype) for a, e in zip(part, identity))
    before = ident
    upto = tuple(part)
    shift = 1
    while shift < count:
        arrived = unpack(from_behind(pack(upto), axis, shift))
        arrived = tuple(jnp.where(place >= shift, r, i) for r, i in zip(arrived, ident))
        before = combine(arrived, before)
        upto = combine(arrived, upto)
        shift *= 2
    return before


def segment_ids(positions, genome_lengths):
    starts = jnp.cumsum(genome_lengths) - genome_lengths
    at_or_past = (positions[:, None] >= starts[None, :]).astype(jnp.int32)
    return jnp.sum(at_or_past, axis=1) - 1


def short_filter(keys_in, values_in, seg_list, out_rows, short_taps):
    gated = keys_in.astype(jnp.float32) * values_in.astype(jnp.float32)
    total_rows = keys_in.shape[0]
    lead_rows = total_rows - out_rows
    own_segs = seg_list[lead_rows:]
    result = jnp.zeros((out_rows, keys_in.shape[1]), jnp.float32)
    for lag_index in range(short_taps.shape[0]):
        shifted = gated[lead_rows - lag_index : total_rows - lag_index]
        same_genome = (seg_list[lead_rows - lag_index : total_rows - lag_index] == own_segs).astype(
            jnp.float32
        )
        result = (
            result
            + short_taps[lag_index].astype(jnp.float32)[None, :] * shifted * same_genome[:, None]
        )
    return result.astype(jnp.bfloat16)


def circulants(table):
    lag_count, width = table.shape
    lag_ids = lax.optimization_barrier(jnp.arange(lag_count, dtype=jnp.int32))
    out_pos = jnp.arange(tile_rows, dtype=jnp.int32)[:, None]
    in_pos = jnp.arange(tile_rows, dtype=jnp.int32)[None, :]
    lag_grid = (out_pos - in_pos + tile_rows) % tile_rows
    one_hot = (lag_grid.reshape(1, tile_rows * tile_rows) == lag_ids[:, None]).astype(table.dtype)
    picked = jnp.dot(table.T, one_hot, preferred_element_type=jnp.float32)
    return picked.astype(table.dtype).reshape(width, tile_rows, tile_rows)


def modal_tables(modal_poles):
    decay_rate = modal_poles[0]
    angles = modal_poles[1]
    residue_re = modal_poles[2]
    residue_im = modal_poles[3]
    powers = jnp.arange(tile_rows + 1).astype(jnp.float32)[:, None, None]
    magnitude = jnp.exp(-powers * decay_rate[None])
    power_re = magnitude * jnp.cos(powers * angles[None])
    power_im = magnitude * jnp.sin(powers * angles[None])
    kernel_re = residue_re[None] * power_re - residue_im[None] * power_im
    kernel_im = residue_re[None] * power_im + residue_im[None] * power_re
    kernel = jnp.sum(kernel_re[:tile_rows], axis=2)
    toeplitz = split_table(kernel)
    outward = jnp.transpose(jnp.concatenate((kernel_re[1:], -kernel_im[1:]), axis=2), (1, 0, 2))
    inward = jnp.transpose(
        jnp.concatenate((power_re[tile_rows - 1 :: -1], power_im[tile_rows - 1 :: -1]), axis=2),
        (1, 0, 2),
    )
    return (toeplitz, outward, inward, power_re[tile_rows], power_im[tile_rows])


def split_table(table):
    upper = table.astype(jnp.bfloat16)
    lower = (table - upper.astype(jnp.float32)).astype(jnp.bfloat16)
    return (upper, lower)


def complex_link(earlier, later):
    early_are, early_aim, early_sre, early_sim = earlier
    late_are, late_aim, late_sre, late_sim = later
    lead_re = late_are[..., None, :]
    lead_im = late_aim[..., None, :]
    return (
        late_are * early_are - late_aim * early_aim,
        late_are * early_aim + late_aim * early_are,
        lead_re * early_sre - lead_im * early_sim + late_sre,
        lead_re * early_sim + lead_im * early_sre + late_sim,
    )


def log_probs(logits, targets):
    vocab_ids = jnp.arange(logits.shape[1], dtype=jnp.int32)
    picked = jnp.sum(
        jnp.where(targets[:, None] == vocab_ids[None, :], logits, jnp.zeros_like(logits)), axis=1
    )
    return picked - jnp.log(jnp.sum(jnp.exp(logits), axis=1))


def channel_logits(normed_cols, unembed):
    return lax.dot_general(
        normed_cols, unembed, (((0,), (0,)), ((), ())), preferred_element_type=jnp.float32
    )


def per_device(
    query_proj,
    key_proj,
    value_proj,
    short_taps,
    medium_taps,
    modal_poles,
    skip_gain,
    norm_gain,
    unembed,
    token_ids,
    genome_lengths,
):
    highest = lax.Precision.HIGHEST
    row_count, chan_count = query_proj.shape
    group_count = chan_count // GROUP
    mode_count = modal_poles.shape[2]
    tile_count = row_count // tile_rows
    first_row = lax.axis_index("seq") * row_count
    segments = segment_ids(first_row + jnp.arange(row_count, dtype=jnp.int32), genome_lengths)
    halo = tile_rows + short_margin
    edge_pair = from_behind(
        jnp.stack((key_proj[row_count - halo :], value_proj[row_count - halo :])),
        "seq",
        1,
    )
    ext_segs = segment_ids(
        first_row - halo + jnp.arange(row_count + halo, dtype=jnp.int32),
        genome_lengths,
    )
    filtered = short_filter(
        jnp.concatenate((edge_pair[0], key_proj)),
        jnp.concatenate((edge_pair[1], value_proj)),
        ext_segs,
        row_count + tile_rows,
        short_taps,
    )
    ext_short = filtered.T.reshape(group_count, GROUP, row_count + tile_rows)
    medium_segs = segment_ids(
        first_row - tile_rows + jnp.arange(row_count + tile_rows, dtype=jnp.int32), genome_lengths
    )

    long_toeplitz, outward, inward, decay_re, decay_im = modal_tables(modal_poles)
    circ = circulants(jnp.concatenate((medium_taps, long_toeplitz[0], long_toeplitz[1]), axis=1))
    circ_medium = jnp.concatenate((circ[:group_count], circ[:group_count]), axis=2)
    toeplitz_upper = circ[group_count : 2 * group_count]
    toeplitz_lower = circ[2 * group_count :]
    lag_band = (
        jnp.arange(tile_rows, dtype=jnp.int32)[:, None] + tile_rows
        - jnp.arange(2 * tile_rows, dtype=jnp.int32)[None, :]
    )
    medium_band = (lag_band >= 0) & (lag_band < medium_taps.shape[0])
    long_band = lag_band[:, tile_rows:] >= 0

    def medium_block(tile_index):
        start = tile_index * tile_rows
        window = lax.dynamic_slice_in_dim(ext_short, start, 2 * tile_rows, 2)
        window_segs = lax.dynamic_slice_in_dim(medium_segs, start, 2 * tile_rows, 0)
        own_segs = lax.dynamic_slice_in_dim(segments, start, tile_rows, 0)
        same_genome = (own_segs[:, None] == window_segs[None, :]) & medium_band
        matrix = jnp.where(same_genome[None], circ_medium, jnp.zeros_like(circ_medium))
        return jnp.einsum(
            "gts,gis->git", matrix, window, preferred_element_type=jnp.float32
        ).astype(jnp.bfloat16)

    signal = jnp.stack([medium_block(tile_index) for tile_index in range(tile_count)])
    inward_upper, inward_lower = split_table(inward)
    tile_segs = segments.reshape(tile_count, tile_rows)
    before = segment_ids(
        first_row + jnp.arange(tile_count, dtype=jnp.int32) * tile_rows - 1, genome_lengths
    )

    def intra_block(inputs):
        block_in, own_segs = inputs
        same_genome = ((own_segs[:, None] == own_segs[None, :]) & long_band)[None]
        upper = jnp.where(same_genome, toeplitz_upper, jnp.zeros_like(toeplitz_upper))
        lower = jnp.where(same_genome, toeplitz_lower, jnp.zeros_like(toeplitz_lower))
        return jnp.einsum(
            "gts,gis->git",
            jnp.concatenate((upper, lower), axis=2),
            jnp.concatenate((block_in, block_in), axis=2),
            preferred_element_type=jnp.float32,
        )

    local_part = jnp.stack([intra_block((signal[j], tile_segs[j])) for j in range(tile_count)])
    end_keep = (tile_segs == tile_segs[:, -1:])[:, None, None, :]
    masked_signal = jnp.where(end_keep, signal, jnp.zeros_like(signal))
    states = jnp.einsum(
        "gsm,jgis->jgim", inward_upper, masked_signal, preferred_element_type=jnp.float32
    ) + jnp.einsum(
        "gsm,jgis->jgim", inward_lower, masked_signal, preferred_element_type=jnp.float32
    )
    carried = (tile_segs[:, -1] == before).astype(jnp.float32)

    def chain_link(carry_in, inputs):
        block_states, kept_flag = inputs
        step = (
            decay_re * kept_flag,
            decay_im * kept_flag,
            block_states[..., :mode_count],
            block_states[..., mode_count:],
        )
        return (complex_link(carry_in, step), carry_in)

    state_zero = jnp.zeros((group_count, GROUP, mode_count), jnp.float32)
    start_carry = (
        jnp.ones((group_count, mode_count), jnp.float32),
        jnp.zeros((group_count, mode_count), jnp.float32),
        state_zero,
        state_zero,
    )
    carry = start_carry
    entering_steps = []
    for j in range(tile_count):
        carry, seen = chain_link(carry, (states[j], carried[j]))
        entering_steps.append(seen)
    summary = carry
    entering = tuple(jnp.stack(parts) for parts in zip(*entering_steps))
    incoming = entering_2(
        (summary[0], summary[1], summary[2], summary[3]),
        "seq",
        complex_link,
        (start_carry[0], start_carry[1], start_carry[2], start_carry[3]),
    )
    incoming_re = incoming[2]
    incoming_im = incoming[3]
    reach_re = entering[0][:, :, None, :]
    reach_im = entering[1][:, :, None, :]
    full_re = entering[2] + reach_re * incoming_re - reach_im * incoming_im
    full_im = entering[3] + reach_re * incoming_im + reach_im * incoming_re
    keep_mask = (tile_segs == before[:, None]).astype(jnp.float32)
    carried_part = (
        jnp.einsum(
            "gtm,jgim->jgit",
            outward,
            jnp.concatenate((full_re, full_im), axis=3),
            precision=highest,
        )
        * keep_mask[:, None, None, :]
    )
    longconv = (
        local_part
        + carried_part
        + skip_gain.reshape(group_count, GROUP)[None, :, :, None] * signal.astype(jnp.float32)
    )
    long_cols = jnp.transpose(longconv, (1, 2, 0, 3)).reshape(chan_count, row_count)
    mixed = (query_proj.T.astype(jnp.float32) * long_cols).astype(jnp.bfloat16)
    mixed_wide = mixed.astype(jnp.float32)
    squares = sum_over(jnp.sum(mixed_wide * mixed_wide, axis=0), ("chan", "rep"))
    normed = (mixed_wide * lax.rsqrt(squares / D + norm_eps)[None, :] * norm_gain[:, None]).astype(
        jnp.bfloat16
    )
    partial_value = channel_logits(normed, unembed)
    lanes = ("chan", "rep")
    lane_count = lax.axis_size(lanes)
    piece = row_count // lane_count
    logits, piece_index = scatter_sum(partial_value, lanes)
    piece_at = piece_index * piece
    logprob_piece = log_probs(logits, lax.dynamic_slice_in_dim(token_ids, piece_at, piece, 0))
    logprob = sum_over(
        lax.dynamic_update_slice_in_dim(
            jnp.zeros((row_count,), jnp.float32), logprob_piece, piece_at, 0
        ),
        lanes,
    )
    genome_index = jnp.arange(genome_lengths.shape[0], dtype=jnp.int32)
    genome_part = jnp.sum(
        jnp.where(
            segments[:, None] == genome_index[None, :],
            logprob[:, None],
            jnp.zeros((row_count, genome_lengths.shape[0]), jnp.float32),
        ),
        axis=0,
    )
    totals = sum_over(genome_part, "seq")
    return (logprob, totals / genome_lengths.astype(jnp.float32))


def solution(mesh):
    return jax.shard_map(
        per_device,
        mesh=mesh,
        in_specs=(
            P(("groups", "seq"), ("chan", "rep")),
            P(("groups", "seq"), ("chan", "rep")),
            P(("groups", "seq"), ("chan", "rep")),
            P(None, ("chan", "rep")),
            P(None, ("chan", "rep")),
            P(None, ("chan", "rep"), None),
            P(("chan", "rep")),
            P(("chan", "rep")),
            P(("chan", "rep"), None),
            P(("groups", "seq")),
            P("groups"),
        ),
        out_specs=(P(("groups", "seq")), P("groups")),
        check_vma=False,
    )
```

```python
import jax
import jax.numpy as jnp
from jax import lax
from jax.sharding import PartitionSpec as P

D = 8192
GROUP = 16


tile_rows = 128
short_margin = 8
norm_eps = 1e-05


def from_behind(shard, axis, by):
    count = lax.axis_size(axis)
    pairs = [(i, i + by) for i in range(count) if 0 <= i + by < count]
    return lax.ppermute(shard, axis, pairs)


def scatter_sum(part, axes):
    count = lax.axis_size(axes)
    place = lax.axis_index(axes)
    bit = 1
    piece_index = 0
    while bit < count:
        half = part.shape[0] // 2
        upper = (place & bit) != 0
        keep = jnp.where(upper, part[half:], part[:half])
        give = jnp.where(upper, part[:half], part[half:])
        part = keep + lax.ppermute(give, axes, [(i, i ^ bit) for i in range(count)])
        piece_index = piece_index * 2 + upper.astype(jnp.int32)
        bit *= 2
    return part, piece_index


def sum_over(part, axis):
    count = lax.axis_size(axis)
    if count & (count - 1):
        return lax.psum(part, axis)
    bit = 1
    while bit < count:
        part = part + lax.ppermute(part, axis, [(i, i ^ bit) for i in range(count)])
        bit *= 2
    return part


def entering_2(part, axis, combine, identity):
    place = lax.axis_index(axis)
    count = lax.axis_size(axis)
    lead = part[0].shape[0]
    widths = [a.size // lead for a in part]

    def pack(t):
        return jnp.concatenate([a.reshape(lead, -1) for a in t], axis=1)

    def unpack(flat):
        pieces = []
        offset = 0
        for a, width in zip(part, widths):
            pieces.append(flat[:, offset : offset + width].reshape(a.shape))
            offset += width
        return tuple(pieces)

    ident = tuple(jnp.zeros_like(a) + jnp.asarray(e, a.dtype) for a, e in zip(part, identity))
    before = ident
    upto = tuple(part)
    shift = 1
    while shift < count:
        arrived = unpack(from_behind(pack(upto), axis, shift))
        arrived = tuple(jnp.where(place >= shift, r, i) for r, i in zip(arrived, ident))
        before = combine(arrived, before)
        upto = combine(arrived, upto)
        shift *= 2
    return before


def segment_ids(positions, genome_lengths):
    starts = jnp.cumsum(genome_lengths) - genome_lengths
    at_or_past = (positions[:, None] >= starts[None, :]).astype(jnp.int32)
    return jnp.sum(at_or_past, axis=1) - 1


def short_filter(keys_in, values_in, seg_list, out_rows, short_taps):
    gated = keys_in.astype(jnp.float32) * values_in.astype(jnp.float32)
    total_rows = keys_in.shape[0]
    lead_rows = total_rows - out_rows
    own_segs = seg_list[lead_rows:]
    result = jnp.zeros((out_rows, keys_in.shape[1]), jnp.float32)
    for lag_index in range(short_taps.shape[0]):
        shifted = gated[lead_rows - lag_index : total_rows - lag_index]
        same_genome = (seg_list[lead_rows - lag_index : total_rows - lag_index] == own_segs).astype(
            jnp.float32
        )
        result = (
            result
            + short_taps[lag_index].astype(jnp.float32)[None, :] * shifted * same_genome[:, None]
        )
    return result.astype(jnp.bfloat16)


def circulants(table):
    lag_count, width = table.shape
    lag_ids = lax.optimization_barrier(jnp.arange(lag_count, dtype=jnp.int32))
    out_pos = jnp.arange(tile_rows, dtype=jnp.int32)[:, None]
    in_pos = jnp.arange(tile_rows, dtype=jnp.int32)[None, :]
    lag_grid = (out_pos - in_pos + tile_rows) % tile_rows
    one_hot = (lag_grid.reshape(1, tile_rows * tile_rows) == lag_ids[:, None]).astype(table.dtype)
    picked = jnp.dot(table.T, one_hot, preferred_element_type=jnp.float32)
    return picked.astype(table.dtype).reshape(width, tile_rows, tile_rows)


def modal_tables(modal_poles):
    decay_rate = modal_poles[0]
    angles = modal_poles[1]
    residue_re = modal_poles[2]
    residue_im = modal_poles[3]
    powers = jnp.arange(tile_rows + 1).astype(jnp.float32)[:, None, None]
    magnitude = jnp.exp(-powers * decay_rate[None])
    power_re = magnitude * jnp.cos(powers * angles[None])
    power_im = magnitude * jnp.sin(powers * angles[None])
    kernel_re = residue_re[None] * power_re - residue_im[None] * power_im
    kernel_im = residue_re[None] * power_im + residue_im[None] * power_re
    kernel = jnp.sum(kernel_re[:tile_rows], axis=2)
    toeplitz = split_table(kernel)
    outward = jnp.transpose(jnp.concatenate((kernel_re[1:], -kernel_im[1:]), axis=2), (1, 0, 2))
    inward = jnp.transpose(
        jnp.concatenate((power_re[tile_rows - 1 :: -1], power_im[tile_rows - 1 :: -1]), axis=2),
        (1, 0, 2),
    )
    return (toeplitz, outward, inward, power_re[tile_rows], power_im[tile_rows])


def split_table(table):
    upper = table.astype(jnp.bfloat16)
    lower = (table - upper.astype(jnp.float32)).astype(jnp.bfloat16)
    return (upper, lower)


def complex_link(earlier, later):
    early_are, early_aim, early_sre, early_sim = earlier
    late_are, late_aim, late_sre, late_sim = later
    lead_re = late_are[..., None, :]
    lead_im = late_aim[..., None, :]
    return (
        late_are * early_are - late_aim * early_aim,
        late_are * early_aim + late_aim * early_are,
        lead_re * early_sre - lead_im * early_sim + late_sre,
        lead_re * early_sim + lead_im * early_sre + late_sim,
    )


def log_probs(logits, targets):
    vocab_ids = jnp.arange(logits.shape[1], dtype=jnp.int32)
    picked = jnp.sum(
        jnp.where(targets[:, None] == vocab_ids[None, :], logits, jnp.zeros_like(logits)), axis=1
    )
    return picked - jnp.log(jnp.sum(jnp.exp(logits), axis=1))


def channel_logits(normed_cols, unembed):
    return lax.dot_general(
        normed_cols, unembed, (((0,), (0,)), ((), ())), preferred_element_type=jnp.float32
    )


def per_device(
    query_proj,
    key_proj,
    value_proj,
    short_taps,
    medium_taps,
    modal_poles,
    skip_gain,
    norm_gain,
    unembed,
    token_ids,
    genome_lengths,
):
    highest = lax.Precision.HIGHEST
    row_count, chan_count = query_proj.shape
    group_count = chan_count // GROUP
    mode_count = modal_poles.shape[2]
    tile_count = row_count // tile_rows
    first_row = lax.axis_index("seq") * row_count
    segments = segment_ids(first_row + jnp.arange(row_count, dtype=jnp.int32), genome_lengths)
    halo = tile_rows + short_margin
    edge_pair = from_behind(
        jnp.stack((key_proj[row_count - halo :], value_proj[row_count - halo :])),
        "seq",
        1,
    )
    ext_segs = segment_ids(
        first_row - halo + jnp.arange(row_count + halo, dtype=jnp.int32),
        genome_lengths,
    )
    filtered = short_filter(
        jnp.concatenate((edge_pair[0], key_proj)),
        jnp.concatenate((edge_pair[1], value_proj)),
        ext_segs,
        row_count + tile_rows,
        short_taps,
    )
    ext_short = filtered.T.reshape(group_count, GROUP, row_count + tile_rows)
    medium_segs = segment_ids(
        first_row - tile_rows + jnp.arange(row_count + tile_rows, dtype=jnp.int32), genome_lengths
    )

    long_toeplitz, outward, inward, decay_re, decay_im = modal_tables(modal_poles)
    circ = circulants(jnp.concatenate((medium_taps, long_toeplitz[0], long_toeplitz[1]), axis=1))
    circ_medium = jnp.concatenate((circ[:group_count], circ[:group_count]), axis=2)
    toeplitz_upper = circ[group_count : 2 * group_count]
    toeplitz_lower = circ[2 * group_count :]
    lag_band = (
        jnp.arange(tile_rows, dtype=jnp.int32)[:, None] + tile_rows
        - jnp.arange(2 * tile_rows, dtype=jnp.int32)[None, :]
    )
    medium_band = (lag_band >= 0) & (lag_band < medium_taps.shape[0])
    long_band = lag_band[:, tile_rows:] >= 0

    def medium_block(tile_index):
        start = tile_index * tile_rows
        window = lax.dynamic_slice_in_dim(ext_short, start, 2 * tile_rows, 2)
        window_segs = lax.dynamic_slice_in_dim(medium_segs, start, 2 * tile_rows, 0)
        own_segs = lax.dynamic_slice_in_dim(segments, start, tile_rows, 0)
        same_genome = (own_segs[:, None] == window_segs[None, :]) & medium_band
        matrix = jnp.where(same_genome[None], circ_medium, jnp.zeros_like(circ_medium))
        return jnp.einsum(
            "gts,gis->git", matrix, window, preferred_element_type=jnp.float32
        ).astype(jnp.bfloat16)

    signal = jnp.stack([medium_block(tile_index) for tile_index in range(tile_count)])
    inward_upper, inward_lower = split_table(inward)
    tile_segs = segments.reshape(tile_count, tile_rows)
    before = segment_ids(
        first_row + jnp.arange(tile_count, dtype=jnp.int32) * tile_rows - 1, genome_lengths
    )

    def intra_block(inputs):
        block_in, own_segs = inputs
        same_genome = ((own_segs[:, None] == own_segs[None, :]) & long_band)[None]
        upper = jnp.where(same_genome, toeplitz_upper, jnp.zeros_like(toeplitz_upper))
        lower = jnp.where(same_genome, toeplitz_lower, jnp.zeros_like(toeplitz_lower))
        return jnp.einsum(
            "gts,gis->git",
            jnp.concatenate((upper, lower), axis=2),
            jnp.concatenate((block_in, block_in), axis=2),
            preferred_element_type=jnp.float32,
        )

    local_part = jnp.stack([intra_block((signal[j], tile_segs[j])) for j in range(tile_count)])
    end_keep = (tile_segs == tile_segs[:, -1:])[:, None, None, :]
    masked_signal = jnp.where(end_keep, signal, jnp.zeros_like(signal))
    states = jnp.einsum(
        "gsm,jgis->jgim",
        jnp.concatenate((inward_upper, inward_lower), axis=1),
        jnp.concatenate((masked_signal, masked_signal), axis=3),
        preferred_element_type=jnp.float32,
    )
    carried = (tile_segs[:, -1] == before).astype(jnp.float32)

    def chain_link(carry_in, inputs):
        block_states, kept_flag = inputs
        step = (
            decay_re * kept_flag,
            decay_im * kept_flag,
            block_states[..., :mode_count],
            block_states[..., mode_count:],
        )
        return (complex_link(carry_in, step), carry_in)

    state_zero = jnp.zeros((group_count, GROUP, mode_count), jnp.float32)
    start_carry = (
        jnp.ones((group_count, mode_count), jnp.float32),
        jnp.zeros((group_count, mode_count), jnp.float32),
        state_zero,
        state_zero,
    )
    carry = start_carry
    entering_steps = []
    for j in range(tile_count):
        carry, seen = chain_link(carry, (states[j], carried[j]))
        entering_steps.append(seen)
    summary = carry
    entering = tuple(jnp.stack(parts) for parts in zip(*entering_steps))
    incoming = entering_2(
        (summary[0], summary[1], summary[2], summary[3]),
        "seq",
        complex_link,
        (start_carry[0], start_carry[1], start_carry[2], start_carry[3]),
    )
    incoming_re = incoming[2]
    incoming_im = incoming[3]
    reach_re = entering[0][:, :, None, :]
    reach_im = entering[1][:, :, None, :]
    full_re = entering[2] + reach_re * incoming_re - reach_im * incoming_im
    full_im = entering[3] + reach_re * incoming_im + reach_im * incoming_re
    keep_mask = (tile_segs == before[:, None]).astype(jnp.float32)
    carried_part = (
        jnp.einsum(
            "gtm,jgim->jgit",
            outward,
            jnp.concatenate((full_re, full_im), axis=3),
            precision=highest,
        )
        * keep_mask[:, None, None, :]
    )
    longconv = (
        local_part
        + carried_part
        + skip_gain.reshape(group_count, GROUP)[None, :, :, None] * signal.astype(jnp.float32)
    )
    long_cols = jnp.transpose(longconv, (1, 2, 0, 3)).reshape(chan_count, row_count)
    mixed = (query_proj.T.astype(jnp.float32) * long_cols).astype(jnp.bfloat16)
    mixed_wide = mixed.astype(jnp.float32)
    squares = sum_over(jnp.sum(mixed_wide * mixed_wide, axis=0), ("chan", "rep"))
    normed = (mixed_wide * lax.rsqrt(squares / D + norm_eps)[None, :] * norm_gain[:, None]).astype(
        jnp.bfloat16
    )
    partial_value = channel_logits(normed, unembed)
    lanes = ("chan", "rep")
    lane_count = lax.axis_size(lanes)
    piece = row_count // lane_count
    logits, piece_index = scatter_sum(partial_value, lanes)
    piece_at = piece_index * piece
    logprob_piece = log_probs(logits, lax.dynamic_slice_in_dim(token_ids, piece_at, piece, 0))
    logprob = sum_over(
        lax.dynamic_update_slice_in_dim(
            jnp.zeros((row_count,), jnp.float32), logprob_piece, piece_at, 0
        ),
        lanes,
    )
    genome_index = jnp.arange(genome_lengths.shape[0], dtype=jnp.int32)
    genome_part = jnp.sum(
        jnp.where(
            segments[:, None] == genome_index[None, :],
            logprob[:, None],
            jnp.zeros((row_count, genome_lengths.shape[0]), jnp.float32),
        ),
        axis=0,
    )
    totals = sum_over(genome_part, "seq")
    return (logprob, totals / genome_lengths.astype(jnp.float32))


def solution(mesh):
    return jax.shard_map(
        per_device,
        mesh=mesh,
        in_specs=(
            P(("groups", "seq"), ("chan", "rep")),
            P(("groups", "seq"), ("chan", "rep")),
            P(("groups", "seq"), ("chan", "rep")),
            P(None, ("chan", "rep")),
            P(None, ("chan", "rep")),
            P(None, ("chan", "rep"), None),
            P(("chan", "rep")),
            P(("chan", "rep")),
            P(("chan", "rep"), None),
            P(("groups", "seq")),
            P("groups"),
        ),
        out_specs=(P(("groups", "seq")), P("groups")),
        check_vma=False,
    )
```

```python
import jax
import jax.numpy as jnp
from jax import lax
from jax.sharding import PartitionSpec as P

D = 8192
GROUP = 16


tile_rows = 128
short_margin = 8
norm_eps = 1e-05


def from_behind(shard, axis, by):
    count = lax.axis_size(axis)
    pairs = [(i, i + by) for i in range(count) if 0 <= i + by < count]
    return lax.ppermute(shard, axis, pairs)


def scatter_sum(part, axes):
    count = lax.axis_size(axes)
    place = lax.axis_index(axes)
    bit = 1
    piece_index = 0
    while bit < count:
        half = part.shape[0] // 2
        upper = (place & bit) != 0
        keep = jnp.where(upper, part[half:], part[:half])
        give = jnp.where(upper, part[:half], part[half:])
        part = keep + lax.ppermute(give, axes, [(i, i ^ bit) for i in range(count)])
        piece_index = piece_index * 2 + upper.astype(jnp.int32)
        bit *= 2
    return part, piece_index


def sum_over(part, axis):
    count = lax.axis_size(axis)
    if count & (count - 1):
        return lax.psum(part, axis)
    bit = 1
    while bit < count:
        part = part + lax.ppermute(part, axis, [(i, i ^ bit) for i in range(count)])
        bit *= 2
    return part


def entering_2(part, axis, combine, identity):
    place = lax.axis_index(axis)
    count = lax.axis_size(axis)
    lead = part[0].shape[0]
    widths = [a.size // lead for a in part]

    def pack(t):
        return jnp.concatenate([a.reshape(lead, -1) for a in t], axis=1)

    def unpack(flat):
        pieces = []
        offset = 0
        for a, width in zip(part, widths):
            pieces.append(flat[:, offset : offset + width].reshape(a.shape))
            offset += width
        return tuple(pieces)

    ident = tuple(jnp.zeros_like(a) + jnp.asarray(e, a.dtype) for a, e in zip(part, identity))
    before = ident
    upto = tuple(part)
    shift = 1
    while shift < count:
        arrived = unpack(from_behind(pack(upto), axis, shift))
        arrived = tuple(jnp.where(place >= shift, r, i) for r, i in zip(arrived, ident))
        before = combine(arrived, before)
        upto = combine(arrived, upto)
        shift *= 2
    return before


def segment_ids(positions, genome_lengths):
    starts = jnp.cumsum(genome_lengths) - genome_lengths
    at_or_past = (positions[:, None] >= starts[None, :]).astype(jnp.int32)
    return jnp.sum(at_or_past, axis=1) - 1


def short_filter(keys_in, values_in, seg_list, out_rows, short_taps):
    gated = keys_in.astype(jnp.float32) * values_in.astype(jnp.float32)
    total_rows = keys_in.shape[0]
    lead_rows = total_rows - out_rows
    own_segs = seg_list[lead_rows:]
    result = jnp.zeros((out_rows, keys_in.shape[1]), jnp.float32)
    for lag_index in range(short_taps.shape[0]):
        shifted = gated[lead_rows - lag_index : total_rows - lag_index]
        same_genome = (seg_list[lead_rows - lag_index : total_rows - lag_index] == own_segs).astype(
            jnp.float32
        )
        result = (
            result
            + short_taps[lag_index].astype(jnp.float32)[None, :] * shifted * same_genome[:, None]
        )
    return result.astype(jnp.bfloat16)


def circulants(table):
    lag_count, width = table.shape
    lag_ids = lax.optimization_barrier(jnp.arange(lag_count, dtype=jnp.int32))
    out_pos = jnp.arange(tile_rows, dtype=jnp.int32)[:, None]
    in_pos = jnp.arange(tile_rows, dtype=jnp.int32)[None, :]
    lag_grid = (out_pos - in_pos + tile_rows) % tile_rows
    one_hot = (lag_grid.reshape(1, tile_rows * tile_rows) == lag_ids[:, None]).astype(table.dtype)
    picked = jnp.dot(table.T, one_hot, preferred_element_type=jnp.float32)
    return picked.astype(table.dtype).reshape(width, tile_rows, tile_rows)


def modal_tables(modal_poles):
    decay_rate = modal_poles[0]
    angles = modal_poles[1]
    residue_re = modal_poles[2]
    residue_im = modal_poles[3]
    powers = jnp.arange(tile_rows + 1).astype(jnp.float32)[:, None, None]
    magnitude = jnp.exp(-powers * decay_rate[None])
    power_re = magnitude * jnp.cos(powers * angles[None])
    power_im = magnitude * jnp.sin(powers * angles[None])
    kernel_re = residue_re[None] * power_re - residue_im[None] * power_im
    kernel_im = residue_re[None] * power_im + residue_im[None] * power_re
    kernel = jnp.sum(kernel_re[:tile_rows], axis=2)
    toeplitz = split_table(kernel)
    outward = jnp.transpose(jnp.concatenate((kernel_re[1:], -kernel_im[1:]), axis=2), (1, 0, 2))
    inward = jnp.transpose(
        jnp.concatenate((power_re[tile_rows - 1 :: -1], power_im[tile_rows - 1 :: -1]), axis=2),
        (1, 0, 2),
    )
    return (toeplitz, outward, inward, power_re[tile_rows], power_im[tile_rows])


def split_table(table):
    upper = table.astype(jnp.bfloat16)
    lower = (table - upper.astype(jnp.float32)).astype(jnp.bfloat16)
    return (upper, lower)


def complex_link(earlier, later):
    early_are, early_aim, early_sre, early_sim = earlier
    late_are, late_aim, late_sre, late_sim = later
    lead_re = late_are[..., None, :]
    lead_im = late_aim[..., None, :]
    return (
        late_are * early_are - late_aim * early_aim,
        late_are * early_aim + late_aim * early_are,
        lead_re * early_sre - lead_im * early_sim + late_sre,
        lead_re * early_sim + lead_im * early_sre + late_sim,
    )


def log_probs(logits, targets):
    vocab_ids = jnp.arange(logits.shape[1], dtype=jnp.int32)
    picked = jnp.sum(
        jnp.where(targets[:, None] == vocab_ids[None, :], logits, jnp.zeros_like(logits)), axis=1
    )
    return picked - jnp.log(jnp.sum(jnp.exp(logits), axis=1))


def channel_logits(normed_cols, unembed):
    return lax.dot_general(
        normed_cols, unembed, (((0,), (0,)), ((), ())), preferred_element_type=jnp.float32
    )


def per_device(
    query_proj,
    key_proj,
    value_proj,
    short_taps,
    medium_taps,
    modal_poles,
    skip_gain,
    norm_gain,
    unembed,
    token_ids,
    genome_lengths,
):
    highest = lax.Precision.HIGHEST
    row_count, chan_count = query_proj.shape
    group_count = chan_count // GROUP
    mode_count = modal_poles.shape[2]
    tile_count = row_count // tile_rows
    first_row = lax.axis_index("seq") * row_count
    segments = segment_ids(first_row + jnp.arange(row_count, dtype=jnp.int32), genome_lengths)
    halo = tile_rows + short_margin
    edge_pair = from_behind(
        jnp.stack((key_proj[row_count - halo :], value_proj[row_count - halo :])),
        "seq",
        1,
    )
    ext_segs = segment_ids(
        first_row - halo + jnp.arange(row_count + halo, dtype=jnp.int32),
        genome_lengths,
    )
    filtered = short_filter(
        jnp.concatenate((edge_pair[0], key_proj)),
        jnp.concatenate((edge_pair[1], value_proj)),
        ext_segs,
        row_count + tile_rows,
        short_taps,
    )
    ext_short = filtered.T.reshape(group_count, GROUP, row_count + tile_rows)
    medium_segs = segment_ids(
        first_row - tile_rows + jnp.arange(row_count + tile_rows, dtype=jnp.int32), genome_lengths
    )

    long_toeplitz, outward, inward, decay_re, decay_im = modal_tables(modal_poles)
    circ = circulants(jnp.concatenate((medium_taps, long_toeplitz[0], long_toeplitz[1]), axis=1))
    circ_medium = jnp.concatenate((circ[:group_count], circ[:group_count]), axis=2)
    toeplitz_upper = circ[group_count : 2 * group_count]
    toeplitz_lower = circ[2 * group_count :]
    lag_band = (
        jnp.arange(tile_rows, dtype=jnp.int32)[:, None] + tile_rows
        - jnp.arange(2 * tile_rows, dtype=jnp.int32)[None, :]
    )
    medium_band = (lag_band >= 0) & (lag_band < medium_taps.shape[0])
    long_band = lag_band[:, tile_rows:] >= 0

    def medium_block(tile_index):
        start = tile_index * tile_rows
        window = lax.dynamic_slice_in_dim(ext_short, start, 2 * tile_rows, 2)
        window_segs = lax.dynamic_slice_in_dim(medium_segs, start, 2 * tile_rows, 0)
        own_segs = lax.dynamic_slice_in_dim(segments, start, tile_rows, 0)
        same_genome = (own_segs[:, None] == window_segs[None, :]) & medium_band
        matrix = jnp.where(same_genome[None], circ_medium, jnp.zeros_like(circ_medium))
        return jnp.einsum(
            "gts,gis->git", matrix, window, preferred_element_type=jnp.float32
        ).astype(jnp.bfloat16)

    signal = jnp.stack([medium_block(tile_index) for tile_index in range(tile_count)])
    inward_upper, inward_lower = split_table(inward)
    tile_segs = segments.reshape(tile_count, tile_rows)
    before = segment_ids(
        first_row + jnp.arange(tile_count, dtype=jnp.int32) * tile_rows - 1, genome_lengths
    )

    def intra_block(inputs):
        block_in, own_segs = inputs
        same_genome = ((own_segs[:, None] == own_segs[None, :]) & long_band)[None]
        upper = jnp.where(same_genome, toeplitz_upper, jnp.zeros_like(toeplitz_upper))
        lower = jnp.where(same_genome, toeplitz_lower, jnp.zeros_like(toeplitz_lower))
        return jnp.einsum(
            "gts,gis->git",
            jnp.concatenate((upper, lower), axis=2),
            jnp.concatenate((block_in, block_in), axis=2),
            preferred_element_type=jnp.float32,
        )

    local_part = jnp.stack([intra_block((signal[j], tile_segs[j])) for j in range(tile_count)])
    end_keep = (tile_segs == tile_segs[:, -1:])[:, None, None, :]
    masked_signal = jnp.where(end_keep, signal, jnp.zeros_like(signal))
    states = jnp.einsum(
        "gsm,jgis->jgim",
        jnp.concatenate((inward_upper, inward_lower), axis=1),
        jnp.concatenate((masked_signal, masked_signal), axis=3),
        preferred_element_type=jnp.float32,
    )
    carried = (tile_segs[:, -1] == before).astype(jnp.float32)

    def chain_link(carry_in, inputs):
        block_states, kept_flag = inputs
        step = (
            decay_re * kept_flag,
            decay_im * kept_flag,
            block_states[..., :mode_count],
            block_states[..., mode_count:],
        )
        return (complex_link(carry_in, step), carry_in)

    state_zero = jnp.zeros((group_count, GROUP, mode_count), jnp.float32)
    start_carry = (
        jnp.ones((group_count, mode_count), jnp.float32),
        jnp.zeros((group_count, mode_count), jnp.float32),
        state_zero,
        state_zero,
    )
    carry = start_carry
    entering_steps = []
    for j in range(tile_count):
        carry, seen = chain_link(carry, (states[j], carried[j]))
        entering_steps.append(seen)
    summary = carry
    entering = tuple(jnp.stack(parts) for parts in zip(*entering_steps))
    incoming = entering_2(
        (summary[0], summary[1], summary[2], summary[3]),
        "seq",
        complex_link,
        (start_carry[0], start_carry[1], start_carry[2], start_carry[3]),
    )
    incoming_re = incoming[2]
    incoming_im = incoming[3]
    reach_re = entering[0][:, :, None, :]
    reach_im = entering[1][:, :, None, :]
    full_re = entering[2] + reach_re * incoming_re - reach_im * incoming_im
    full_im = entering[3] + reach_re * incoming_im + reach_im * incoming_re
    keep_mask = (tile_segs == before[:, None]).astype(jnp.float32)
    carried_part = (
        jnp.einsum(
            "gtm,jgim->jgit",
            outward,
            jnp.concatenate((full_re, full_im), axis=3),
            precision=highest,
        )
        * keep_mask[:, None, None, :]
    )
    longconv = (
        local_part
        + carried_part
        + skip_gain.reshape(group_count, GROUP)[None, :, :, None] * signal.astype(jnp.float32)
    )
    long_cols = jnp.transpose(longconv, (1, 2, 0, 3)).reshape(chan_count, row_count)
    mixed = (query_proj.T.astype(jnp.float32) * long_cols).astype(jnp.bfloat16)
    mixed_wide = mixed.astype(jnp.float32)
    squares = jnp.sum(mixed_wide * mixed_wide, axis=0)
    gained = (mixed_wide * norm_gain[:, None]).astype(jnp.bfloat16)
    partial_value = jnp.concatenate((channel_logits(gained, unembed), squares[:, None]), axis=1)
    lanes = ("chan", "rep")
    lane_count = lax.axis_size(lanes)
    piece = row_count // lane_count
    summed, piece_index = scatter_sum(partial_value, lanes)
    vocab = unembed.shape[1]
    logits = summed[:, :vocab] * lax.rsqrt(summed[:, vocab] / D + norm_eps)[:, None]
    piece_at = piece_index * piece
    logprob_piece = log_probs(logits, lax.dynamic_slice_in_dim(token_ids, piece_at, piece, 0))
    logprob = sum_over(
        lax.dynamic_update_slice_in_dim(
            jnp.zeros((row_count,), jnp.float32), logprob_piece, piece_at, 0
        ),
        lanes,
    )
    genome_index = jnp.arange(genome_lengths.shape[0], dtype=jnp.int32)
    genome_part = jnp.sum(
        jnp.where(
            segments[:, None] == genome_index[None, :],
            logprob[:, None],
            jnp.zeros((row_count, genome_lengths.shape[0]), jnp.float32),
        ),
        axis=0,
    )
    totals = sum_over(genome_part, "seq")
    return (logprob, totals / genome_lengths.astype(jnp.float32))


def solution(mesh):
    return jax.shard_map(
        per_device,
        mesh=mesh,
        in_specs=(
            P(("groups", "seq"), ("chan", "rep")),
            P(("groups", "seq"), ("chan", "rep")),
            P(("groups", "seq"), ("chan", "rep")),
            P(None, ("chan", "rep")),
            P(None, ("chan", "rep")),
            P(None, ("chan", "rep"), None),
            P(("chan", "rep")),
            P(("chan", "rep")),
            P(("chan", "rep"), None),
            P(("groups", "seq")),
            P("groups"),
        ),
        out_specs=(P(("groups", "seq")), P("groups")),
        check_vma=False,
    )
```

```python
import jax
import jax.numpy as jnp
from jax import lax
from jax.sharding import PartitionSpec as P

D = 8192
GROUP = 16


tile_rows = 128
short_margin = 8
norm_eps = 1e-05


def from_behind(shard, axis, by):
    count = lax.axis_size(axis)
    pairs = [(i, i + by) for i in range(count) if 0 <= i + by < count]
    return lax.ppermute(shard, axis, pairs)


def scatter_sum(part, axes):
    count = lax.axis_size(axes)
    place = lax.axis_index(axes)
    bit = 1
    piece_index = 0
    while bit < count:
        half = part.shape[0] // 2
        upper = (place & bit) != 0
        keep = jnp.where(upper, part[half:], part[:half])
        give = jnp.where(upper, part[:half], part[half:])
        part = keep + lax.ppermute(give, axes, [(i, i ^ bit) for i in range(count)])
        piece_index = piece_index * 2 + upper.astype(jnp.int32)
        bit *= 2
    return part, piece_index


def sum_over(part, axis):
    count = lax.axis_size(axis)
    if count & (count - 1):
        return lax.psum(part, axis)
    bit = 1
    while bit < count:
        part = part + lax.ppermute(part, axis, [(i, i ^ bit) for i in range(count)])
        bit *= 2
    return part


def entering_2(part, axis, combine, identity):
    place = lax.axis_index(axis)
    count = lax.axis_size(axis)
    lead = part[0].shape[0]
    widths = [a.size // lead for a in part]

    def pack(t):
        return jnp.concatenate([a.reshape(lead, -1) for a in t], axis=1)

    def unpack(flat):
        pieces = []
        offset = 0
        for a, width in zip(part, widths):
            pieces.append(flat[:, offset : offset + width].reshape(a.shape))
            offset += width
        return tuple(pieces)

    ident = tuple(jnp.zeros_like(a) + jnp.asarray(e, a.dtype) for a, e in zip(part, identity))
    before = ident
    upto = tuple(part)
    shift = 1
    while shift < count:
        arrived = unpack(from_behind(pack(upto), axis, shift))
        arrived = tuple(jnp.where(place >= shift, r, i) for r, i in zip(arrived, ident))
        before = combine(arrived, before)
        upto = combine(arrived, upto)
        shift *= 2
    return before


def segment_ids(positions, genome_lengths):
    starts = jnp.cumsum(genome_lengths) - genome_lengths
    at_or_past = (positions[:, None] >= starts[None, :]).astype(jnp.int32)
    return jnp.sum(at_or_past, axis=1) - 1


def short_filter(keys_in, values_in, seg_list, out_rows, short_taps):
    gated = keys_in.astype(jnp.float32) * values_in.astype(jnp.float32)
    total_rows = keys_in.shape[0]
    lead_rows = total_rows - out_rows
    own_segs = seg_list[lead_rows:]
    result = jnp.zeros((out_rows, keys_in.shape[1]), jnp.float32)
    for lag_index in range(short_taps.shape[0]):
        shifted = gated[lead_rows - lag_index : total_rows - lag_index]
        same_genome = (seg_list[lead_rows - lag_index : total_rows - lag_index] == own_segs).astype(
            jnp.float32
        )
        result = (
            result
            + short_taps[lag_index].astype(jnp.float32)[None, :] * shifted * same_genome[:, None]
        )
    return result.astype(jnp.bfloat16)


def circulants(table):
    lag_count, width = table.shape
    lag_ids = lax.optimization_barrier(jnp.arange(lag_count, dtype=jnp.int32))
    out_pos = jnp.arange(tile_rows, dtype=jnp.int32)[:, None]
    in_pos = jnp.arange(tile_rows, dtype=jnp.int32)[None, :]
    lag_grid = (out_pos - in_pos + tile_rows) % tile_rows
    one_hot = (lag_grid.reshape(1, tile_rows * tile_rows) == lag_ids[:, None]).astype(table.dtype)
    picked = jnp.dot(table.T, one_hot, preferred_element_type=jnp.float32)
    return picked.astype(table.dtype).reshape(width, tile_rows, tile_rows)


def modal_tables(modal_poles):
    decay_rate = modal_poles[0]
    angles = modal_poles[1]
    residue_re = modal_poles[2]
    residue_im = modal_poles[3]
    powers = jnp.arange(tile_rows + 1).astype(jnp.float32)[:, None, None]
    magnitude = jnp.exp(-powers * decay_rate[None])
    power_re = magnitude * jnp.cos(powers * angles[None])
    power_im = magnitude * jnp.sin(powers * angles[None])
    kernel_re = residue_re[None] * power_re - residue_im[None] * power_im
    kernel_im = residue_re[None] * power_im + residue_im[None] * power_re
    kernel = jnp.sum(kernel_re[:tile_rows], axis=2)
    toeplitz = split_table(kernel)
    outward = jnp.transpose(jnp.concatenate((kernel_re[1:], -kernel_im[1:]), axis=2), (1, 0, 2))
    inward = jnp.transpose(
        jnp.concatenate((power_re[tile_rows - 1 :: -1], power_im[tile_rows - 1 :: -1]), axis=2),
        (1, 0, 2),
    )
    return (toeplitz, outward, inward, power_re[tile_rows], power_im[tile_rows])


def split_table(table):
    upper = table.astype(jnp.bfloat16)
    lower = (table - upper.astype(jnp.float32)).astype(jnp.bfloat16)
    return (upper, lower)


def complex_link(earlier, later):
    early_are, early_aim, early_sre, early_sim = earlier
    late_are, late_aim, late_sre, late_sim = later
    lead_re = late_are[..., None, :]
    lead_im = late_aim[..., None, :]
    return (
        late_are * early_are - late_aim * early_aim,
        late_are * early_aim + late_aim * early_are,
        lead_re * early_sre - lead_im * early_sim + late_sre,
        lead_re * early_sim + lead_im * early_sre + late_sim,
    )


def log_probs(logits, targets):
    vocab_ids = jnp.arange(logits.shape[1], dtype=jnp.int32)
    picked = jnp.sum(
        jnp.where(targets[:, None] == vocab_ids[None, :], logits, jnp.zeros_like(logits)), axis=1
    )
    return picked - jnp.log(jnp.sum(jnp.exp(logits), axis=1))


def channel_logits(normed_cols, unembed):
    return lax.dot_general(
        normed_cols, unembed, (((0,), (0,)), ((), ())), preferred_element_type=jnp.float32
    )


def per_device(
    query_proj,
    key_proj,
    value_proj,
    short_taps,
    medium_taps,
    modal_poles,
    skip_gain,
    norm_gain,
    unembed,
    token_ids,
    genome_lengths,
):
    highest = lax.Precision.HIGHEST
    row_count, chan_count = query_proj.shape
    group_count = chan_count // GROUP
    mode_count = modal_poles.shape[2]
    tile_count = row_count // tile_rows
    first_row = lax.axis_index("seq") * row_count
    segments = segment_ids(first_row + jnp.arange(row_count, dtype=jnp.int32), genome_lengths)
    halo = tile_rows + short_margin
    edge_pair = from_behind(
        jnp.stack((key_proj[row_count - halo :], value_proj[row_count - halo :])),
        "seq",
        1,
    )
    ext_segs = segment_ids(
        first_row - halo + jnp.arange(row_count + halo, dtype=jnp.int32),
        genome_lengths,
    )
    filtered = short_filter(
        jnp.concatenate((edge_pair[0], key_proj)),
        jnp.concatenate((edge_pair[1], value_proj)),
        ext_segs,
        row_count + tile_rows,
        short_taps,
    )
    ext_short = filtered.T.reshape(group_count, GROUP, row_count + tile_rows)
    medium_segs = segment_ids(
        first_row - tile_rows + jnp.arange(row_count + tile_rows, dtype=jnp.int32), genome_lengths
    )

    long_toeplitz, outward, inward, decay_re, decay_im = modal_tables(modal_poles)
    circ = circulants(jnp.concatenate((medium_taps, long_toeplitz[0], long_toeplitz[1]), axis=1))
    circ_medium = jnp.concatenate((circ[:group_count], circ[:group_count]), axis=2)
    toeplitz_upper = circ[group_count : 2 * group_count]
    toeplitz_lower = circ[2 * group_count :]
    lag_band = (
        jnp.arange(tile_rows, dtype=jnp.int32)[:, None] + tile_rows
        - jnp.arange(2 * tile_rows, dtype=jnp.int32)[None, :]
    )
    medium_band = (lag_band >= 0) & (lag_band < medium_taps.shape[0])
    long_band = lag_band[:, tile_rows:] >= 0

    def medium_block(tile_index):
        start = tile_index * tile_rows
        window = lax.dynamic_slice_in_dim(ext_short, start, 2 * tile_rows, 2)
        window_segs = lax.dynamic_slice_in_dim(medium_segs, start, 2 * tile_rows, 0)
        own_segs = lax.dynamic_slice_in_dim(segments, start, tile_rows, 0)
        same_genome = (own_segs[:, None] == window_segs[None, :]) & medium_band
        matrix = jnp.where(same_genome[None], circ_medium, jnp.zeros_like(circ_medium))
        return jnp.einsum(
            "gts,gis->git", matrix, window, preferred_element_type=jnp.float32
        ).astype(jnp.bfloat16)

    signal = jnp.stack([medium_block(tile_index) for tile_index in range(tile_count)])
    inward_upper, inward_lower = split_table(inward)
    tile_segs = segments.reshape(tile_count, tile_rows)
    before = segment_ids(
        first_row + jnp.arange(tile_count, dtype=jnp.int32) * tile_rows - 1, genome_lengths
    )

    def intra_block(inputs):
        block_in, own_segs = inputs
        same_genome = ((own_segs[:, None] == own_segs[None, :]) & long_band)[None]
        upper = jnp.where(same_genome, toeplitz_upper, jnp.zeros_like(toeplitz_upper))
        lower = jnp.where(same_genome, toeplitz_lower, jnp.zeros_like(toeplitz_lower))
        return jnp.einsum(
            "gts,gis->git",
            jnp.concatenate((upper, lower), axis=2),
            jnp.concatenate((block_in, block_in), axis=2),
            preferred_element_type=jnp.float32,
        )

    local_part = jnp.stack([intra_block((signal[j], tile_segs[j])) for j in range(tile_count)])
    end_keep = (tile_segs == tile_segs[:, -1:])[:, None, None, :]
    masked_signal = jnp.where(end_keep, signal, jnp.zeros_like(signal))
    states = jnp.einsum(
        "gsm,jgis->jgim",
        jnp.concatenate((inward_upper, inward_lower), axis=1),
        jnp.concatenate((masked_signal, masked_signal), axis=3),
        preferred_element_type=jnp.float32,
    )
    carried = (tile_segs[:, -1] == before).astype(jnp.float32)

    def chain_link(carry_in, inputs):
        block_states, kept_flag = inputs
        step = (
            decay_re * kept_flag,
            decay_im * kept_flag,
            block_states[..., :mode_count],
            block_states[..., mode_count:],
        )
        return (complex_link(carry_in, step), carry_in)

    state_zero = jnp.zeros((group_count, GROUP, mode_count), jnp.float32)
    start_carry = (
        jnp.ones((group_count, mode_count), jnp.float32),
        jnp.zeros((group_count, mode_count), jnp.float32),
        state_zero,
        state_zero,
    )
    carry = start_carry
    entering_steps = []
    for j in range(tile_count):
        carry, seen = chain_link(carry, (states[j], carried[j]))
        entering_steps.append(seen)
    summary = carry
    entering = tuple(jnp.stack(parts) for parts in zip(*entering_steps))
    incoming = entering_2(
        (summary[0], summary[1], summary[2], summary[3]),
        "seq",
        complex_link,
        (start_carry[0], start_carry[1], start_carry[2], start_carry[3]),
    )
    incoming_re = incoming[2]
    incoming_im = incoming[3]
    reach_re = entering[0][:, :, None, :]
    reach_im = entering[1][:, :, None, :]
    full_re = entering[2] + reach_re * incoming_re - reach_im * incoming_im
    full_im = entering[3] + reach_re * incoming_im + reach_im * incoming_re
    keep_mask = (tile_segs == before[:, None]).astype(jnp.float32)
    carried_part = (
        jnp.einsum(
            "gtm,jgim->jgit",
            outward,
            jnp.concatenate((full_re, full_im), axis=3),
            precision=highest,
        )
        * keep_mask[:, None, None, :]
    )
    longconv = (
        local_part
        + carried_part
        + skip_gain.reshape(group_count, GROUP)[None, :, :, None] * signal.astype(jnp.float32)
    )
    long_rows = jnp.transpose(longconv, (0, 3, 1, 2)).reshape(row_count, chan_count)
    mixed = (query_proj.astype(jnp.float32) * long_rows).astype(jnp.bfloat16)
    mixed_wide = mixed.astype(jnp.float32)
    squares = jnp.sum(mixed_wide * mixed_wide, axis=1)
    gained = (mixed_wide * norm_gain[None, :]).astype(jnp.bfloat16)
    partial_value = jnp.concatenate(
        (jnp.dot(gained, unembed, preferred_element_type=jnp.float32), squares[:, None]), axis=1
    )
    lanes = ("chan", "rep")
    lane_count = lax.axis_size(lanes)
    piece = row_count // lane_count
    summed, piece_index = scatter_sum(partial_value, lanes)
    vocab = unembed.shape[1]
    logits = summed[:, :vocab] * lax.rsqrt(summed[:, vocab] / D + norm_eps)[:, None]
    piece_at = piece_index * piece
    logprob_piece = log_probs(logits, lax.dynamic_slice_in_dim(token_ids, piece_at, piece, 0))
    logprob = sum_over(
        lax.dynamic_update_slice_in_dim(
            jnp.zeros((row_count,), jnp.float32), logprob_piece, piece_at, 0
        ),
        lanes,
    )
    genome_index = jnp.arange(genome_lengths.shape[0], dtype=jnp.int32)
    genome_part = jnp.sum(
        jnp.where(
            segments[:, None] == genome_index[None, :],
            logprob[:, None],
            jnp.zeros((row_count, genome_lengths.shape[0]), jnp.float32),
        ),
        axis=0,
    )
    totals = sum_over(genome_part, "seq")
    return (logprob, totals / genome_lengths.astype(jnp.float32))


def solution(mesh):
    return jax.shard_map(
        per_device,
        mesh=mesh,
        in_specs=(
            P(("groups", "seq"), ("chan", "rep")),
            P(("groups", "seq"), ("chan", "rep")),
            P(("groups", "seq"), ("chan", "rep")),
            P(None, ("chan", "rep")),
            P(None, ("chan", "rep")),
            P(None, ("chan", "rep"), None),
            P(("chan", "rep")),
            P(("chan", "rep")),
            P(("chan", "rep"), None),
            P(("groups", "seq")),
            P("groups"),
        ),
        out_specs=(P(("groups", "seq")), P("groups")),
        check_vma=False,
    )
```

```python
import jax
import jax.numpy as jnp
from jax import lax
from jax.sharding import PartitionSpec as P

D = 8192
GROUP = 16


tile_rows = 128
short_margin = 8
norm_eps = 1e-05


def from_behind(shard, axis, by):
    count = lax.axis_size(axis)
    pairs = [(i, i + by) for i in range(count) if 0 <= i + by < count]
    return lax.ppermute(shard, axis, pairs)


def scatter_sum(part, axes):
    count = lax.axis_size(axes)
    place = lax.axis_index(axes)
    bit = 1
    piece_index = 0
    while bit < count:
        half = part.shape[0] // 2
        upper = (place & bit) != 0
        keep = jnp.where(upper, part[half:], part[:half])
        give = jnp.where(upper, part[:half], part[half:])
        part = keep + lax.ppermute(give, axes, [(i, i ^ bit) for i in range(count)])
        piece_index = piece_index * 2 + upper.astype(jnp.int32)
        bit *= 2
    return part, piece_index


def sum_over(part, axis):
    count = lax.axis_size(axis)
    if count & (count - 1):
        return lax.psum(part, axis)
    bit = 1
    while bit < count:
        part = part + lax.ppermute(part, axis, [(i, i ^ bit) for i in range(count)])
        bit *= 2
    return part


def entering_2(part, axis, combine, identity):
    place = lax.axis_index(axis)
    count = lax.axis_size(axis)
    lead = part[0].shape[0]
    widths = [a.size // lead for a in part]

    def pack(t):
        return jnp.concatenate([a.reshape(lead, -1) for a in t], axis=1)

    def unpack(flat):
        pieces = []
        offset = 0
        for a, width in zip(part, widths):
            pieces.append(flat[:, offset : offset + width].reshape(a.shape))
            offset += width
        return tuple(pieces)

    ident = tuple(jnp.zeros_like(a) + jnp.asarray(e, a.dtype) for a, e in zip(part, identity))
    before = ident
    upto = tuple(part)
    shift = 1
    while shift < count:
        arrived = unpack(from_behind(pack(upto), axis, shift))
        arrived = tuple(jnp.where(place >= shift, r, i) for r, i in zip(arrived, ident))
        before = combine(arrived, before)
        upto = combine(arrived, upto)
        shift *= 2
    return before


def segment_ids(positions, genome_lengths):
    starts = jnp.cumsum(genome_lengths) - genome_lengths
    at_or_past = (positions[:, None] >= starts[None, :]).astype(jnp.int32)
    return jnp.sum(at_or_past, axis=1) - 1


def short_filter(keys_in, values_in, seg_list, out_rows, short_taps):
    gated = keys_in.astype(jnp.float32) * values_in.astype(jnp.float32)
    total_rows = keys_in.shape[0]
    lead_rows = total_rows - out_rows
    own_segs = seg_list[lead_rows:]
    result = jnp.zeros((out_rows, keys_in.shape[1]), jnp.float32)
    for lag_index in range(short_taps.shape[0]):
        shifted = gated[lead_rows - lag_index : total_rows - lag_index]
        same_genome = (seg_list[lead_rows - lag_index : total_rows - lag_index] == own_segs).astype(
            jnp.float32
        )
        result = (
            result
            + short_taps[lag_index].astype(jnp.float32)[None, :] * shifted * same_genome[:, None]
        )
    return result.astype(jnp.bfloat16)


def circulants(table):
    lag_count, width = table.shape
    lag_ids = lax.optimization_barrier(jnp.arange(lag_count, dtype=jnp.int32))
    out_pos = jnp.arange(tile_rows, dtype=jnp.int32)[:, None]
    in_pos = jnp.arange(tile_rows, dtype=jnp.int32)[None, :]
    lag_grid = (out_pos - in_pos + tile_rows) % tile_rows
    one_hot = (lag_grid.reshape(1, tile_rows * tile_rows) == lag_ids[:, None]).astype(table.dtype)
    picked = jnp.dot(table.T, one_hot, preferred_element_type=jnp.float32)
    return picked.astype(table.dtype).reshape(width, tile_rows, tile_rows)


def modal_tables(modal_poles):
    decay_rate = modal_poles[0]
    angles = modal_poles[1]
    residue_re = modal_poles[2]
    residue_im = modal_poles[3]
    powers = jnp.arange(tile_rows + 1).astype(jnp.float32)[:, None, None]
    magnitude = jnp.exp(-powers * decay_rate[None])
    power_re = magnitude * jnp.cos(powers * angles[None])
    power_im = magnitude * jnp.sin(powers * angles[None])
    kernel_re = residue_re[None] * power_re - residue_im[None] * power_im
    kernel_im = residue_re[None] * power_im + residue_im[None] * power_re
    kernel = jnp.sum(kernel_re[:tile_rows], axis=2)
    toeplitz = split_table(kernel)
    outward = jnp.transpose(jnp.concatenate((kernel_re[1:], -kernel_im[1:]), axis=2), (1, 0, 2))
    inward = jnp.transpose(
        jnp.concatenate((power_re[tile_rows - 1 :: -1], power_im[tile_rows - 1 :: -1]), axis=2),
        (1, 0, 2),
    )
    return (toeplitz, outward, inward, power_re[tile_rows], power_im[tile_rows])


def split_table(table):
    upper = table.astype(jnp.bfloat16)
    lower = (table - upper.astype(jnp.float32)).astype(jnp.bfloat16)
    return (upper, lower)


def complex_link(earlier, later):
    early_are, early_aim, early_sre, early_sim = earlier
    late_are, late_aim, late_sre, late_sim = later
    lead_re = late_are[..., None, :]
    lead_im = late_aim[..., None, :]
    return (
        late_are * early_are - late_aim * early_aim,
        late_are * early_aim + late_aim * early_are,
        lead_re * early_sre - lead_im * early_sim + late_sre,
        lead_re * early_sim + lead_im * early_sre + late_sim,
    )


def log_probs(logits, targets):
    vocab_ids = jnp.arange(logits.shape[1], dtype=jnp.int32)
    picked = jnp.sum(
        jnp.where(targets[:, None] == vocab_ids[None, :], logits, jnp.zeros_like(logits)), axis=1
    )
    return picked - jnp.log(jnp.sum(jnp.exp(logits), axis=1))


def channel_logits(normed_cols, unembed):
    return lax.dot_general(
        normed_cols, unembed, (((0,), (0,)), ((), ())), preferred_element_type=jnp.float32
    )


def per_device(
    query_proj,
    key_proj,
    value_proj,
    short_taps,
    medium_taps,
    modal_poles,
    skip_gain,
    norm_gain,
    unembed,
    token_ids,
    genome_lengths,
):
    highest = lax.Precision.HIGHEST
    row_count, chan_count = query_proj.shape
    group_count = chan_count // GROUP
    mode_count = modal_poles.shape[2]
    tile_count = row_count // tile_rows
    first_row = lax.axis_index("seq") * row_count
    segments = segment_ids(first_row + jnp.arange(row_count, dtype=jnp.int32), genome_lengths)
    halo = tile_rows + short_margin
    edge_pair = (
        from_behind(key_proj[row_count - halo :], "seq", 1),
        from_behind(value_proj[row_count - halo :], "seq", 1),
    )
    ext_segs = segment_ids(
        first_row - halo + jnp.arange(row_count + halo, dtype=jnp.int32),
        genome_lengths,
    )
    filtered = short_filter(
        jnp.concatenate((edge_pair[0], key_proj)),
        jnp.concatenate((edge_pair[1], value_proj)),
        ext_segs,
        row_count + tile_rows,
        short_taps,
    )
    ext_short = filtered.T.reshape(group_count, GROUP, row_count + tile_rows)
    medium_segs = segment_ids(
        first_row - tile_rows + jnp.arange(row_count + tile_rows, dtype=jnp.int32), genome_lengths
    )

    long_toeplitz, outward, inward, decay_re, decay_im = modal_tables(modal_poles)
    circ = circulants(jnp.concatenate((medium_taps, long_toeplitz[0], long_toeplitz[1]), axis=1))
    circ_medium = jnp.concatenate((circ[:group_count], circ[:group_count]), axis=2)
    toeplitz_upper = circ[group_count : 2 * group_count]
    toeplitz_lower = circ[2 * group_count :]
    lag_band = (
        jnp.arange(tile_rows, dtype=jnp.int32)[:, None] + tile_rows
        - jnp.arange(2 * tile_rows, dtype=jnp.int32)[None, :]
    )
    medium_band = (lag_band >= 0) & (lag_band < medium_taps.shape[0])
    long_band = lag_band[:, tile_rows:] >= 0

    def medium_block(tile_index):
        start = tile_index * tile_rows
        window = lax.dynamic_slice_in_dim(ext_short, start, 2 * tile_rows, 2)
        window_segs = lax.dynamic_slice_in_dim(medium_segs, start, 2 * tile_rows, 0)
        own_segs = lax.dynamic_slice_in_dim(segments, start, tile_rows, 0)
        same_genome = (own_segs[:, None] == window_segs[None, :]) & medium_band
        matrix = jnp.where(same_genome[None], circ_medium, jnp.zeros_like(circ_medium))
        return jnp.einsum(
            "gts,gis->git", matrix, window, preferred_element_type=jnp.float32
        ).astype(jnp.bfloat16)

    signal = jnp.stack([medium_block(tile_index) for tile_index in range(tile_count)])
    inward_upper, inward_lower = split_table(inward)
    tile_segs = segments.reshape(tile_count, tile_rows)
    before = segment_ids(
        first_row + jnp.arange(tile_count, dtype=jnp.int32) * tile_rows - 1, genome_lengths
    )

    def intra_block(inputs):
        block_in, own_segs = inputs
        same_genome = ((own_segs[:, None] == own_segs[None, :]) & long_band)[None]
        upper = jnp.where(same_genome, toeplitz_upper, jnp.zeros_like(toeplitz_upper))
        lower = jnp.where(same_genome, toeplitz_lower, jnp.zeros_like(toeplitz_lower))
        return jnp.einsum(
            "gts,gis->git",
            jnp.concatenate((upper, lower), axis=2),
            jnp.concatenate((block_in, block_in), axis=2),
            preferred_element_type=jnp.float32,
        )

    local_part = jnp.stack([intra_block((signal[j], tile_segs[j])) for j in range(tile_count)])
    end_keep = (tile_segs == tile_segs[:, -1:])[:, None, None, :]
    masked_signal = jnp.where(end_keep, signal, jnp.zeros_like(signal))
    states = jnp.einsum(
        "gsm,jgis->jgim",
        jnp.concatenate((inward_upper, inward_lower), axis=1),
        jnp.concatenate((masked_signal, masked_signal), axis=3),
        preferred_element_type=jnp.float32,
    )
    carried = (tile_segs[:, -1] == before).astype(jnp.float32)

    def chain_link(carry_in, inputs):
        block_states, kept_flag = inputs
        step = (
            decay_re * kept_flag,
            decay_im * kept_flag,
            block_states[..., :mode_count],
            block_states[..., mode_count:],
        )
        return (complex_link(carry_in, step), carry_in)

    state_zero = jnp.zeros((group_count, GROUP, mode_count), jnp.float32)
    start_carry = (
        jnp.ones((group_count, mode_count), jnp.float32),
        jnp.zeros((group_count, mode_count), jnp.float32),
        state_zero,
        state_zero,
    )
    carry = start_carry
    entering_steps = []
    for j in range(tile_count):
        carry, seen = chain_link(carry, (states[j], carried[j]))
        entering_steps.append(seen)
    summary = carry
    entering = tuple(jnp.stack(parts) for parts in zip(*entering_steps))
    incoming = entering_2(
        (summary[0], summary[1], summary[2], summary[3]),
        "seq",
        complex_link,
        (start_carry[0], start_carry[1], start_carry[2], start_carry[3]),
    )
    incoming_re = incoming[2]
    incoming_im = incoming[3]
    reach_re = entering[0][:, :, None, :]
    reach_im = entering[1][:, :, None, :]
    full_re = entering[2] + reach_re * incoming_re - reach_im * incoming_im
    full_im = entering[3] + reach_re * incoming_im + reach_im * incoming_re
    keep_mask = (tile_segs == before[:, None]).astype(jnp.float32)
    carried_part = (
        jnp.einsum(
            "gtm,jgim->jgit",
            outward,
            jnp.concatenate((full_re, full_im), axis=3),
            precision=highest,
        )
        * keep_mask[:, None, None, :]
    )
    longconv = (
        local_part
        + carried_part
        + skip_gain.reshape(group_count, GROUP)[None, :, :, None] * signal.astype(jnp.float32)
    )
    long_rows = jnp.transpose(longconv, (0, 3, 1, 2)).reshape(row_count, chan_count)
    mixed = (query_proj.astype(jnp.float32) * long_rows).astype(jnp.bfloat16)
    mixed_wide = mixed.astype(jnp.float32)
    squares = jnp.sum(mixed_wide * mixed_wide, axis=1)
    gained = (mixed_wide * norm_gain[None, :]).astype(jnp.bfloat16)
    partial_value = jnp.concatenate(
        (jnp.dot(gained, unembed, preferred_element_type=jnp.float32), squares[:, None]), axis=1
    )
    lanes = ("chan", "rep")
    lane_count = lax.axis_size(lanes)
    piece = row_count // lane_count
    summed, piece_index = scatter_sum(partial_value, lanes)
    vocab = unembed.shape[1]
    logits = summed[:, :vocab] * lax.rsqrt(summed[:, vocab] / D + norm_eps)[:, None]
    piece_at = piece_index * piece
    logprob_piece = log_probs(logits, lax.dynamic_slice_in_dim(token_ids, piece_at, piece, 0))
    logprob = sum_over(
        lax.dynamic_update_slice_in_dim(
            jnp.zeros((row_count,), jnp.float32), logprob_piece, piece_at, 0
        ),
        lanes,
    )
    genome_index = jnp.arange(genome_lengths.shape[0], dtype=jnp.int32)
    genome_part = jnp.sum(
        jnp.where(
            segments[:, None] == genome_index[None, :],
            logprob[:, None],
            jnp.zeros((row_count, genome_lengths.shape[0]), jnp.float32),
        ),
        axis=0,
    )
    totals = sum_over(genome_part, "seq")
    return (logprob, totals / genome_lengths.astype(jnp.float32))


def solution(mesh):
    return jax.shard_map(
        per_device,
        mesh=mesh,
        in_specs=(
            P(("groups", "seq"), ("chan", "rep")),
            P(("groups", "seq"), ("chan", "rep")),
            P(("groups", "seq"), ("chan", "rep")),
            P(None, ("chan", "rep")),
            P(None, ("chan", "rep")),
            P(None, ("chan", "rep"), None),
            P(("chan", "rep")),
            P(("chan", "rep")),
            P(("chan", "rep"), None),
            P(("groups", "seq")),
            P("groups"),
        ),
        out_specs=(P(("groups", "seq")), P("groups")),
        check_vma=False,
    )
```

```python
import jax
import jax.numpy as jnp
from jax import lax
from jax.sharding import PartitionSpec as P

D = 8192
GROUP = 16


tile_rows = 128
short_margin = 8
norm_eps = 1e-05


def from_behind(shard, axis, by):
    count = lax.axis_size(axis)
    pairs = [(i, i + by) for i in range(count) if 0 <= i + by < count]
    return lax.ppermute(shard, axis, pairs)


def scatter_sum(part, axes):
    count = lax.axis_size(axes)
    place = lax.axis_index(axes)
    bit = 1
    piece_index = 0
    while bit < count:
        half = part.shape[0] // 2
        upper = (place & bit) != 0
        keep = jnp.where(upper, part[half:], part[:half])
        give = jnp.where(upper, part[:half], part[half:])
        part = keep + lax.ppermute(give, axes, [(i, i ^ bit) for i in range(count)])
        piece_index = piece_index * 2 + upper.astype(jnp.int32)
        bit *= 2
    return part, piece_index


def sum_over(part, axis):
    count = lax.axis_size(axis)
    if count & (count - 1):
        return lax.psum(part, axis)
    bit = 1
    while bit < count:
        part = part + lax.ppermute(part, axis, [(i, i ^ bit) for i in range(count)])
        bit *= 2
    return part


def entering_2(part, axis, combine, identity):
    place = lax.axis_index(axis)
    count = lax.axis_size(axis)
    lead = part[0].shape[0]
    widths = [a.size // lead for a in part]

    def pack(t):
        return jnp.concatenate([a.reshape(lead, -1) for a in t], axis=1)

    def unpack(flat):
        pieces = []
        offset = 0
        for a, width in zip(part, widths):
            pieces.append(flat[:, offset : offset + width].reshape(a.shape))
            offset += width
        return tuple(pieces)

    ident = tuple(jnp.zeros_like(a) + jnp.asarray(e, a.dtype) for a, e in zip(part, identity))
    before = ident
    upto = tuple(part)
    shift = 1
    while shift < count:
        arrived = tuple(from_behind(a, axis, shift) for a in upto)
        arrived = tuple(jnp.where(place >= shift, r, i) for r, i in zip(arrived, ident))
        before = combine(arrived, before)
        upto = combine(arrived, upto)
        shift *= 2
    return before


def segment_ids(positions, genome_lengths):
    starts = jnp.cumsum(genome_lengths) - genome_lengths
    at_or_past = (positions[:, None] >= starts[None, :]).astype(jnp.int32)
    return jnp.sum(at_or_past, axis=1) - 1


def short_filter(keys_in, values_in, seg_list, out_rows, short_taps):
    gated = keys_in.astype(jnp.float32) * values_in.astype(jnp.float32)
    total_rows = keys_in.shape[0]
    lead_rows = total_rows - out_rows
    own_segs = seg_list[lead_rows:]
    result = jnp.zeros((out_rows, keys_in.shape[1]), jnp.float32)
    for lag_index in range(short_taps.shape[0]):
        shifted = gated[lead_rows - lag_index : total_rows - lag_index]
        same_genome = (seg_list[lead_rows - lag_index : total_rows - lag_index] == own_segs).astype(
            jnp.float32
        )
        result = (
            result
            + short_taps[lag_index].astype(jnp.float32)[None, :] * shifted * same_genome[:, None]
        )
    return result.astype(jnp.bfloat16)


def circulants(table):
    lag_count, width = table.shape
    lag_ids = lax.optimization_barrier(jnp.arange(lag_count, dtype=jnp.int32))
    out_pos = jnp.arange(tile_rows, dtype=jnp.int32)[:, None]
    in_pos = jnp.arange(tile_rows, dtype=jnp.int32)[None, :]
    lag_grid = (out_pos - in_pos + tile_rows) % tile_rows
    one_hot = (lag_grid.reshape(1, tile_rows * tile_rows) == lag_ids[:, None]).astype(table.dtype)
    picked = jnp.dot(table.T, one_hot, preferred_element_type=jnp.float32)
    return picked.astype(table.dtype).reshape(width, tile_rows, tile_rows)


def modal_tables(modal_poles):
    decay_rate = modal_poles[0]
    angles = modal_poles[1]
    residue_re = modal_poles[2]
    residue_im = modal_poles[3]
    powers = jnp.arange(tile_rows + 1).astype(jnp.float32)[:, None, None]
    magnitude = jnp.exp(-powers * decay_rate[None])
    power_re = magnitude * jnp.cos(powers * angles[None])
    power_im = magnitude * jnp.sin(powers * angles[None])
    kernel_re = residue_re[None] * power_re - residue_im[None] * power_im
    kernel_im = residue_re[None] * power_im + residue_im[None] * power_re
    kernel = jnp.sum(kernel_re[:tile_rows], axis=2)
    toeplitz = split_table(kernel)
    outward = jnp.transpose(jnp.concatenate((kernel_re[1:], -kernel_im[1:]), axis=2), (1, 0, 2))
    inward = jnp.transpose(
        jnp.concatenate((power_re[tile_rows - 1 :: -1], power_im[tile_rows - 1 :: -1]), axis=2),
        (1, 0, 2),
    )
    return (toeplitz, outward, inward, power_re[tile_rows], power_im[tile_rows])


def split_table(table):
    upper = table.astype(jnp.bfloat16)
    lower = (table - upper.astype(jnp.float32)).astype(jnp.bfloat16)
    return (upper, lower)


def complex_link(earlier, later):
    early_are, early_aim, early_sre, early_sim = earlier
    late_are, late_aim, late_sre, late_sim = later
    lead_re = late_are[..., None, :]
    lead_im = late_aim[..., None, :]
    return (
        late_are * early_are - late_aim * early_aim,
        late_are * early_aim + late_aim * early_are,
        lead_re * early_sre - lead_im * early_sim + late_sre,
        lead_re * early_sim + lead_im * early_sre + late_sim,
    )


def log_probs(logits, targets):
    vocab_ids = jnp.arange(logits.shape[1], dtype=jnp.int32)
    picked = jnp.sum(
        jnp.where(targets[:, None] == vocab_ids[None, :], logits, jnp.zeros_like(logits)), axis=1
    )
    return picked - jnp.log(jnp.sum(jnp.exp(logits), axis=1))


def channel_logits(normed_cols, unembed):
    return lax.dot_general(
        normed_cols, unembed, (((0,), (0,)), ((), ())), preferred_element_type=jnp.float32
    )


def per_device(
    query_proj,
    key_proj,
    value_proj,
    short_taps,
    medium_taps,
    modal_poles,
    skip_gain,
    norm_gain,
    unembed,
    token_ids,
    genome_lengths,
):
    highest = lax.Precision.HIGHEST
    row_count, chan_count = query_proj.shape
    group_count = chan_count // GROUP
    mode_count = modal_poles.shape[2]
    tile_count = row_count // tile_rows
    first_row = lax.axis_index("seq") * row_count
    segments = segment_ids(first_row + jnp.arange(row_count, dtype=jnp.int32), genome_lengths)
    halo = tile_rows + short_margin
    edge_pair = (
        from_behind(key_proj[row_count - halo :], "seq", 1),
        from_behind(value_proj[row_count - halo :], "seq", 1),
    )
    ext_segs = segment_ids(
        first_row - halo + jnp.arange(row_count + halo, dtype=jnp.int32),
        genome_lengths,
    )
    filtered = short_filter(
        jnp.concatenate((edge_pair[0], key_proj)),
        jnp.concatenate((edge_pair[1], value_proj)),
        ext_segs,
        row_count + tile_rows,
        short_taps,
    )
    ext_short = filtered.T.reshape(group_count, GROUP, row_count + tile_rows)
    medium_segs = segment_ids(
        first_row - tile_rows + jnp.arange(row_count + tile_rows, dtype=jnp.int32), genome_lengths
    )

    long_toeplitz, outward, inward, decay_re, decay_im = modal_tables(modal_poles)
    circ = circulants(jnp.concatenate((medium_taps, long_toeplitz[0], long_toeplitz[1]), axis=1))
    circ_medium = jnp.concatenate((circ[:group_count], circ[:group_count]), axis=2)
    toeplitz_upper = circ[group_count : 2 * group_count]
    toeplitz_lower = circ[2 * group_count :]
    lag_band = (
        jnp.arange(tile_rows, dtype=jnp.int32)[:, None] + tile_rows
        - jnp.arange(2 * tile_rows, dtype=jnp.int32)[None, :]
    )
    medium_band = (lag_band >= 0) & (lag_band < medium_taps.shape[0])
    long_band = lag_band[:, tile_rows:] >= 0

    def medium_block(tile_index):
        start = tile_index * tile_rows
        window = lax.dynamic_slice_in_dim(ext_short, start, 2 * tile_rows, 2)
        window_segs = lax.dynamic_slice_in_dim(medium_segs, start, 2 * tile_rows, 0)
        own_segs = lax.dynamic_slice_in_dim(segments, start, tile_rows, 0)
        same_genome = (own_segs[:, None] == window_segs[None, :]) & medium_band
        matrix = jnp.where(same_genome[None], circ_medium, jnp.zeros_like(circ_medium))
        return jnp.einsum(
            "gts,gis->git", matrix, window, preferred_element_type=jnp.float32
        ).astype(jnp.bfloat16)

    signal = jnp.stack([medium_block(tile_index) for tile_index in range(tile_count)])
    inward_upper, inward_lower = split_table(inward)
    tile_segs = segments.reshape(tile_count, tile_rows)
    before = segment_ids(
        first_row + jnp.arange(tile_count, dtype=jnp.int32) * tile_rows - 1, genome_lengths
    )

    def intra_block(inputs):
        block_in, own_segs = inputs
        same_genome = ((own_segs[:, None] == own_segs[None, :]) & long_band)[None]
        upper = jnp.where(same_genome, toeplitz_upper, jnp.zeros_like(toeplitz_upper))
        lower = jnp.where(same_genome, toeplitz_lower, jnp.zeros_like(toeplitz_lower))
        return jnp.einsum(
            "gts,gis->git",
            jnp.concatenate((upper, lower), axis=2),
            jnp.concatenate((block_in, block_in), axis=2),
            preferred_element_type=jnp.float32,
        )

    local_part = jnp.stack([intra_block((signal[j], tile_segs[j])) for j in range(tile_count)])
    end_keep = (tile_segs == tile_segs[:, -1:])[:, None, None, :]
    masked_signal = jnp.where(end_keep, signal, jnp.zeros_like(signal))
    states = jnp.einsum(
        "gsm,jgis->jgim",
        jnp.concatenate((inward_upper, inward_lower), axis=1),
        jnp.concatenate((masked_signal, masked_signal), axis=3),
        preferred_element_type=jnp.float32,
    )
    carried = (tile_segs[:, -1] == before).astype(jnp.float32)

    def chain_link(carry_in, inputs):
        block_states, kept_flag = inputs
        step = (
            decay_re * kept_flag,
            decay_im * kept_flag,
            block_states[..., :mode_count],
            block_states[..., mode_count:],
        )
        return (complex_link(carry_in, step), carry_in)

    state_zero = jnp.zeros((group_count, GROUP, mode_count), jnp.float32)
    start_carry = (
        jnp.ones((group_count, mode_count), jnp.float32),
        jnp.zeros((group_count, mode_count), jnp.float32),
        state_zero,
        state_zero,
    )
    carry = start_carry
    entering_steps = []
    for j in range(tile_count):
        carry, seen = chain_link(carry, (states[j], carried[j]))
        entering_steps.append(seen)
    summary = carry
    entering = tuple(jnp.stack(parts) for parts in zip(*entering_steps))
    incoming = entering_2(
        (summary[0], summary[1], summary[2], summary[3]),
        "seq",
        complex_link,
        (start_carry[0], start_carry[1], start_carry[2], start_carry[3]),
    )
    incoming_re = incoming[2]
    incoming_im = incoming[3]
    reach_re = entering[0][:, :, None, :]
    reach_im = entering[1][:, :, None, :]
    full_re = entering[2] + reach_re * incoming_re - reach_im * incoming_im
    full_im = entering[3] + reach_re * incoming_im + reach_im * incoming_re
    keep_mask = (tile_segs == before[:, None]).astype(jnp.float32)
    carried_part = (
        jnp.einsum(
            "gtm,jgim->jgit",
            outward,
            jnp.concatenate((full_re, full_im), axis=3),
            precision=highest,
        )
        * keep_mask[:, None, None, :]
    )
    longconv = (
        local_part
        + carried_part
        + skip_gain.reshape(group_count, GROUP)[None, :, :, None] * signal.astype(jnp.float32)
    )
    long_rows = jnp.transpose(longconv, (0, 3, 1, 2)).reshape(row_count, chan_count)
    mixed = (query_proj.astype(jnp.float32) * long_rows).astype(jnp.bfloat16)
    mixed_wide = mixed.astype(jnp.float32)
    squares = jnp.sum(mixed_wide * mixed_wide, axis=1)
    gained = (mixed_wide * norm_gain[None, :]).astype(jnp.bfloat16)
    partial_value = jnp.concatenate(
        (jnp.dot(gained, unembed, preferred_element_type=jnp.float32), squares[:, None]), axis=1
    )
    lanes = ("chan", "rep")
    lane_count = lax.axis_size(lanes)
    piece = row_count // lane_count
    summed, piece_index = scatter_sum(partial_value, lanes)
    vocab = unembed.shape[1]
    logits = summed[:, :vocab] * lax.rsqrt(summed[:, vocab] / D + norm_eps)[:, None]
    piece_at = piece_index * piece
    logprob_piece = log_probs(logits, lax.dynamic_slice_in_dim(token_ids, piece_at, piece, 0))
    logprob = sum_over(
        lax.dynamic_update_slice_in_dim(
            jnp.zeros((row_count,), jnp.float32), logprob_piece, piece_at, 0
        ),
        lanes,
    )
    genome_index = jnp.arange(genome_lengths.shape[0], dtype=jnp.int32)
    genome_part = jnp.sum(
        jnp.where(
            segments[:, None] == genome_index[None, :],
            logprob[:, None],
            jnp.zeros((row_count, genome_lengths.shape[0]), jnp.float32),
        ),
        axis=0,
    )
    totals = sum_over(genome_part, "seq")
    return (logprob, totals / genome_lengths.astype(jnp.float32))


def solution(mesh):
    return jax.shard_map(
        per_device,
        mesh=mesh,
        in_specs=(
            P(("groups", "seq"), ("chan", "rep")),
            P(("groups", "seq"), ("chan", "rep")),
            P(("groups", "seq"), ("chan", "rep")),
            P(None, ("chan", "rep")),
            P(None, ("chan", "rep")),
            P(None, ("chan", "rep"), None),
            P(("chan", "rep")),
            P(("chan", "rep")),
            P(("chan", "rep"), None),
            P(("groups", "seq")),
            P("groups"),
        ),
        out_specs=(P(("groups", "seq")), P("groups")),
        check_vma=False,
    )
```
